32 devices in a mesh: pairs: 2 (over x), rows: 16 (over z, y, core).
Axes of the slice: x: 2, y: 2, z: 4, core: 2. Of those that a mesh axis runs over, the one named last changes fastest.
Arguments:
- specimen_pair_inputs: bfloat16 [2, 256, 256, 128], P(None, ('pairs', 'rows')), parts along dimension 1, may hold values from -120 to 120
- initial_kernel_tensor: bfloat16 [3, 3, 128, 128], replicated, may hold values from -0.1875 to 0.1875
- latter_kernel_tensor: bfloat16 [3, 3, 128, 128], replicated, may hold values from -0.1875 to 0.1875
- latter_kernel_intercept: float32 [128], replicated, may hold values from -3 to 3
- patch_horizontal_shift: int32 [32, 2], P(('pairs', 'rows')), parts along dimension 0, may hold values from -4 to 4
- specimen_presence: int32 [32, 2], P(('pairs', 'rows')), parts along dimension 0, may hold values 0 or 1
- softmax_sharpening: float32 [32, 2], P(('pairs', 'rows')), parts along dimension 0, may hold values from 2 to 300
Outputs:
- flow_field: float32 [2, 256, 256], P(None, ('pairs', 'rows')), parts along dimension 1
The draws below stay inside these ranges and needn't reach their ends.
There are 2 independent parts, one for each index of `pairs`. The reference program is written for one: setup_inputs(seed, part) draws one part's arguments, and reference() takes and returns one part's arrays. A program takes and returns all parts, laid end to end along the dimension named above; an argument that names none is the same for every part. Nothing has to cross between parts.
All inputs are finite; a program needn't handle non-finite values. No bound on the sum of `specimen_presence` on one device may be relied on, other than what follows from the above.
Results may differ from the reference program's by a relative error of at most 0.006.
The reference program's roundings to bfloat16 on the way count: a program that leaves them out, or rounds other values in their place, can miss the bound.
Values may be sent and summed in bfloat16 or wider, within the bound.
No kernel may reach another device: no remote copies, remote signals or barrier semaphores. Data moves between devices by JAX's collectives and lax.ppermute only.
A program may use at most 64 MiB of HBM per device.

```python
import jax
import jax.numpy as jnp
from jax import lax

DEPTH_OF_EMBED = 128
W = 256
RADIUS = 4
PATCH_HEIGHT_PX = 8
PATCH_WIDTH_PX = 128
H = 128


def draw_specimen_pair_inputs(key, part):
    keys = jax.random.split(key, 5)
    rising = 3.0 ** (jnp.arange(H, dtype=jnp.float32) / H)
    row_scale = rising * jnp.exp(jnp.log(10.0) * jax.random.uniform(keys[0], (H,)))
    col_scale = jnp.exp(jnp.log(10.0) * jax.random.uniform(keys[1], (W,)))
    scale_map = (row_scale[:, None] * col_scale[None, :] / 10.0)[:, :, None]
    base = jnp.clip(jax.random.normal(keys[2], (H + 2, W + 4, DEPTH_OF_EMBED)), -4.0, 4.0)
    noise_a = jnp.clip(jax.random.normal(keys[3], (H, W, DEPTH_OF_EMBED)), -4.0, 4.0)
    noise_b = jnp.clip(jax.random.normal(keys[4], (H, W, DEPTH_OF_EMBED)), -4.0, 4.0)
    first_slide = (0.8 * base[1:H + 1, 2:W + 2] + 0.6 * noise_a) * scale_map
    second_slide = (0.8 * base[0:H, 0:W] + 0.6 * noise_b) * scale_map
    both = jnp.clip(jnp.stack([first_slide, second_slide], axis=0), -120.0, 120.0)
    return both.astype(jnp.bfloat16)


def draw_softmax_sharpening(key, part):
    uniform_part = jax.random.uniform(key, (H // PATCH_HEIGHT_PX, W // PATCH_WIDTH_PX))
    lower, upper = (2.0, 40.0)
    return jnp.exp(jnp.log(lower) + uniform_part * jnp.log(upper / lower)).astype(jnp.float32)


def place_ends(result, key, smallest, largest):
    index_at = [jax.random.randint(jax.random.fold_in(key, axis), (), 0, length) for axis, length in enumerate(result.shape)]
    widest = result.shape.index(max(result.shape))
    neighbour = index_at[:widest] + [(index_at[widest] + 1) % result.shape[widest]] + index_at[widest + 1:]
    return result.at[tuple(index_at)].set(smallest).at[tuple(neighbour)].set(largest)


def centred(rng, shape, scale, most, held_as=jnp.bfloat16):
    return jnp.clip(scale * jax.random.normal(rng, shape, jnp.float32), -most, most).astype(held_as)


def setup_inputs(seed: int = 0, part: int = 0) -> dict:
    seeds = jax.random.split(jax.random.key(seed), 8)
    own_keys = jax.random.split(jax.random.fold_in(seeds[7], part), 8)
    return {
        "specimen_pair_inputs": draw_specimen_pair_inputs(jax.random.fold_in(jax.random.fold_in(seeds[7], part), 71), part),
        "initial_kernel_tensor": centred(seeds[1], (3, 3, DEPTH_OF_EMBED, DEPTH_OF_EMBED), (9 * DEPTH_OF_EMBED) ** -0.5, 0.1875),
        "latter_kernel_tensor": centred(seeds[2], (3, 3, DEPTH_OF_EMBED, DEPTH_OF_EMBED), (9 * DEPTH_OF_EMBED) ** -0.5, 0.1875),
        "latter_kernel_intercept": centred(seeds[3], (DEPTH_OF_EMBED,), 0.5, 3.0, jnp.float32),
        "patch_horizontal_shift": place_ends(jax.random.randint(own_keys[4], (H // PATCH_HEIGHT_PX, W // PATCH_WIDTH_PX), -4, 5), jax.random.fold_in(own_keys[4], 1), -4, 4).astype(jnp.int32),
        "specimen_presence": place_ends((jax.random.randint(own_keys[5], (H // PATCH_HEIGHT_PX, W // PATCH_WIDTH_PX), 0, 4) < 3).astype(jnp.int32), jax.random.fold_in(own_keys[5], 1), 0, 1),
        "softmax_sharpening": draw_softmax_sharpening(jax.random.fold_in(jax.random.fold_in(seeds[7], part), 71), part),
    }


def conv_same(field, kernel):
    return lax.conv_general_dilated(field.astype(jnp.float32)[None], kernel.astype(jnp.float32), (1, 1), ((1, 1), (1, 1)), dimension_numbers=('NHWC', 'HWIO', 'NHWC'), precision=lax.Precision.HIGHEST)[0]

def reference(specimen_pair_inputs, initial_kernel_tensor, latter_kernel_tensor, latter_kernel_intercept, patch_horizontal_shift, specimen_presence, softmax_sharpening):
    feature_list = []
    for which in range(2):
        first_out = conv_same(specimen_pair_inputs[which], initial_kernel_tensor)
        average = lax.optimization_barrier(jnp.mean(first_out, axis=(0, 1)))
        variance = lax.optimization_barrier(jnp.mean(jnp.square(first_out - average), axis=(0, 1)))
        hidden = jax.nn.relu((first_out - average) * lax.rsqrt(variance + 1e-05)).astype(jnp.bfloat16)
        second_out = conv_same(hidden, latter_kernel_tensor) + latter_kernel_intercept.astype(jnp.float32)
        scaled = second_out * lax.rsqrt(lax.optimization_barrier(jnp.mean(second_out * second_out, axis=-1, keepdims=True)) + 1e-06)
        feature_list.append(scaled.astype(jnp.bfloat16))
    source_descriptors = feature_list[0].astype(jnp.float32)
    padded_b = jnp.pad(feature_list[1].astype(jnp.float32), ((RADIUS, RADIUS), (8, 8), (0, 0)))
    col_shift = jnp.repeat(jnp.repeat(patch_horizontal_shift, PATCH_HEIGHT_PX, axis=0), PATCH_WIDTH_PX, axis=1).astype(jnp.int32)
    col_index = jnp.arange(W, dtype=jnp.int32)[None, :] + col_shift + (8 - RADIUS)
    score_list = []
    for row_step in range(2 * RADIUS + 1):
        band_rows = padded_b[row_step:row_step + H]
        for col_step in range(2 * RADIUS + 1):
            picked = jnp.take_along_axis(band_rows, (col_index + col_step)[:, :, None], axis=1)
            score_list.append(lax.optimization_barrier(jnp.sum(source_descriptors * picked, axis=-1)))
    pairing_probabilities = jnp.stack(score_list, axis=-1)
    sharpening_grid = jnp.repeat(jnp.repeat(softmax_sharpening, PATCH_HEIGHT_PX, axis=0), PATCH_WIDTH_PX, axis=1)
    pairing_energies = pairing_probabilities * (sharpening_grid / DEPTH_OF_EMBED)[:, :, None]
    probability = jax.nn.softmax(pairing_energies, axis=-1)
    steps_all = jnp.arange((2 * RADIUS + 1) ** 2, dtype=jnp.int32)
    row_disp = (steps_all // (2 * RADIUS + 1) - RADIUS).astype(jnp.float32)
    col_disp = (steps_all % (2 * RADIUS + 1) - RADIUS).astype(jnp.float32)
    flow_y = lax.optimization_barrier(jnp.sum(probability * row_disp, axis=-1))
    flow_x = lax.optimization_barrier(jnp.sum(probability * col_disp, axis=-1)) + col_shift.astype(jnp.float32)
    tissue_map = jnp.repeat(jnp.repeat(specimen_presence, PATCH_HEIGHT_PX, axis=0), PATCH_WIDTH_PX, axis=1).astype(jnp.float32)
    return jnp.stack([flow_y, flow_x], axis=0) * tissue_map[None]
```

```python
import jax
import jax.numpy as jnp
from jax import lax
from jax.sharding import PartitionSpec as P
from jax.experimental import pallas as pl
from jax.experimental.pallas import tpu as pltpu

DISP = 81


def _corr_kernel(shift_ref, sharp_ref, pres_ref, f0_ref, win_ref, out_ref, acc_ref):
    rows = f0_ref.shape[0]
    half = f0_ref.shape[1] // 4
    lane = lax.broadcasted_iota(jnp.int32, (half, 128), 1)
    band = lane // 9
    valid = lane < DISP
    vlane = lax.broadcasted_iota(jnp.int32, (8, 128), 1)
    vrow = lax.broadcasted_iota(jnp.int32, (8, 128), 0)
    weights = jnp.where(
        vlane < DISP,
        jnp.where(vrow == 0, 1.0, jnp.where(vrow == 1, (vlane // 9 - 4).astype(jnp.float32),
                                             jnp.where(vrow == 2, (4 - vlane % 9).astype(jnp.float32), 0.0))),
        0.0,
    ).astype(jnp.float32)
    for t in range(2):
        shift_t = shift_ref[0, t]
        scale = sharp_ref[0, t] / 128.0
        present = pres_ref[0, t].astype(jnp.float32)
        for q in range(2):
            cols = slice(128 * t + half * q, 128 * t + half * (q + 1))
            acc_ref[...] = jnp.zeros_like(acc_ref)
            for hp in range(rows + 8):
                lo, hi = max(0, hp - 8), min(rows - 1, hp)
                lhs = f0_ref[lo:hi + 1, cols, :].reshape((hi - lo + 1) * half, 128)
                w = win_ref[2 * t + q, hp]
                s = lax.dot_general(lhs, w, (((1,), (1,)), ((), ())), preferred_element_type=jnp.float32)
                for h in range(lo, hi + 1):
                    a = hp - h
                    blk = s[(h - lo) * half:(h - lo + 1) * half]
                    rolled = pltpu.roll(blk, 9 + 9 * a, 1, stride=1, stride_axis=0)
                    acc_ref[h] = jnp.where(band == a, rolled, acc_ref[h])
            for h in range(rows):
                energy = acc_ref[h] * scale
                energy = jnp.where(valid, energy, -jnp.inf)
                top = jnp.max(energy, axis=1, keepdims=True)
                p = jnp.exp(energy - top)
                r = lax.dot_general(weights, p, (((1,), (1,)), ((), ())), preferred_element_type=jnp.float32,
                                    precision=lax.Precision.HIGHEST)
                inv = 1.0 / r[0:1]
                out_ref[0, h:h + 1, cols] = r[1:2] * inv * present
                out_ref[1, h:h + 1, cols] = (r[2:3] * inv + shift_t.astype(jnp.float32)) * present


def correlation(f0, f1ext, shift, presence, sharp):
    rows, width, depth = f0.shape
    half = 64
    f1pad = jnp.pad(f1ext, ((0, 0), (8, 64), (0, 0)))
    frev = f1pad[:, ::-1, :]
    P = f1pad.shape[1]
    wins = []
    for t in range(2):
        for q in range(2):
            col0 = 128 * t + half * q + shift[0, t] - 4
            start = P - 136 - col0
            wins.append(lax.dynamic_slice(frev, (0, start, 0), (rows + 8, 128, depth)))
    win = jnp.stack(wins)
    return pl.pallas_call(
        _corr_kernel,
        out_shape=jax.ShapeDtypeStruct((2, rows, width), jnp.float32),
        in_specs=[pl.BlockSpec(memory_space=pltpu.SMEM)] * 3 + [pl.BlockSpec(memory_space=pltpu.VMEM)] * 2,
        out_specs=pl.BlockSpec(memory_space=pltpu.VMEM),
        scratch_shapes=[pltpu.VMEM((rows, half, 128), jnp.float32)],
    )(shift, sharp, presence, f0, win)


def extended(array, sides, width):
    for axis, dim in sides:
        size, length = (lax.axis_size(axis), array.shape[dim])
        up = [(i, (i + 1) % size) for i in range(size - 1)]
        down = [(j, i) for i, j in up]
        last = lax.slice_in_dim(array, length - width, length, axis=dim)
        initial = lax.slice_in_dim(array, 0, width, axis=dim)
        before = lax.ppermute(last, axis, up)
        after = lax.ppermute(initial, axis, down)
        array = jnp.concatenate([before, array, after], axis=dim)
    return array


def conv_rows(field, kernel):
    return lax.conv_general_dilated(
        field,
        kernel,
        (1, 1),
        ((0, 0), (1, 1)),
        dimension_numbers=("NHWC", "HWIO", "NHWC"),
        preferred_element_type=jnp.float32,
    )


def finish_features(second_out, latter_kernel_intercept):
    shifted = second_out + latter_kernel_intercept
    return (
        shifted * lax.rsqrt(jnp.mean(shifted * shifted, axis=-1, keepdims=True) + 1e-06)
    ).astype(jnp.bfloat16)


def local(
    specimen_pair_inputs,
    initial_kernel_tensor,
    latter_kernel_tensor,
    latter_kernel_intercept,
    patch_horizontal_shift,
    specimen_presence,
    softmax_sharpening,
):
    rows_dev = specimen_pair_inputs.shape[1]
    width = specimen_pair_inputs.shape[2]
    total_rows = rows_dev * lax.axis_size("rows")
    cells_all = total_rows * width
    padded = extended(specimen_pair_inputs, (("rows", 1),), 1)
    own_rows = conv_rows(padded, initial_kernel_tensor)
    first_a = own_rows[0:1]
    first_b = own_rows[1:2]
    total, squares = lax.psum(
        (jnp.sum(own_rows, axis=(1, 2)), jnp.sum(own_rows * own_rows, axis=(1, 2))), "rows"
    )
    average = total / cells_all
    variance = squares / cells_all - average * average
    inv_scale = lax.rsqrt(variance + 1e-05)

    def normed(field, which):
        return jax.nn.relu((field - average[which]) * inv_scale[which])

    hidden = jnp.concatenate([normed(first_a, 0), normed(first_b, 1)], axis=0).astype(jnp.bfloat16)
    hidden_ext = extended(hidden, (("rows", 1),), 1)
    features = finish_features(conv_rows(hidden_ext, latter_kernel_tensor), latter_kernel_intercept)
    source_descriptors = features[0]
    target_descriptors_padded = extended(features[1], (("rows", 0),), 4)
    return correlation(
        source_descriptors,
        target_descriptors_padded,
        patch_horizontal_shift,
        specimen_presence,
        softmax_sharpening,
    )


def solution(mesh):
    return jax.shard_map(
        local,
        mesh=mesh,
        in_specs=(
            P(None, ("pairs", "rows"), None, None),
            P(),
            P(),
            P(),
            P(("pairs", "rows"), None),
            P(("pairs", "rows"), None),
            P(("pairs", "rows"), None),
        ),
        out_specs=P(None, ("pairs", "rows"), None),
        check_vma=False,
    )
```

```python
import jax
import jax.numpy as jnp
from jax import lax
from jax.sharding import PartitionSpec as P
from jax.experimental import pallas as pl
from jax.experimental.pallas import tpu as pltpu

DISP = 81


def _corr_kernel(shift_ref, sharp_ref, pres_ref, f0_ref, win_ref, out_ref, acc_ref):
    rows = f0_ref.shape[0]
    half = f0_ref.shape[1] // 4
    lane = lax.broadcasted_iota(jnp.int32, (half, 128), 1)
    band = lane // 9
    valid = lane < DISP
    vlane = lax.broadcasted_iota(jnp.int32, (8, 128), 1)
    vrow = lax.broadcasted_iota(jnp.int32, (8, 128), 0)
    weights = jnp.where(
        vlane < DISP,
        jnp.where(vrow == 0, 1.0, jnp.where(vrow == 1, (vlane // 9 - 4).astype(jnp.float32),
                                             jnp.where(vrow == 2, (4 - vlane % 9).astype(jnp.float32), 0.0))),
        0.0,
    ).astype(jnp.float32)
    for t in range(2):
        shift_t = shift_ref[0, t]
        scale = sharp_ref[0, t] / 128.0
        present = pres_ref[0, t].astype(jnp.float32)
        for q in range(2):
            cols = slice(128 * t + half * q, 128 * t + half * (q + 1))
            acc_ref[...] = jnp.zeros_like(acc_ref)
            for hp in range(rows + 8):
                lo, hi = max(0, hp - 8), min(rows - 1, hp)
                lhs = f0_ref[lo:hi + 1, cols, :].reshape((hi - lo + 1) * half, 128)
                w = win_ref[2 * t + q, hp]
                s = lax.dot_general(lhs, w, (((1,), (1,)), ((), ())), preferred_element_type=jnp.float32)
                for h in range(lo, hi + 1):
                    a = hp - h
                    blk = s[(h - lo) * half:(h - lo + 1) * half]
                    rolled = pltpu.roll(blk, 9 + 9 * a, 1, stride=1, stride_axis=0)
                    acc_ref[h] = jnp.where(band == a, rolled, acc_ref[h])
            for h in range(rows):
                energy = acc_ref[h] * scale
                energy = jnp.where(valid, energy, -jnp.inf)
                top = jnp.max(energy, axis=1, keepdims=True)
                p = jnp.exp(energy - top)
                r = lax.dot_general(weights, p, (((1,), (1,)), ((), ())), preferred_element_type=jnp.float32,
                                    precision=lax.Precision.HIGHEST)
                inv = 1.0 / r[0:1]
                out_ref[0, h:h + 1, cols] = r[1:2] * inv * present
                out_ref[1, h:h + 1, cols] = (r[2:3] * inv + shift_t.astype(jnp.float32)) * present


def correlation(f0, f1ext, shift, presence, sharp):
    rows, width, depth = f0.shape
    half = 64
    f1pad = jnp.pad(f1ext, ((0, 0), (8, 64), (0, 0)))
    frev = f1pad[:, ::-1, :]
    P = f1pad.shape[1]
    wins = []
    for t in range(2):
        for q in range(2):
            col0 = 128 * t + half * q + shift[0, t] - 4
            start = P - 136 - col0
            wins.append(lax.dynamic_slice(frev, (0, start, 0), (rows + 8, 128, depth)))
    win = jnp.stack(wins)
    return pl.pallas_call(
        _corr_kernel,
        out_shape=jax.ShapeDtypeStruct((2, rows, width), jnp.float32),
        in_specs=[pl.BlockSpec(memory_space=pltpu.SMEM)] * 3 + [pl.BlockSpec(memory_space=pltpu.VMEM)] * 2,
        out_specs=pl.BlockSpec(memory_space=pltpu.VMEM),
        scratch_shapes=[pltpu.VMEM((rows, half, 128), jnp.float32)],
    )(shift, sharp, presence, f0, win)


def extended(array, sides, width):
    for axis, dim in sides:
        size, length = (lax.axis_size(axis), array.shape[dim])
        up = [(i, (i + 1) % size) for i in range(size - 1)]
        down = [(j, i) for i, j in up]
        last = lax.slice_in_dim(array, length - width, length, axis=dim)
        initial = lax.slice_in_dim(array, 0, width, axis=dim)
        before = lax.ppermute(last, axis, up)
        after = lax.ppermute(initial, axis, down)
        array = jnp.concatenate([before, array, after], axis=dim)
    return array


def butterfly_sum(x, axis):
    size = lax.axis_size(axis)
    if size & (size - 1):
        return lax.psum(x, axis)
    step = 1
    while step < size:
        x = x + lax.ppermute(x, axis, [(i, i ^ step) for i in range(size)])
        step *= 2
    return x


def conv_rows(field, kernel):
    return lax.conv_general_dilated(
        field,
        kernel,
        (1, 1),
        ((0, 0), (1, 1)),
        dimension_numbers=("NHWC", "HWIO", "NHWC"),
        preferred_element_type=jnp.float32,
    )


def finish_features(second_out, latter_kernel_intercept):
    shifted = second_out + latter_kernel_intercept
    return (
        shifted * lax.rsqrt(jnp.mean(shifted * shifted, axis=-1, keepdims=True) + 1e-06)
    ).astype(jnp.bfloat16)


def local(
    specimen_pair_inputs,
    initial_kernel_tensor,
    latter_kernel_tensor,
    latter_kernel_intercept,
    patch_horizontal_shift,
    specimen_presence,
    softmax_sharpening,
):
    rows_dev = specimen_pair_inputs.shape[1]
    width = specimen_pair_inputs.shape[2]
    total_rows = rows_dev * lax.axis_size("rows")
    cells_all = total_rows * width
    padded = extended(specimen_pair_inputs, (("rows", 1),), 1)
    own_rows = conv_rows(padded, initial_kernel_tensor)
    first_a = own_rows[0:1]
    first_b = own_rows[1:2]
    stats = jnp.concatenate(
        [jnp.sum(own_rows, axis=(1, 2)), jnp.sum(own_rows * own_rows, axis=(1, 2))], axis=0
    )
    stats = butterfly_sum(stats, "rows")
    total, squares = stats[0:2], stats[2:4]
    average = total / cells_all
    variance = squares / cells_all - average * average
    inv_scale = lax.rsqrt(variance + 1e-05)

    def normed(field, which):
        return jax.nn.relu((field - average[which]) * inv_scale[which])

    hidden = jnp.concatenate([normed(first_a, 0), normed(first_b, 1)], axis=0).astype(jnp.bfloat16)
    hidden_ext = extended(hidden, (("rows", 1),), 1)
    features = finish_features(conv_rows(hidden_ext, latter_kernel_tensor), latter_kernel_intercept)
    source_descriptors = features[0]
    target_descriptors_padded = extended(features[1], (("rows", 0),), 4)
    return correlation(
        source_descriptors,
        target_descriptors_padded,
        patch_horizontal_shift,
        specimen_presence,
        softmax_sharpening,
    )


def solution(mesh):
    return jax.shard_map(
        local,
        mesh=mesh,
        in_specs=(
            P(None, ("pairs", "rows"), None, None),
            P(),
            P(),
            P(),
            P(("pairs", "rows"), None),
            P(("pairs", "rows"), None),
            P(("pairs", "rows"), None),
        ),
        out_specs=P(None, ("pairs", "rows"), None),
        check_vma=False,
    )
```

```python
import jax
import jax.numpy as jnp
from jax import lax
from jax.sharding import PartitionSpec as P
from jax.experimental import pallas as pl
from jax.experimental.pallas import tpu as pltpu

DISP = 81


def _corr_kernel(shift_ref, sharp_ref, pres_ref, f0_ref, frev_hbm, out_ref, win_ref, acc_ref, sems):
    rows = f0_ref.shape[0]
    half = f0_ref.shape[1] // 4
    copies = []
    for t in range(2):
        for q in range(2):
            start = 196 - 128 * t - half * q - shift_ref[0, t]
            cp = pltpu.make_async_copy(frev_hbm.at[:, pl.ds(start, 128), :], win_ref.at[2 * t + q],
                                       sems.at[2 * t + q])
            cp.start()
            copies.append(cp)
    lane = lax.broadcasted_iota(jnp.int32, (half, 128), 1)
    band = lane // 9
    li = lax.broadcasted_iota(jnp.int32, (128, 1), 0)
    valid = li < DISP
    row_d = jnp.where(valid, li // 9 - 4, 0).astype(jnp.float32)
    col_d = jnp.where(valid, 4 - li % 9, 0).astype(jnp.float32)
    for t in range(2):
        shift_t = shift_ref[0, t].astype(jnp.float32)
        scale = sharp_ref[0, t] / 128.0
        present = pres_ref[0, t].astype(jnp.float32)
        for q in range(2):
            cols = slice(128 * t + half * q, 128 * t + half * (q + 1))
            copies[2 * t + q].wait()
            acc_ref[...] = jnp.zeros_like(acc_ref)
            for hp in range(rows + 8):
                lo, hi = max(0, hp - 8), min(rows - 1, hp)
                lhs = f0_ref[lo:hi + 1, cols, :].reshape((hi - lo + 1) * half, 128)
                w = win_ref[2 * t + q, hp].astype(jnp.bfloat16)
                s = lax.dot_general(lhs, w, (((1,), (1,)), ((), ())), preferred_element_type=jnp.float32)
                for h in range(lo, hi + 1):
                    a = hp - h
                    blk = s[(h - lo) * half:(h - lo + 1) * half]
                    rolled = pltpu.roll(blk, 9 + 9 * a, 1, stride=1, stride_axis=0)
                    acc_ref[h] = jnp.where(band == a, rolled, acc_ref[h])
            for i in range(rows // 2):
                pair = acc_ref[2 * i:2 * i + 2].reshape(2 * half, 128)
                energy = jnp.transpose(pair) * scale
                energy = jnp.where(valid, energy, -jnp.inf)
                top = jnp.max(energy, axis=0, keepdims=True)
                p = jnp.exp(energy - top)
                inv = 1.0 / jnp.sum(p, axis=0, keepdims=True)
                fy = jnp.sum(p * row_d, axis=0, keepdims=True) * inv * present
                fx = (jnp.sum(p * col_d, axis=0, keepdims=True) * inv + shift_t) * present
                for k in range(2):
                    out_ref[0, 2 * i + k:2 * i + k + 1, cols] = fy[:, k * half:(k + 1) * half]
                    out_ref[1, 2 * i + k:2 * i + k + 1, cols] = fx[:, k * half:(k + 1) * half]


def correlation(f0, f1rev_ext, shift, presence, sharp):
    rows, width, depth = f0.shape
    frev = jnp.pad(f1rev_ext.astype(jnp.float32), ((0, 0), (64, 8), (0, 0)))
    return pl.pallas_call(
        _corr_kernel,
        out_shape=jax.ShapeDtypeStruct((2, rows, width), jnp.float32),
        in_specs=[pl.BlockSpec(memory_space=pltpu.SMEM)] * 3
        + [pl.BlockSpec(memory_space=pltpu.VMEM), pl.BlockSpec(memory_space=pl.ANY)],
        out_specs=pl.BlockSpec(memory_space=pltpu.VMEM),
        scratch_shapes=[
            pltpu.VMEM((4, rows + 8, 128, depth), jnp.float32),
            pltpu.VMEM((rows, 64, 128), jnp.float32),
            pltpu.SemaphoreType.DMA((4,)),
        ],
    )(shift, sharp, presence, f0, frev)


def extended(array, sides, width):
    for axis, dim in sides:
        size, length = (lax.axis_size(axis), array.shape[dim])
        up = [(i, (i + 1) % size) for i in range(size - 1)]
        down = [(j, i) for i, j in up]
        last = lax.slice_in_dim(array, length - width, length, axis=dim)
        initial = lax.slice_in_dim(array, 0, width, axis=dim)
        before = lax.ppermute(last, axis, up)
        after = lax.ppermute(initial, axis, down)
        array = jnp.concatenate([before, array, after], axis=dim)
    return array


def butterfly_sum(x, axis):
    size = lax.axis_size(axis)
    if size & (size - 1):
        return lax.psum(x, axis)
    step = 1
    while step < size:
        x = x + lax.ppermute(x, axis, [(i, i ^ step) for i in range(size)])
        step *= 2
    return x


def conv_rows(field, kernel):
    return lax.conv_general_dilated(
        field,
        kernel,
        (1, 1),
        ((0, 0), (1, 1)),
        dimension_numbers=("NHWC", "HWIO", "NHWC"),
        preferred_element_type=jnp.float32,
    )


def finish_features(second_out, latter_kernel_intercept):
    shifted = second_out + latter_kernel_intercept
    return (
        shifted * lax.rsqrt(jnp.mean(shifted * shifted, axis=-1, keepdims=True) + 1e-06)
    ).astype(jnp.bfloat16)


def local(
    specimen_pair_inputs,
    initial_kernel_tensor,
    latter_kernel_tensor,
    latter_kernel_intercept,
    patch_horizontal_shift,
    specimen_presence,
    softmax_sharpening,
):
    rows_dev = specimen_pair_inputs.shape[1]
    width = specimen_pair_inputs.shape[2]
    total_rows = rows_dev * lax.axis_size("rows")
    cells_all = total_rows * width
    padded = extended(specimen_pair_inputs, (("rows", 1),), 1)
    own_rows = conv_rows(padded, initial_kernel_tensor)
    first_a = own_rows[0:1]
    first_b = own_rows[1:2]
    stats = jnp.concatenate(
        [jnp.sum(own_rows, axis=(1, 2)), jnp.sum(own_rows * own_rows, axis=(1, 2))], axis=0
    )
    stats = butterfly_sum(stats, "rows")
    total, squares = stats[0:2], stats[2:4]
    average = total / cells_all
    variance = squares / cells_all - average * average
    inv_scale = lax.rsqrt(variance + 1e-05)

    def normed(field, which):
        return jax.nn.relu((field - average[which]) * inv_scale[which])

    hidden = jnp.concatenate([normed(first_a, 0), normed(first_b, 1)], axis=0).astype(jnp.bfloat16)
    hidden_ext = extended(hidden, (("rows", 1),), 1)
    features = finish_features(conv_rows(hidden_ext, latter_kernel_tensor), latter_kernel_intercept)
    source_descriptors = features[0]
    target_reversed = extended(features[1][:, ::-1, :], (("rows", 0),), 4)
    return correlation(
        source_descriptors,
        target_reversed,
        patch_horizontal_shift,
        specimen_presence,
        softmax_sharpening,
    )


def solution(mesh):
    return jax.shard_map(
        local,
        mesh=mesh,
        in_specs=(
            P(None, ("pairs", "rows"), None, None),
            P(),
            P(),
            P(),
            P(("pairs", "rows"), None),
            P(("pairs", "rows"), None),
            P(("pairs", "rows"), None),
        ),
        out_specs=P(None, ("pairs", "rows"), None),
        check_vma=False,
    )
```

```python
import jax
import jax.numpy as jnp
from jax import lax
from jax.sharding import PartitionSpec as P
from jax.experimental import pallas as pl
from jax.experimental.pallas import tpu as pltpu

DISP = 81


def _corr_kernel(shift_ref, sharp_ref, pres_ref, f0_ref, frev_hbm, out_ref, win_ref, acc_ref, sems):
    rows = f0_ref.shape[0]
    half = f0_ref.shape[1] // 4
    copies = []
    for t in range(2):
        for q in range(2):
            start = 196 - 128 * t - half * q - shift_ref[0, t]
            cp = pltpu.make_async_copy(frev_hbm.at[:, pl.ds(start, 128), :], win_ref.at[2 * t + q],
                                       sems.at[2 * t + q])
            cp.start()
            copies.append(cp)
    lane = lax.broadcasted_iota(jnp.int32, (half, 128), 1)
    band = lane // 9
    li = lax.broadcasted_iota(jnp.int32, (128, 1), 0)
    valid = li < DISP
    row_d = jnp.where(valid, li // 9 - 4, 0).astype(jnp.float32)
    col_d = jnp.where(valid, 4 - li % 9, 0).astype(jnp.float32)
    for t in range(2):
        shift_t = shift_ref[0, t].astype(jnp.float32)
        scale = sharp_ref[0, t] / 128.0
        present = pres_ref[0, t].astype(jnp.float32)
        for q in range(2):
            cols = slice(128 * t + half * q, 128 * t + half * (q + 1))
            copies[2 * t + q].wait()
            acc_ref[...] = jnp.zeros_like(acc_ref)
            for hp in range(rows + 8):
                lo, hi = max(0, hp - 8), min(rows - 1, hp)
                lhs = f0_ref[lo:hi + 1, cols, :].reshape((hi - lo + 1) * half, 128)
                w = win_ref[2 * t + q, hp].astype(jnp.bfloat16)
                s = lax.dot_general(lhs, w, (((1,), (1,)), ((), ())), preferred_element_type=jnp.float32)
                for h in range(lo, hi + 1):
                    a = hp - h
                    blk = s[(h - lo) * half:(h - lo + 1) * half]
                    rolled = pltpu.roll(blk, 9 + 9 * a, 1, stride=1, stride_axis=0)
                    acc_ref[h] = jnp.where(band == a, rolled, acc_ref[h])
            for i in range(rows // 2):
                pair = acc_ref[2 * i:2 * i + 2].reshape(2 * half, 128)
                energy = jnp.transpose(pair) * scale
                energy = jnp.where(valid, energy, -jnp.inf)
                top = jnp.max(energy, axis=0, keepdims=True)
                p = jnp.exp(energy - top)
                inv = 1.0 / jnp.sum(p, axis=0, keepdims=True)
                fy = jnp.sum(p * row_d, axis=0, keepdims=True) * inv * present
                fx = (jnp.sum(p * col_d, axis=0, keepdims=True) * inv + shift_t) * present
                for k in range(2):
                    out_ref[0, 2 * i + k:2 * i + k + 1, cols] = fy[:, k * half:(k + 1) * half]
                    out_ref[1, 2 * i + k:2 * i + k + 1, cols] = fx[:, k * half:(k + 1) * half]


def correlation(f0, f1rev_ext, shift, presence, sharp):
    rows, width, depth = f0.shape
    frev = jnp.pad(f1rev_ext.astype(jnp.float32), ((0, 0), (64, 8), (0, 0)))
    return pl.pallas_call(
        _corr_kernel,
        out_shape=jax.ShapeDtypeStruct((2, rows, width), jnp.float32),
        in_specs=[pl.BlockSpec(memory_space=pltpu.SMEM)] * 3
        + [pl.BlockSpec(memory_space=pltpu.VMEM), pl.BlockSpec(memory_space=pl.ANY)],
        out_specs=pl.BlockSpec(memory_space=pltpu.VMEM),
        scratch_shapes=[
            pltpu.VMEM((4, rows + 8, 128, depth), jnp.float32),
            pltpu.VMEM((rows, 64, 128), jnp.float32),
            pltpu.SemaphoreType.DMA((4,)),
        ],
    )(shift, sharp, presence, f0, frev)


def extended(array, sides, width):
    for axis, dim in sides:
        size, length = (lax.axis_size(axis), array.shape[dim])
        up = [(i, (i + 1) % size) for i in range(size - 1)]
        down = [(j, i) for i, j in up]
        last = lax.slice_in_dim(array, length - width, length, axis=dim)
        initial = lax.slice_in_dim(array, 0, width, axis=dim)
        before = lax.ppermute(last, axis, up)
        after = lax.ppermute(initial, axis, down)
        array = jnp.concatenate([before, array, after], axis=dim)
    return array


def butterfly_sum(x, axis):
    size = lax.axis_size(axis)
    if size & (size - 1):
        return lax.psum(x, axis)
    step = 1
    while step < size:
        x = x + lax.ppermute(x, axis, [(i, i ^ step) for i in range(size)])
        step *= 2
    return x


def conv_rows(field, kernel):
    return lax.conv_general_dilated(
        field,
        kernel,
        (1, 1),
        ((0, 0), (1, 1)),
        dimension_numbers=("NHWC", "HWIO", "NHWC"),
        preferred_element_type=jnp.float32,
    )


def finish_features(second_out, latter_kernel_intercept):
    shifted = second_out + latter_kernel_intercept
    return (
        shifted * lax.rsqrt(jnp.mean(shifted * shifted, axis=-1, keepdims=True) + 1e-06)
    ).astype(jnp.bfloat16)


def in_map(rows_from, count, rows_dev):
    total = rows_dev * lax.axis_size("rows")
    first = lax.axis_index("rows") * rows_dev + rows_from
    row = first + lax.broadcasted_iota(jnp.int32, (count, 1, 1), 0)
    return (row >= 0) & (row < total)


def local(
    specimen_pair_inputs,
    initial_kernel_tensor,
    latter_kernel_tensor,
    latter_kernel_intercept,
    patch_horizontal_shift,
    specimen_presence,
    softmax_sharpening,
):
    x = specimen_pair_inputs
    rows_dev = x.shape[1]
    width = x.shape[2]
    size = lax.axis_size("rows")
    cells_all = rows_dev * size * width
    near, far = 2, 6
    up = [(i, i + 1) for i in range(size - 1)]
    down = [(i + 1, i) for i in range(size - 1)]
    before = lax.ppermute(
        jnp.concatenate([x[0, rows_dev - near:], x[1, rows_dev - far:]], axis=0), "rows", up
    )
    after = lax.ppermute(jnp.concatenate([x[0, :near], x[1, :far]], axis=0), "rows", down)
    b0, b1 = before[:near], before[near:]
    a0, a1 = after[:near], after[near:]
    own_in = jnp.concatenate(
        [jnp.stack([b0[-1:], b1[-1:]]), x, jnp.stack([a0[:1], a1[:1]])], axis=1
    )
    own = conv_rows(own_in, initial_kernel_tensor)
    stats = jnp.concatenate(
        [jnp.sum(own, axis=(1, 2)), jnp.sum(own * own, axis=(1, 2))], axis=0
    )
    stats = butterfly_sum(stats, "rows")
    average = stats[0:2] / cells_all
    variance = stats[2:4] / cells_all - average * average
    inv_scale = lax.rsqrt(variance + 1e-05)
    edge0 = conv_rows(
        jnp.stack([jnp.concatenate([b0, x[0, :1]]), jnp.concatenate([x[0, rows_dev - 1:], a0])]),
        initial_kernel_tensor,
    )
    edge1 = conv_rows(
        jnp.stack([jnp.concatenate([b1, x[1, :1]]), jnp.concatenate([x[1, rows_dev - 1:], a1])]),
        initial_kernel_tensor,
    )
    first0 = jnp.concatenate([edge0[0], own[0], edge0[1]], axis=0)
    first1 = jnp.concatenate([edge1[0], own[1], edge1[1]], axis=0)

    def hidden_of(field, which, rows_from):
        value = jax.nn.relu((field - average[which]) * inv_scale[which])
        value = jnp.where(in_map(rows_from, field.shape[0], rows_dev), value, 0.0)
        return value.astype(jnp.bfloat16)

    hidden0 = hidden_of(first0, 0, -1)
    hidden1 = hidden_of(first1, 1, 1 - far)
    source = finish_features(conv_rows(hidden0[None], latter_kernel_tensor)[0], latter_kernel_intercept)
    target = finish_features(conv_rows(hidden1[None], latter_kernel_tensor)[0], latter_kernel_intercept)
    target = jnp.where(in_map(2 - far, target.shape[0], rows_dev), target, jnp.zeros_like(target))
    return correlation(
        source,
        target[:, ::-1, :],
        patch_horizontal_shift,
        specimen_presence,
        softmax_sharpening,
    )


def solution(mesh):
    return jax.shard_map(
        local,
        mesh=mesh,
        in_specs=(
            P(None, ("pairs", "rows"), None, None),
            P(),
            P(),
            P(),
            P(("pairs", "rows"), None),
            P(("pairs", "rows"), None),
            P(("pairs", "rows"), None),
        ),
        out_specs=P(None, ("pairs", "rows"), None),
        check_vma=False,
    )
```

```python
import jax
import jax.numpy as jnp
from jax import lax
from jax.sharding import PartitionSpec as P
from jax.experimental import pallas as pl
from jax.experimental.pallas import tpu as pltpu

DISP = 81


def _corr_kernel(shift_ref, sharp_ref, pres_ref, f0_ref, frev_hbm, out_ref, win_ref, acc_ref, sems):
    rows = f0_ref.shape[0]
    half = f0_ref.shape[1] // 4
    copies = []
    for t in range(2):
        for q in range(2):
            start = 196 - 128 * t - half * q - shift_ref[0, t]
            cp = pltpu.make_async_copy(frev_hbm.at[:, pl.ds(start, 128), :], win_ref.at[2 * t + q],
                                       sems.at[2 * t + q])
            cp.start()
            copies.append(cp)
    lane = lax.broadcasted_iota(jnp.int32, (half, 128), 1)
    band = lane // 9
    li = lax.broadcasted_iota(jnp.int32, (128, 1), 0)
    valid = li < DISP
    row_d = jnp.where(valid, li // 9 - 4, 0).astype(jnp.float32)
    col_d = jnp.where(valid, 4 - li % 9, 0).astype(jnp.float32)
    for t in range(2):
        shift_t = shift_ref[0, t].astype(jnp.float32)
        scale = sharp_ref[0, t] / 128.0
        present = pres_ref[0, t].astype(jnp.float32)
        for q in range(2):
            cols = slice(128 * t + half * q, 128 * t + half * (q + 1))
            copies[2 * t + q].wait()
            acc_ref[...] = jnp.zeros_like(acc_ref)
            for hp in range(rows + 8):
                lo, hi = max(0, hp - 8), min(rows - 1, hp)
                lhs = f0_ref[lo:hi + 1, cols, :].reshape((hi - lo + 1) * half, 128)
                w = win_ref[2 * t + q, hp].astype(jnp.bfloat16)
                s = lax.dot_general(lhs, w, (((1,), (1,)), ((), ())), preferred_element_type=jnp.float32)
                for h in range(lo, hi + 1):
                    a = hp - h
                    blk = s[(h - lo) * half:(h - lo + 1) * half]
                    rolled = pltpu.roll(blk, 9 + 9 * a, 1, stride=1, stride_axis=0)
                    acc_ref[h] = jnp.where(band == a, rolled, acc_ref[h])
            for i in range(rows // 2):
                pair = acc_ref[2 * i:2 * i + 2].reshape(2 * half, 128)
                energy = jnp.transpose(pair) * scale
                energy = jnp.where(valid, energy, -jnp.inf)
                top = jnp.max(energy, axis=0, keepdims=True)
                p = jnp.exp(energy - top)
                inv = 1.0 / jnp.sum(p, axis=0, keepdims=True)
                fy = jnp.sum(p * row_d, axis=0, keepdims=True) * inv * present
                fx = (jnp.sum(p * col_d, axis=0, keepdims=True) * inv + shift_t) * present
                for k in range(2):
                    out_ref[0, 2 * i + k:2 * i + k + 1, cols] = fy[:, k * half:(k + 1) * half]
                    out_ref[1, 2 * i + k:2 * i + k + 1, cols] = fx[:, k * half:(k + 1) * half]


def correlation(f0, f1rev_ext, shift, presence, sharp):
    rows, width, depth = f0.shape
    frev = jnp.pad(f1rev_ext.astype(jnp.float32), ((0, 0), (64, 8), (0, 0)))
    return pl.pallas_call(
        _corr_kernel,
        out_shape=jax.ShapeDtypeStruct((2, rows, width), jnp.float32),
        in_specs=[pl.BlockSpec(memory_space=pltpu.SMEM)] * 3
        + [pl.BlockSpec(memory_space=pltpu.VMEM), pl.BlockSpec(memory_space=pl.ANY)],
        out_specs=pl.BlockSpec(memory_space=pltpu.VMEM),
        scratch_shapes=[
            pltpu.VMEM((4, rows + 8, 128, depth), jnp.float32),
            pltpu.VMEM((rows, 64, 128), jnp.float32),
            pltpu.SemaphoreType.DMA((4,)),
        ],
    )(shift, sharp, presence, f0, frev)


def extended(array, sides, width):
    for axis, dim in sides:
        size, length = (lax.axis_size(axis), array.shape[dim])
        up = [(i, (i + 1) % size) for i in range(size - 1)]
        down = [(j, i) for i, j in up]
        last = lax.slice_in_dim(array, length - width, length, axis=dim)
        initial = lax.slice_in_dim(array, 0, width, axis=dim)
        before = lax.ppermute(last, axis, up)
        after = lax.ppermute(initial, axis, down)
        array = jnp.concatenate([before, array, after], axis=dim)
    return array


def butterfly_sum(x, axis):
    size = lax.axis_size(axis)
    if size & (size - 1):
        return lax.psum(x, axis)
    step = 1
    while step < size:
        x = x + lax.ppermute(x, axis, [(i, i ^ step) for i in range(size)])
        step *= 2
    return x


def _conv_kernel(x_ref, w_ref, o_ref):
    count, rows_out, width, depth = o_ref.shape
    chunk = 4 if rows_out % 4 == 0 else (2 if rows_out % 2 == 0 else 1)
    m = chunk * width
    flat = lax.broadcasted_iota(jnp.int32, (m, depth), 0) % width
    left = flat != 0
    right = flat != width - 1
    for n in range(count):
        for r0 in range(0, rows_out, chunk):
            lhs = jnp.concatenate(
                [x_ref[n, r0 + dr:r0 + dr + chunk].reshape(m, depth) for dr in range(3)], axis=1
            )
            y = jnp.dot(lhs, w_ref[...], preferred_element_type=jnp.float32)
            out = (
                y[:, depth:2 * depth]
                + jnp.where(left, pltpu.roll(y[:, :depth], 1, 0), 0.0)
                + jnp.where(right, pltpu.roll(y[:, 2 * depth:], m - 1, 0), 0.0)
            )
            o_ref[n, r0:r0 + chunk] = out.reshape(chunk, width, depth)


def conv_rows(field, kernel):
    count, rows_in, width, depth = field.shape
    taps = jnp.transpose(kernel, (0, 2, 1, 3)).reshape(3 * depth, 3 * kernel.shape[3])
    return pl.pallas_call(
        _conv_kernel,
        out_shape=jax.ShapeDtypeStruct((count, rows_in - 2, width, kernel.shape[3]), jnp.float32),
        in_specs=[pl.BlockSpec(memory_space=pltpu.VMEM)] * 2,
        out_specs=pl.BlockSpec(memory_space=pltpu.VMEM),
    )(field, taps.astype(field.dtype))


def finish_features(second_out, latter_kernel_intercept):
    shifted = second_out + latter_kernel_intercept
    return (
        shifted * lax.rsqrt(jnp.mean(shifted * shifted, axis=-1, keepdims=True) + 1e-06)
    ).astype(jnp.bfloat16)


def in_map(rows_from, count, rows_dev):
    total = rows_dev * lax.axis_size("rows")
    first = lax.axis_index("rows") * rows_dev + rows_from
    row = first + lax.broadcasted_iota(jnp.int32, (count, 1, 1), 0)
    return (row >= 0) & (row < total)


def local(
    specimen_pair_inputs,
    initial_kernel_tensor,
    latter_kernel_tensor,
    latter_kernel_intercept,
    patch_horizontal_shift,
    specimen_presence,
    softmax_sharpening,
):
    x = specimen_pair_inputs
    rows_dev = x.shape[1]
    width = x.shape[2]
    size = lax.axis_size("rows")
    cells_all = rows_dev * size * width
    near, far = 2, 6
    up = [(i, i + 1) for i in range(size - 1)]
    down = [(i + 1, i) for i in range(size - 1)]
    before = lax.ppermute(
        jnp.concatenate([x[0, rows_dev - near:], x[1, rows_dev - far:]], axis=0), "rows", up
    )
    after = lax.ppermute(jnp.concatenate([x[0, :near], x[1, :far]], axis=0), "rows", down)
    b0, b1 = before[:near], before[near:]
    a0, a1 = after[:near], after[near:]
    own_in = jnp.concatenate(
        [jnp.stack([b0[-1:], b1[-1:]]), x, jnp.stack([a0[:1], a1[:1]])], axis=1
    )
    own = conv_rows(own_in, initial_kernel_tensor)
    stats = jnp.concatenate(
        [jnp.sum(own, axis=(1, 2)), jnp.sum(own * own, axis=(1, 2))], axis=0
    )
    stats = butterfly_sum(stats, "rows")
    average = stats[0:2] / cells_all
    variance = stats[2:4] / cells_all - average * average
    inv_scale = lax.rsqrt(variance + 1e-05)
    edge0 = conv_rows(
        jnp.stack([jnp.concatenate([b0, x[0, :1]]), jnp.concatenate([x[0, rows_dev - 1:], a0])]),
        initial_kernel_tensor,
    )
    edge1 = conv_rows(
        jnp.stack([jnp.concatenate([b1, x[1, :1]]), jnp.concatenate([x[1, rows_dev - 1:], a1])]),
        initial_kernel_tensor,
    )
    first0 = jnp.concatenate([edge0[0], own[0], edge0[1]], axis=0)
    first1 = jnp.concatenate([edge1[0], own[1], edge1[1]], axis=0)

    def hidden_of(field, which, rows_from):
        value = jax.nn.relu((field - average[which]) * inv_scale[which])
        value = jnp.where(in_map(rows_from, field.shape[0], rows_dev), value, 0.0)
        return value.astype(jnp.bfloat16)

    hidden0 = hidden_of(first0, 0, -1)
    hidden1 = hidden_of(first1, 1, 1 - far)
    source = finish_features(conv_rows(hidden0[None], latter_kernel_tensor)[0], latter_kernel_intercept)
    target = finish_features(conv_rows(hidden1[None], latter_kernel_tensor)[0], latter_kernel_intercept)
    target = jnp.where(in_map(2 - far, target.shape[0], rows_dev), target, jnp.zeros_like(target))
    return correlation(
        source,
        target[:, ::-1, :],
        patch_horizontal_shift,
        specimen_presence,
        softmax_sharpening,
    )


def solution(mesh):
    return jax.shard_map(
        local,
        mesh=mesh,
        in_specs=(
            P(None, ("pairs", "rows"), None, None),
            P(),
            P(),
            P(),
            P(("pairs", "rows"), None),
            P(("pairs", "rows"), None),
            P(("pairs", "rows"), None),
        ),
        out_specs=P(None, ("pairs", "rows"), None),
        check_vma=False,
    )
```

```python
import functools

import jax
import jax.numpy as jnp
from jax import lax
from jax.sharding import PartitionSpec as P
from jax.experimental import pallas as pl
from jax.experimental.pallas import tpu as pltpu

DISP = 81


def _corr_kernel(shift_ref, sharp_ref, pres_ref, f0_ref, frev_hbm, out_ref, win_ref, acc_ref, sems):
    rows = f0_ref.shape[0]
    half = f0_ref.shape[1] // 4
    copies = []
    for t in range(2):
        for q in range(2):
            start = 196 - 128 * t - half * q - shift_ref[0, t]
            cp = pltpu.make_async_copy(frev_hbm.at[:, pl.ds(start, 128), :], win_ref.at[2 * t + q],
                                       sems.at[2 * t + q])
            cp.start()
            copies.append(cp)
    lane = lax.broadcasted_iota(jnp.int32, (half, 128), 1)
    band = lane // 9
    li = lax.broadcasted_iota(jnp.int32, (128, 1), 0)
    valid = li < DISP
    row_d = jnp.where(valid, li // 9 - 4, 0).astype(jnp.float32)
    col_d = jnp.where(valid, 4 - li % 9, 0).astype(jnp.float32)
    for t in range(2):
        shift_t = shift_ref[0, t].astype(jnp.float32)
        scale = sharp_ref[0, t] / 128.0
        present = pres_ref[0, t].astype(jnp.float32)
        for q in range(2):
            cols = slice(128 * t + half * q, 128 * t + half * (q + 1))
            copies[2 * t + q].wait()
            acc_ref[...] = jnp.zeros_like(acc_ref)
            for hp in range(rows + 8):
                lo, hi = max(0, hp - 8), min(rows - 1, hp)
                lhs = f0_ref[lo:hi + 1, cols, :].reshape((hi - lo + 1) * half, 128)
                w = win_ref[2 * t + q, hp].astype(jnp.bfloat16)
                s = lax.dot_general(lhs, w, (((1,), (1,)), ((), ())), preferred_element_type=jnp.float32)
                for h in range(lo, hi + 1):
                    a = hp - h
                    blk = s[(h - lo) * half:(h - lo + 1) * half]
                    rolled = pltpu.roll(blk, 9 + 9 * a, 1, stride=1, stride_axis=0)
                    acc_ref[h] = jnp.where(band == a, rolled, acc_ref[h])
            for i in range(rows // 2):
                pair = acc_ref[2 * i:2 * i + 2].reshape(2 * half, 128)
                energy = jnp.transpose(pair) * scale
                energy = jnp.where(valid, energy, -jnp.inf)
                top = jnp.max(energy, axis=0, keepdims=True)
                p = jnp.exp(energy - top)
                inv = 1.0 / jnp.sum(p, axis=0, keepdims=True)
                fy = jnp.sum(p * row_d, axis=0, keepdims=True) * inv * present
                fx = (jnp.sum(p * col_d, axis=0, keepdims=True) * inv + shift_t) * present
                for k in range(2):
                    out_ref[0, 2 * i + k:2 * i + k + 1, cols] = fy[:, k * half:(k + 1) * half]
                    out_ref[1, 2 * i + k:2 * i + k + 1, cols] = fx[:, k * half:(k + 1) * half]


def correlation(f0, f1rev_ext, shift, presence, sharp):
    rows, width, depth = f0.shape
    frev = jnp.pad(f1rev_ext.astype(jnp.float32), ((0, 0), (64, 8), (0, 0)))
    return pl.pallas_call(
        _corr_kernel,
        out_shape=jax.ShapeDtypeStruct((2, rows, width), jnp.float32),
        in_specs=[pl.BlockSpec(memory_space=pltpu.SMEM)] * 3
        + [pl.BlockSpec(memory_space=pltpu.VMEM), pl.BlockSpec(memory_space=pl.ANY)],
        out_specs=pl.BlockSpec(memory_space=pltpu.VMEM),
        scratch_shapes=[
            pltpu.VMEM((4, rows + 8, 128, depth), jnp.float32),
            pltpu.VMEM((rows, 64, 128), jnp.float32),
            pltpu.SemaphoreType.DMA((4,)),
        ],
    )(shift, sharp, presence, f0, frev)


def extended(array, sides, width):
    for axis, dim in sides:
        size, length = (lax.axis_size(axis), array.shape[dim])
        up = [(i, (i + 1) % size) for i in range(size - 1)]
        down = [(j, i) for i, j in up]
        last = lax.slice_in_dim(array, length - width, length, axis=dim)
        initial = lax.slice_in_dim(array, 0, width, axis=dim)
        before = lax.ppermute(last, axis, up)
        after = lax.ppermute(initial, axis, down)
        array = jnp.concatenate([before, array, after], axis=dim)
    return array


def butterfly_sum(x, axis):
    size = lax.axis_size(axis)
    if size & (size - 1):
        return lax.psum(x, axis)
    step = 1
    while step < size:
        x = x + lax.ppermute(x, axis, [(i, i ^ step) for i in range(size)])
        step *= 2
    return x


def _conv_kernel(*refs, finish):
    if finish:
        where_ref, x_ref, w_ref, bias_ref, o_ref = refs
    else:
        x_ref, w_ref, o_ref = refs
    count, rows_out, width, depth = o_ref.shape
    chunk = 4 if rows_out % 4 == 0 else (2 if rows_out % 2 == 0 else 1)
    m = chunk * width
    flat = lax.broadcasted_iota(jnp.int32, (m, depth), 0)
    left = flat % width != 0
    right = flat % width != width - 1
    for n in range(count):
        for r0 in range(0, rows_out, chunk):
            lhs = jnp.concatenate(
                [x_ref[n, r0 + dr:r0 + dr + chunk].reshape(m, depth) for dr in range(3)], axis=1
            )
            y = jnp.dot(lhs, w_ref[...], preferred_element_type=jnp.float32)
            out = (
                y[:, depth:2 * depth]
                + jnp.where(left, pltpu.roll(y[:, :depth], 1, 0), 0.0)
                + jnp.where(right, pltpu.roll(y[:, 2 * depth:], m - 1, 0), 0.0)
            )
            if finish:
                out = out + bias_ref[...]
                ms = jnp.mean(out * out, axis=1, keepdims=True)
                out = out * lax.rsqrt(ms + 1e-06)
                row = where_ref[0] + r0 + flat[:, 0:1] // width
                out = jnp.where((row >= 0) & (row < where_ref[1]), out, 0.0)
            o_ref[n, r0:r0 + chunk] = out.reshape(chunk, width, depth).astype(o_ref.dtype)


def conv_rows(field, kernel, bias=None, first_row=None, total_rows=None):
    count, rows_in, width, depth = field.shape
    taps = jnp.transpose(kernel, (0, 2, 1, 3)).reshape(3 * depth, 3 * kernel.shape[3])
    vmem = pl.BlockSpec(memory_space=pltpu.VMEM)
    finish = bias is not None
    args = [field, taps.astype(field.dtype)]
    specs = [vmem, vmem]
    if finish:
        where = jnp.stack([first_row, total_rows]).astype(jnp.int32)
        args = [where] + args + [bias.astype(jnp.float32).reshape(1, -1)]
        specs = [pl.BlockSpec(memory_space=pltpu.SMEM)] + specs + [vmem]
    return pl.pallas_call(
        functools.partial(_conv_kernel, finish=finish),
        out_shape=jax.ShapeDtypeStruct(
            (count, rows_in - 2, width, kernel.shape[3]), jnp.bfloat16 if finish else jnp.float32
        ),
        in_specs=specs,
        out_specs=vmem,
    )(*args)


def finish_features(second_out, latter_kernel_intercept):
    shifted = second_out + latter_kernel_intercept
    return (
        shifted * lax.rsqrt(jnp.mean(shifted * shifted, axis=-1, keepdims=True) + 1e-06)
    ).astype(jnp.bfloat16)


def in_map(rows_from, count, rows_dev):
    total = rows_dev * lax.axis_size("rows")
    first = lax.axis_index("rows") * rows_dev + rows_from
    row = first + lax.broadcasted_iota(jnp.int32, (count, 1, 1), 0)
    return (row >= 0) & (row < total)


def local(
    specimen_pair_inputs,
    initial_kernel_tensor,
    latter_kernel_tensor,
    latter_kernel_intercept,
    patch_horizontal_shift,
    specimen_presence,
    softmax_sharpening,
):
    x = specimen_pair_inputs
    rows_dev = x.shape[1]
    width = x.shape[2]
    size = lax.axis_size("rows")
    cells_all = rows_dev * size * width
    near, far = 2, 6
    up = [(i, i + 1) for i in range(size - 1)]
    down = [(i + 1, i) for i in range(size - 1)]
    before = lax.ppermute(
        jnp.concatenate([x[0, rows_dev - near:], x[1, rows_dev - far:]], axis=0), "rows", up
    )
    after = lax.ppermute(jnp.concatenate([x[0, :near], x[1, :far]], axis=0), "rows", down)
    b0, b1 = before[:near], before[near:]
    a0, a1 = after[:near], after[near:]
    own_in = jnp.concatenate(
        [jnp.stack([b0[-1:], b1[-1:]]), x, jnp.stack([a0[:1], a1[:1]])], axis=1
    )
    own = conv_rows(own_in, initial_kernel_tensor)
    stats = jnp.concatenate(
        [jnp.sum(own, axis=(1, 2)), jnp.sum(own * own, axis=(1, 2))], axis=0
    )
    stats = butterfly_sum(stats, "rows")
    average = stats[0:2] / cells_all
    variance = stats[2:4] / cells_all - average * average
    inv_scale = lax.rsqrt(variance + 1e-05)
    edge0 = conv_rows(
        jnp.stack([jnp.concatenate([b0, x[0, :1]]), jnp.concatenate([x[0, rows_dev - 1:], a0])]),
        initial_kernel_tensor,
    )
    edge1 = conv_rows(
        jnp.stack([jnp.concatenate([b1, x[1, :1]]), jnp.concatenate([x[1, rows_dev - 1:], a1])]),
        initial_kernel_tensor,
    )
    first0 = jnp.concatenate([edge0[0], own[0], edge0[1]], axis=0)
    first1 = jnp.concatenate([edge1[0], own[1], edge1[1]], axis=0)

    def hidden_of(field, which, rows_from):
        value = jax.nn.relu((field - average[which]) * inv_scale[which])
        value = jnp.where(in_map(rows_from, field.shape[0], rows_dev), value, 0.0)
        return value.astype(jnp.bfloat16)

    hidden0 = hidden_of(first0, 0, -1)
    hidden1 = hidden_of(first1, 1, 1 - far)
    total = rows_dev * size
    first = lax.axis_index("rows") * rows_dev
    source = conv_rows(hidden0[None], latter_kernel_tensor, latter_kernel_intercept, first, total)[0]
    target = conv_rows(
        hidden1[None], latter_kernel_tensor, latter_kernel_intercept, first + 2 - far, total
    )[0]
    return correlation(
        source,
        target[:, ::-1, :],
        patch_horizontal_shift,
        specimen_presence,
        softmax_sharpening,
    )


def solution(mesh):
    return jax.shard_map(
        local,
        mesh=mesh,
        in_specs=(
            P(None, ("pairs", "rows"), None, None),
            P(),
            P(),
            P(),
            P(("pairs", "rows"), None),
            P(("pairs", "rows"), None),
            P(("pairs", "rows"), None),
        ),
        out_specs=P(None, ("pairs", "rows"), None),
        check_vma=False,
    )
```

```python
import functools

import jax
import jax.numpy as jnp
from jax import lax
from jax.sharding import PartitionSpec as P
from jax.experimental import pallas as pl
from jax.experimental.pallas import tpu as pltpu

DISP = 81


def _corr_kernel(shift_ref, sharp_ref, pres_ref, f0_ref, frev_hbm, out_ref, win_ref, acc_ref, sems):
    rows = f0_ref.shape[0]
    half = f0_ref.shape[1] // 4
    copies = []
    for t in range(2):
        for q in range(2):
            start = 196 - 128 * t - half * q - shift_ref[0, t]
            cp = pltpu.make_async_copy(frev_hbm.at[:, pl.ds(start, 128), :], win_ref.at[2 * t + q],
                                       sems.at[2 * t + q])
            cp.start()
            copies.append(cp)
    lane = lax.broadcasted_iota(jnp.int32, (half, 128), 1)
    band = lane // 9
    li = lax.broadcasted_iota(jnp.int32, (128, 1), 0)
    valid = li < DISP
    row_d = jnp.where(valid, li // 9 - 4, 0).astype(jnp.float32)
    col_d = jnp.where(valid, 4 - li % 9, 0).astype(jnp.float32)
    for t in range(2):
        shift_t = shift_ref[0, t].astype(jnp.float32)
        scale = sharp_ref[0, t] / 128.0
        present = pres_ref[0, t].astype(jnp.float32)
        for q in range(2):
            cols = slice(128 * t + half * q, 128 * t + half * (q + 1))
            copies[2 * t + q].wait()
            acc_ref[...] = jnp.zeros_like(acc_ref)
            for hp in range(rows + 8):
                lo, hi = max(0, hp - 8), min(rows - 1, hp)
                lhs = f0_ref[lo:hi + 1, cols, :].reshape((hi - lo + 1) * half, 128)
                w = win_ref[2 * t + q, hp].astype(jnp.bfloat16)
                s = lax.dot_general(lhs, w, (((1,), (1,)), ((), ())), preferred_element_type=jnp.float32)
                for h in range(lo, hi + 1):
                    a = hp - h
                    blk = s[(h - lo) * half:(h - lo + 1) * half]
                    rolled = pltpu.roll(blk, 9 + 9 * a, 1, stride=1, stride_axis=0)
                    acc_ref[h] = jnp.where(band == a, rolled, acc_ref[h])
            for i in range(rows // 2):
                pair = acc_ref[2 * i:2 * i + 2].reshape(2 * half, 128)
                energy = jnp.transpose(pair) * scale
                energy = jnp.where(valid, energy, -jnp.inf)
                top = jnp.max(energy, axis=0, keepdims=True)
                p = jnp.exp(energy - top)
                inv = 1.0 / jnp.sum(p, axis=0, keepdims=True)
                fy = jnp.sum(p * row_d, axis=0, keepdims=True) * inv * present
                fx = (jnp.sum(p * col_d, axis=0, keepdims=True) * inv + shift_t) * present
                for k in range(2):
                    out_ref[0, 2 * i + k:2 * i + k + 1, cols] = fy[:, k * half:(k + 1) * half]
                    out_ref[1, 2 * i + k:2 * i + k + 1, cols] = fx[:, k * half:(k + 1) * half]


def correlation(f0, f1rev_ext, shift, presence, sharp):
    rows, width, depth = f0.shape
    frev = f1rev_ext
    return pl.pallas_call(
        _corr_kernel,
        out_shape=jax.ShapeDtypeStruct((2, rows, width), jnp.float32),
        in_specs=[pl.BlockSpec(memory_space=pltpu.SMEM)] * 3
        + [pl.BlockSpec(memory_space=pltpu.VMEM), pl.BlockSpec(memory_space=pl.ANY)],
        out_specs=pl.BlockSpec(memory_space=pltpu.VMEM),
        scratch_shapes=[
            pltpu.VMEM((4, rows + 8, 128, depth), jnp.float32),
            pltpu.VMEM((rows, 64, 128), jnp.float32),
            pltpu.SemaphoreType.DMA((4,)),
        ],
    )(shift, sharp, presence, f0, frev)


def extended(array, sides, width):
    for axis, dim in sides:
        size, length = (lax.axis_size(axis), array.shape[dim])
        up = [(i, (i + 1) % size) for i in range(size - 1)]
        down = [(j, i) for i, j in up]
        last = lax.slice_in_dim(array, length - width, length, axis=dim)
        initial = lax.slice_in_dim(array, 0, width, axis=dim)
        before = lax.ppermute(last, axis, up)
        after = lax.ppermute(initial, axis, down)
        array = jnp.concatenate([before, array, after], axis=dim)
    return array


def butterfly_sum(x, axis):
    size = lax.axis_size(axis)
    if size & (size - 1):
        return lax.psum(x, axis)
    step = 1
    while step < size:
        x = x + lax.ppermute(x, axis, [(i, i ^ step) for i in range(size)])
        step *= 2
    return x


def _conv_kernel(*refs, finish, lead, trail):
    if finish:
        where_ref, x_ref, w_ref, bias_ref, o_ref = refs
    else:
        x_ref, w_ref, o_ref = refs
    count, rows_out, _, depth = o_ref.shape
    width = x_ref.shape[2]
    if lead:
        o_ref[:, :, :lead] = jnp.zeros((count, rows_out, lead, depth), o_ref.dtype)
    if trail:
        o_ref[:, :, lead + width:] = jnp.zeros((count, rows_out, trail, depth), o_ref.dtype)
    chunk = 4 if rows_out % 4 == 0 else (2 if rows_out % 2 == 0 else 1)
    m = chunk * width
    flat = lax.broadcasted_iota(jnp.int32, (m, depth), 0)
    left = flat % width != 0
    right = flat % width != width - 1
    for n in range(count):
        for r0 in range(0, rows_out, chunk):
            lhs = jnp.concatenate(
                [x_ref[n, r0 + dr:r0 + dr + chunk].reshape(m, depth) for dr in range(3)], axis=1
            )
            y = jnp.dot(lhs, w_ref[...], preferred_element_type=jnp.float32)
            out = (
                y[:, depth:2 * depth]
                + jnp.where(left, pltpu.roll(y[:, :depth], 1, 0), 0.0)
                + jnp.where(right, pltpu.roll(y[:, 2 * depth:], m - 1, 0), 0.0)
            )
            if finish:
                out = out + bias_ref[...]
                ms = jnp.mean(out * out, axis=1, keepdims=True)
                out = out * lax.rsqrt(ms + 1e-06)
                row = where_ref[0] + r0 + flat[:, 0:1] // width
                out = jnp.where((row >= 0) & (row < where_ref[1]), out, 0.0)
            o_ref[n, r0:r0 + chunk, lead:lead + width] = out.reshape(chunk, width, depth).astype(o_ref.dtype)


def conv_rows(field, kernel, bias=None, first_row=None, total_rows=None, pad=(0, 0), dtype=jnp.bfloat16):
    count, rows_in, width, depth = field.shape
    taps = jnp.transpose(kernel, (0, 2, 1, 3)).reshape(3 * depth, 3 * kernel.shape[3])
    vmem = pl.BlockSpec(memory_space=pltpu.VMEM)
    finish = bias is not None
    args = [field, taps.astype(field.dtype)]
    specs = [vmem, vmem]
    if finish:
        where = jnp.stack([first_row, total_rows]).astype(jnp.int32)
        args = [where] + args + [bias.astype(jnp.float32).reshape(1, -1)]
        specs = [pl.BlockSpec(memory_space=pltpu.SMEM)] + specs + [vmem]
    return pl.pallas_call(
        functools.partial(_conv_kernel, finish=finish, lead=pad[0], trail=pad[1]),
        out_shape=jax.ShapeDtypeStruct(
            (count, rows_in - 2, pad[0] + width + pad[1], kernel.shape[3]), dtype if finish else jnp.float32
        ),
        in_specs=specs,
        out_specs=vmem,
    )(*args)


def finish_features(second_out, latter_kernel_intercept):
    shifted = second_out + latter_kernel_intercept
    return (
        shifted * lax.rsqrt(jnp.mean(shifted * shifted, axis=-1, keepdims=True) + 1e-06)
    ).astype(jnp.bfloat16)


def in_map(rows_from, count, rows_dev):
    total = rows_dev * lax.axis_size("rows")
    first = lax.axis_index("rows") * rows_dev + rows_from
    row = first + lax.broadcasted_iota(jnp.int32, (count, 1, 1), 0)
    return (row >= 0) & (row < total)


def local(
    specimen_pair_inputs,
    initial_kernel_tensor,
    latter_kernel_tensor,
    latter_kernel_intercept,
    patch_horizontal_shift,
    specimen_presence,
    softmax_sharpening,
):
    x = specimen_pair_inputs
    rows_dev = x.shape[1]
    width = x.shape[2]
    size = lax.axis_size("rows")
    cells_all = rows_dev * size * width
    near, far = 2, 6
    up = [(i, i + 1) for i in range(size - 1)]
    down = [(i + 1, i) for i in range(size - 1)]
    before = lax.ppermute(
        jnp.concatenate([x[0, rows_dev - near:], x[1, rows_dev - far:]], axis=0), "rows", up
    )
    after = lax.ppermute(jnp.concatenate([x[0, :near], x[1, :far]], axis=0), "rows", down)
    b0, b1 = before[:near], before[near:]
    a0, a1 = after[:near], after[near:]
    own_in = jnp.concatenate(
        [jnp.stack([b0[-1:], b1[-1:]]), x, jnp.stack([a0[:1], a1[:1]])], axis=1
    )
    own = conv_rows(own_in, initial_kernel_tensor)
    stats = jnp.concatenate(
        [jnp.sum(own, axis=(1, 2)), jnp.sum(own * own, axis=(1, 2))], axis=0
    )
    stats = butterfly_sum(stats, "rows")
    average = stats[0:2] / cells_all
    variance = stats[2:4] / cells_all - average * average
    inv_scale = lax.rsqrt(variance + 1e-05)
    edge0 = conv_rows(
        jnp.stack([jnp.concatenate([b0, x[0, :1]]), jnp.concatenate([x[0, rows_dev - 1:], a0])]),
        initial_kernel_tensor,
    )
    edge1 = conv_rows(
        jnp.stack([jnp.concatenate([b1, x[1, :1]]), jnp.concatenate([x[1, rows_dev - 1:], a1])]),
        initial_kernel_tensor,
    )
    first0 = jnp.concatenate([edge0[0], own[0], edge0[1]], axis=0)
    first1 = jnp.concatenate([edge1[0], own[1], edge1[1]], axis=0)

    def hidden_of(field, which, rows_from):
        value = jax.nn.relu((field - average[which]) * inv_scale[which])
        value = jnp.where(in_map(rows_from, field.shape[0], rows_dev), value, 0.0)
        return value.astype(jnp.bfloat16)

    hidden0 = hidden_of(first0, 0, -1)
    hidden1 = hidden_of(first1, 1, 1 - far)
    total = rows_dev * size
    first = lax.axis_index("rows") * rows_dev
    source = conv_rows(hidden0[None], latter_kernel_tensor, latter_kernel_intercept, first, total)[0]
    target_reversed = conv_rows(
        hidden1[None, :, ::-1],
        latter_kernel_tensor[:, ::-1],
        latter_kernel_intercept,
        first + 2 - far,
        total,
        pad=(64, 8),
        dtype=jnp.float32,
    )[0]
    return correlation(
        source,
        target_reversed,
        patch_horizontal_shift,
        specimen_presence,
        softmax_sharpening,
    )


def solution(mesh):
    return jax.shard_map(
        local,
        mesh=mesh,
        in_specs=(
            P(None, ("pairs", "rows"), None, None),
            P(),
            P(),
            P(),
            P(("pairs", "rows"), None),
            P(("pairs", "rows"), None),
            P(("pairs", "rows"), None),
        ),
        out_specs=P(None, ("pairs", "rows"), None),
        check_vma=False,
    )
```

```python
import functools

import jax
import jax.numpy as jnp
from jax import lax
from jax.sharding import PartitionSpec as P
from jax.experimental import pallas as pl
from jax.experimental.pallas import tpu as pltpu

DISP = 81


def _corr_kernel(shift_ref, sharp_ref, pres_ref, f0_ref, frev_hbm, out_ref, win_ref, acc_ref, sems):
    rows = f0_ref.shape[0]
    half = f0_ref.shape[1] // 4
    copies = []
    for t in range(2):
        for q in range(2):
            start = 196 - 128 * t - half * q - shift_ref[0, t]
            cp = pltpu.make_async_copy(frev_hbm.at[:, pl.ds(start, 128), :], win_ref.at[2 * t + q],
                                       sems.at[2 * t + q])
            cp.start()
            copies.append(cp)
    lane = lax.broadcasted_iota(jnp.int32, (half, 128), 1)
    band = lane // 9
    li = lax.broadcasted_iota(jnp.int32, (128, 1), 0)
    valid = li < DISP
    row_d = jnp.where(valid, li // 9 - 4, 0).astype(jnp.float32)
    col_d = jnp.where(valid, 4 - li % 9, 0).astype(jnp.float32)
    for t in range(2):
        shift_t = shift_ref[0, t].astype(jnp.float32)
        scale = sharp_ref[0, t] / 128.0
        present = pres_ref[0, t].astype(jnp.float32)
        for q in range(2):
            cols = slice(128 * t + half * q, 128 * t + half * (q + 1))
            copies[2 * t + q].wait()
            acc_ref[...] = jnp.zeros_like(acc_ref)
            for hp in range(rows + 8):
                lo, hi = max(0, hp - 8), min(rows - 1, hp)
                lhs = f0_ref[lo:hi + 1, cols, :].reshape((hi - lo + 1) * half, 128)
                w = win_ref[2 * t + q, hp].astype(jnp.bfloat16)
                s = lax.dot_general(lhs, w, (((1,), (1,)), ((), ())), preferred_element_type=jnp.float32)
                for h in range(lo, hi + 1):
                    a = hp - h
                    blk = s[(h - lo) * half:(h - lo + 1) * half]
                    rolled = pltpu.roll(blk, 9 + 9 * a, 1, stride=1, stride_axis=0)
                    acc_ref[h] = jnp.where(band == a, rolled, acc_ref[h])
            for i in range(rows // 2):
                pair = acc_ref[2 * i:2 * i + 2].reshape(2 * half, 128)
                energy = jnp.transpose(pair) * scale
                energy = jnp.where(valid, energy, -jnp.inf)
                top = jnp.max(energy, axis=0, keepdims=True)
                p = jnp.exp(energy - top)
                inv = 1.0 / jnp.sum(p, axis=0, keepdims=True)
                fy = jnp.sum(p * row_d, axis=0, keepdims=True) * inv * present
                fx = (jnp.sum(p * col_d, axis=0, keepdims=True) * inv + shift_t) * present
                for k in range(2):
                    out_ref[0, 2 * i + k:2 * i + k + 1, cols] = fy[:, k * half:(k + 1) * half]
                    out_ref[1, 2 * i + k:2 * i + k + 1, cols] = fx[:, k * half:(k + 1) * half]


def correlation(f0, f1rev_ext, shift, presence, sharp):
    rows, width, depth = f0.shape
    frev = f1rev_ext
    return pl.pallas_call(
        _corr_kernel,
        out_shape=jax.ShapeDtypeStruct((2, rows, width), jnp.float32),
        in_specs=[pl.BlockSpec(memory_space=pltpu.SMEM)] * 3
        + [pl.BlockSpec(memory_space=pltpu.VMEM), pl.BlockSpec(memory_space=pl.ANY)],
        out_specs=pl.BlockSpec(memory_space=pltpu.VMEM),
        scratch_shapes=[
            pltpu.VMEM((4, rows + 8, 128, depth), jnp.float32),
            pltpu.VMEM((rows, 64, 128), jnp.float32),
            pltpu.SemaphoreType.DMA((4,)),
        ],
    )(shift, sharp, presence, f0, frev)


def extended(array, sides, width):
    for axis, dim in sides:
        size, length = (lax.axis_size(axis), array.shape[dim])
        up = [(i, (i + 1) % size) for i in range(size - 1)]
        down = [(j, i) for i, j in up]
        last = lax.slice_in_dim(array, length - width, length, axis=dim)
        initial = lax.slice_in_dim(array, 0, width, axis=dim)
        before = lax.ppermute(last, axis, up)
        after = lax.ppermute(initial, axis, down)
        array = jnp.concatenate([before, array, after], axis=dim)
    return array


def butterfly_sum(x, axis):
    size = lax.axis_size(axis)
    if size & (size - 1):
        return lax.psum(x, axis)
    step = 1
    while step < size:
        x = x + lax.ppermute(x, axis, [(i, i ^ step) for i in range(size)])
        step *= 2
    return x


def _conv_kernel(*refs, finish, lead, trail):
    if finish:
        where_ref, x_ref, w_ref, bias_ref, o_ref = refs
    else:
        x_ref, w_ref, o_ref = refs
    count, rows_out, _, depth = o_ref.shape
    width = x_ref.shape[2]
    if lead:
        o_ref[:, :, :lead] = jnp.zeros((count, rows_out, lead, depth), o_ref.dtype)
    if trail:
        o_ref[:, :, lead + width:] = jnp.zeros((count, rows_out, trail, depth), o_ref.dtype)
    chunk = 4 if rows_out % 4 == 0 else (2 if rows_out % 2 == 0 else 1)
    m = chunk * width
    flat = lax.broadcasted_iota(jnp.int32, (m, depth), 0)
    left = flat % width != 0
    right = flat % width != width - 1
    for n in range(count):
        for r0 in range(0, rows_out, chunk):
            lhs = jnp.concatenate(
                [x_ref[n, r0 + dr:r0 + dr + chunk].reshape(m, depth) for dr in range(3)], axis=1
            )
            y = jnp.dot(lhs, w_ref[n], preferred_element_type=jnp.float32)
            out = (
                y[:, depth:2 * depth]
                + jnp.where(left, pltpu.roll(y[:, :depth], 1, 0), 0.0)
                + jnp.where(right, pltpu.roll(y[:, 2 * depth:], m - 1, 0), 0.0)
            )
            if finish:
                out = out + bias_ref[...]
                ms = jnp.mean(out * out, axis=1, keepdims=True)
                out = out * lax.rsqrt(ms + 1e-06)
                row = where_ref[0] + r0 + flat[:, 0:1] // width
                out = jnp.where((row >= 0) & (row < where_ref[1]), out, 0.0)
            o_ref[n, r0:r0 + chunk, lead:lead + width] = out.reshape(chunk, width, depth).astype(o_ref.dtype)


def conv_rows(field, kernel, bias=None, first_row=None, total_rows=None, pad=(0, 0), dtype=jnp.bfloat16):
    count, rows_in, width, depth = field.shape
    if kernel.ndim == 4:
        kernel = jnp.broadcast_to(kernel, (count,) + kernel.shape)
    taps = jnp.transpose(kernel, (0, 1, 3, 2, 4)).reshape(count, 3 * depth, 3 * kernel.shape[4])
    vmem = pl.BlockSpec(memory_space=pltpu.VMEM)
    finish = bias is not None
    args = [field, taps.astype(field.dtype)]
    specs = [vmem, vmem]
    if finish:
        where = jnp.stack([first_row, total_rows]).astype(jnp.int32)
        args = [where] + args + [bias.astype(jnp.float32).reshape(1, -1)]
        specs = [pl.BlockSpec(memory_space=pltpu.SMEM)] + specs + [vmem]
    return pl.pallas_call(
        functools.partial(_conv_kernel, finish=finish, lead=pad[0], trail=pad[1]),
        out_shape=jax.ShapeDtypeStruct(
            (count, rows_in - 2, pad[0] + width + pad[1], kernel.shape[4]), dtype if finish else jnp.float32
        ),
        in_specs=specs,
        out_specs=vmem,
    )(*args)


def finish_features(second_out, latter_kernel_intercept):
    shifted = second_out + latter_kernel_intercept
    return (
        shifted * lax.rsqrt(jnp.mean(shifted * shifted, axis=-1, keepdims=True) + 1e-06)
    ).astype(jnp.bfloat16)


def in_map(rows_from, count, rows_dev):
    total = rows_dev * lax.axis_size("rows")
    first = lax.axis_index("rows") * rows_dev + rows_from
    row = first + lax.broadcasted_iota(jnp.int32, (count, 1, 1), 0)
    return (row >= 0) & (row < total)


def local(
    specimen_pair_inputs,
    initial_kernel_tensor,
    latter_kernel_tensor,
    latter_kernel_intercept,
    patch_horizontal_shift,
    specimen_presence,
    softmax_sharpening,
):
    x0 = specimen_pair_inputs[0]
    x1 = specimen_pair_inputs[1, :, ::-1]
    k1 = initial_kernel_tensor
    k1f = initial_kernel_tensor[:, ::-1]
    rows_dev = x0.shape[0]
    width = x0.shape[1]
    size = lax.axis_size("rows")
    cells_all = rows_dev * size * width
    near, far = 2, 6
    up = [(i, i + 1) for i in range(size - 1)]
    down = [(i + 1, i) for i in range(size - 1)]
    before = lax.ppermute(
        jnp.concatenate([x0[rows_dev - near:], x1[rows_dev - far:]], axis=0), "rows", up
    )
    after = lax.ppermute(jnp.concatenate([x0[:near], x1[:far]], axis=0), "rows", down)
    b0, b1 = before[:near], before[near:]
    a0, a1 = after[:near], after[near:]
    own_in = jnp.stack(
        [jnp.concatenate([b0[-1:], x0, a0[:1]]), jnp.concatenate([b1[-1:], x1, a1[:1]])]
    )
    own = conv_rows(own_in, jnp.stack([k1, k1f]))
    stats = jnp.concatenate(
        [jnp.sum(own, axis=(1, 2)), jnp.sum(own * own, axis=(1, 2))], axis=0
    )
    stats = butterfly_sum(stats, "rows")
    average = stats[0:2] / cells_all
    variance = stats[2:4] / cells_all - average * average
    inv_scale = lax.rsqrt(variance + 1e-05)
    edge0 = conv_rows(
        jnp.stack([jnp.concatenate([b0, x0[:1]]), jnp.concatenate([x0[rows_dev - 1:], a0])]), k1
    )
    edge1 = conv_rows(
        jnp.stack([jnp.concatenate([b1, x1[:1]]), jnp.concatenate([x1[rows_dev - 1:], a1])]), k1f
    )
    first0 = jnp.concatenate([edge0[0], own[0], edge0[1]], axis=0)
    first1 = jnp.concatenate([edge1[0], own[1], edge1[1]], axis=0)

    def hidden_of(field, which, rows_from):
        value = jax.nn.relu((field - average[which]) * inv_scale[which])
        value = jnp.where(in_map(rows_from, field.shape[0], rows_dev), value, 0.0)
        return value.astype(jnp.bfloat16)

    hidden0 = hidden_of(first0, 0, -1)
    hidden1 = hidden_of(first1, 1, 1 - far)
    total = rows_dev * size
    first = lax.axis_index("rows") * rows_dev
    source = conv_rows(hidden0[None], latter_kernel_tensor, latter_kernel_intercept, first, total)[0]
    target_reversed = conv_rows(
        hidden1[None],
        latter_kernel_tensor[:, ::-1],
        latter_kernel_intercept,
        first + 2 - far,
        total,
        pad=(64, 8),
        dtype=jnp.float32,
    )[0]
    return correlation(
        source,
        target_reversed,
        patch_horizontal_shift,
        specimen_presence,
        softmax_sharpening,
    )


def solution(mesh):
    return jax.shard_map(
        local,
        mesh=mesh,
        in_specs=(
            P(None, ("pairs", "rows"), None, None),
            P(),
            P(),
            P(),
            P(("pairs", "rows"), None),
            P(("pairs", "rows"), None),
            P(("pairs", "rows"), None),
        ),
        out_specs=P(None, ("pairs", "rows"), None),
        check_vma=False,
    )
```

```python
import functools

import jax
import jax.numpy as jnp
from jax import lax
from jax.sharding import PartitionSpec as P
from jax.experimental import pallas as pl
from jax.experimental.pallas import tpu as pltpu

DISP = 81


def _corr_kernel(shift_ref, sharp_ref, pres_ref, f0_ref, frev_hbm, out_ref, win_ref, acc_ref, sems):
    rows = f0_ref.shape[0]
    half = f0_ref.shape[1] // 4
    copies = []
    for t in range(2):
        for q in range(2):
            start = 196 - 128 * t - half * q - shift_ref[0, t]
            cp = pltpu.make_async_copy(frev_hbm.at[:, pl.ds(start, 128), :], win_ref.at[2 * t + q],
                                       sems.at[2 * t + q])
            cp.start()
            copies.append(cp)
    lane = lax.broadcasted_iota(jnp.int32, (half, 128), 1)
    band = lane // 9
    li = lax.broadcasted_iota(jnp.int32, (128, 1), 0)
    valid = li < DISP
    row_d = jnp.where(valid, li // 9 - 4, 0).astype(jnp.float32)
    col_d = jnp.where(valid, 4 - li % 9, 0).astype(jnp.float32)
    for t in range(2):
        shift_t = shift_ref[0, t].astype(jnp.float32)
        scale = sharp_ref[0, t] / 128.0
        present = pres_ref[0, t].astype(jnp.float32)
        for q in range(2):
            cols = slice(128 * t + half * q, 128 * t + half * (q + 1))
            copies[2 * t + q].wait()
            acc_ref[...] = jnp.zeros_like(acc_ref)
            for hp in range(rows + 8):
                lo, hi = max(0, hp - 8), min(rows - 1, hp)
                lhs = f0_ref[lo:hi + 1, cols, :].reshape((hi - lo + 1) * half, 128)
                w = win_ref[2 * t + q, hp].astype(jnp.bfloat16)
                s = lax.dot_general(lhs, w, (((1,), (1,)), ((), ())), preferred_element_type=jnp.float32)
                for h in range(lo, hi + 1):
                    a = hp - h
                    blk = s[(h - lo) * half:(h - lo + 1) * half]
                    rolled = pltpu.roll(blk, 9 + 9 * a, 1, stride=1, stride_axis=0)
                    acc_ref[h] = jnp.where(band == a, rolled, acc_ref[h])
            for i in range(rows // 2):
                pair = acc_ref[2 * i:2 * i + 2].reshape(2 * half, 128)
                energy = jnp.transpose(pair) * scale
                energy = jnp.where(valid, energy, -jnp.inf)
                top = jnp.max(energy, axis=0, keepdims=True)
                p = jnp.exp(energy - top)
                inv = 1.0 / jnp.sum(p, axis=0, keepdims=True)
                fy = jnp.sum(p * row_d, axis=0, keepdims=True) * inv * present
                fx = (jnp.sum(p * col_d, axis=0, keepdims=True) * inv + shift_t) * present
                for k in range(2):
                    out_ref[0, 2 * i + k:2 * i + k + 1, cols] = fy[:, k * half:(k + 1) * half]
                    out_ref[1, 2 * i + k:2 * i + k + 1, cols] = fx[:, k * half:(k + 1) * half]


def correlation(f0, f1rev_ext, shift, presence, sharp):
    rows, width, depth = f0.shape
    frev = f1rev_ext
    return pl.pallas_call(
        _corr_kernel,
        out_shape=jax.ShapeDtypeStruct((2, rows, width), jnp.float32),
        in_specs=[pl.BlockSpec(memory_space=pltpu.SMEM)] * 3
        + [pl.BlockSpec(memory_space=pltpu.VMEM), pl.BlockSpec(memory_space=pl.ANY)],
        out_specs=pl.BlockSpec(memory_space=pltpu.VMEM),
        scratch_shapes=[
            pltpu.VMEM((4, rows + 8, 128, depth), jnp.float32),
            pltpu.VMEM((rows, 64, 128), jnp.float32),
            pltpu.SemaphoreType.DMA((4,)),
        ],
    )(shift, sharp, presence, f0, frev)


def extended(array, sides, width):
    for axis, dim in sides:
        size, length = (lax.axis_size(axis), array.shape[dim])
        up = [(i, (i + 1) % size) for i in range(size - 1)]
        down = [(j, i) for i, j in up]
        last = lax.slice_in_dim(array, length - width, length, axis=dim)
        initial = lax.slice_in_dim(array, 0, width, axis=dim)
        before = lax.ppermute(last, axis, up)
        after = lax.ppermute(initial, axis, down)
        array = jnp.concatenate([before, array, after], axis=dim)
    return array


def butterfly_sum(x, axis):
    size = lax.axis_size(axis)
    if size & (size - 1):
        return lax.psum(x, axis)
    step = 1
    while step < size:
        x = x + lax.ppermute(x, axis, [(i, i ^ step) for i in range(size)])
        step *= 2
    return x


def _conv_kernel(*refs, finish, lead, trail, flips):
    if finish:
        where_ref, x_ref, k_ref, bias_ref, o_ref, w_ref = refs
    else:
        x_ref, k_ref, o_ref, w_ref = refs
    count, rows_out, _, depth = o_ref.shape
    width = x_ref.shape[2]
    for n, flip in enumerate(flips):
        for dr in range(3):
            for dc in range(3):
                w_ref[n, dr * depth:(dr + 1) * depth, dc * depth:(dc + 1) * depth] = k_ref[
                    dr, 2 - dc if flip else dc
                ]
    if lead:
        o_ref[:, :, :lead] = jnp.zeros((count, rows_out, lead, depth), o_ref.dtype)
    if trail:
        o_ref[:, :, lead + width:] = jnp.zeros((count, rows_out, trail, depth), o_ref.dtype)
    chunk = 4 if rows_out % 4 == 0 else (2 if rows_out % 2 == 0 else 1)
    m = chunk * width
    flat = lax.broadcasted_iota(jnp.int32, (m, depth), 0)
    left = flat % width != 0
    right = flat % width != width - 1
    for n in range(count):
        for r0 in range(0, rows_out, chunk):
            lhs = jnp.concatenate(
                [x_ref[n, r0 + dr:r0 + dr + chunk].reshape(m, depth) for dr in range(3)], axis=1
            )
            y = jnp.dot(lhs, w_ref[n], preferred_element_type=jnp.float32)
            out = (
                y[:, depth:2 * depth]
                + jnp.where(left, pltpu.roll(y[:, :depth], 1, 0), 0.0)
                + jnp.where(right, pltpu.roll(y[:, 2 * depth:], m - 1, 0), 0.0)
            )
            if finish:
                out = out + bias_ref[...]
                ms = jnp.mean(out * out, axis=1, keepdims=True)
                out = out * lax.rsqrt(ms + 1e-06)
                row = where_ref[0] + r0 + flat[:, 0:1] // width
                out = jnp.where((row >= 0) & (row < where_ref[1]), out, 0.0)
            o_ref[n, r0:r0 + chunk, lead:lead + width] = out.reshape(chunk, width, depth).astype(o_ref.dtype)


def conv_rows(field, kernel, flips, bias=None, first_row=None, total_rows=None, pad=(0, 0), dtype=jnp.bfloat16):
    count, rows_in, width, depth = field.shape
    vmem = pl.BlockSpec(memory_space=pltpu.VMEM)
    finish = bias is not None
    args = [field, kernel.astype(field.dtype)]
    specs = [vmem, vmem]
    if finish:
        where = jnp.stack([first_row, total_rows]).astype(jnp.int32)
        args = [where] + args + [bias.astype(jnp.float32).reshape(1, -1)]
        specs = [pl.BlockSpec(memory_space=pltpu.SMEM)] + specs + [vmem]
    return pl.pallas_call(
        functools.partial(_conv_kernel, finish=finish, lead=pad[0], trail=pad[1], flips=flips),
        out_shape=jax.ShapeDtypeStruct(
            (count, rows_in - 2, pad[0] + width + pad[1], kernel.shape[3]), dtype if finish else jnp.float32
        ),
        in_specs=specs,
        out_specs=vmem,
        scratch_shapes=[pltpu.VMEM((count, 3 * depth, 3 * kernel.shape[3]), field.dtype)],
    )(*args)


def finish_features(second_out, latter_kernel_intercept):
    shifted = second_out + latter_kernel_intercept
    return (
        shifted * lax.rsqrt(jnp.mean(shifted * shifted, axis=-1, keepdims=True) + 1e-06)
    ).astype(jnp.bfloat16)


def in_map(rows_from, count, rows_dev):
    total = rows_dev * lax.axis_size("rows")
    first = lax.axis_index("rows") * rows_dev + rows_from
    row = first + lax.broadcasted_iota(jnp.int32, (count, 1, 1), 0)
    return (row >= 0) & (row < total)


def local(
    specimen_pair_inputs,
    initial_kernel_tensor,
    latter_kernel_tensor,
    latter_kernel_intercept,
    patch_horizontal_shift,
    specimen_presence,
    softmax_sharpening,
):
    x0 = specimen_pair_inputs[0]
    x1 = specimen_pair_inputs[1, :, ::-1]
    k1 = initial_kernel_tensor
    rows_dev = x0.shape[0]
    width = x0.shape[1]
    size = lax.axis_size("rows")
    cells_all = rows_dev * size * width
    near, far = 2, 6
    up = [(i, i + 1) for i in range(size - 1)]
    down = [(i + 1, i) for i in range(size - 1)]
    before = lax.ppermute(
        jnp.concatenate([x0[rows_dev - near:], x1[rows_dev - far:]], axis=0), "rows", up
    )
    after = lax.ppermute(jnp.concatenate([x0[:near], x1[:far]], axis=0), "rows", down)
    b0, b1 = before[:near], before[near:]
    a0, a1 = after[:near], after[near:]
    own_in = jnp.stack(
        [jnp.concatenate([b0[-1:], x0, a0[:1]]), jnp.concatenate([b1[-1:], x1, a1[:1]])]
    )
    own = conv_rows(own_in, k1, (False, True))
    stats = jnp.concatenate(
        [jnp.sum(own, axis=(1, 2)), jnp.sum(own * own, axis=(1, 2))], axis=0
    )
    stats = butterfly_sum(stats, "rows")
    average = stats[0:2] / cells_all
    variance = stats[2:4] / cells_all - average * average
    inv_scale = lax.rsqrt(variance + 1e-05)
    edge0 = conv_rows(
        jnp.stack([jnp.concatenate([b0, x0[:1]]), jnp.concatenate([x0[rows_dev - 1:], a0])]), k1, (False, False)
    )
    edge1 = conv_rows(
        jnp.stack([jnp.concatenate([b1, x1[:1]]), jnp.concatenate([x1[rows_dev - 1:], a1])]), k1, (True, True)
    )
    first0 = jnp.concatenate([edge0[0], own[0], edge0[1]], axis=0)
    first1 = jnp.concatenate([edge1[0], own[1], edge1[1]], axis=0)

    def hidden_of(field, which, rows_from):
        value = jax.nn.relu((field - average[which]) * inv_scale[which])
        value = jnp.where(in_map(rows_from, field.shape[0], rows_dev), value, 0.0)
        return value.astype(jnp.bfloat16)

    hidden0 = hidden_of(first0, 0, -1)
    hidden1 = hidden_of(first1, 1, 1 - far)
    total = rows_dev * size
    first = lax.axis_index("rows") * rows_dev
    source = conv_rows(
        hidden0[None], latter_kernel_tensor, (False,), latter_kernel_intercept, first, total
    )[0]
    target_reversed = conv_rows(
        hidden1[None],
        latter_kernel_tensor,
        (True,),
        latter_kernel_intercept,
        first + 2 - far,
        total,
        pad=(64, 8),
        dtype=jnp.float32,
    )[0]
    return correlation(
        source,
        target_reversed,
        patch_horizontal_shift,
        specimen_presence,
        softmax_sharpening,
    )


def solution(mesh):
    return jax.shard_map(
        local,
        mesh=mesh,
        in_specs=(
            P(None, ("pairs", "rows"), None, None),
            P(),
            P(),
            P(),
            P(("pairs", "rows"), None),
            P(("pairs", "rows"), None),
            P(("pairs", "rows"), None),
        ),
        out_specs=P(None, ("pairs", "rows"), None),
        check_vma=False,
    )
```

```python
import functools

import jax
import jax.numpy as jnp
from jax import lax
from jax.sharding import PartitionSpec as P
from jax.experimental import pallas as pl
from jax.experimental.pallas import tpu as pltpu

DISP = 81


def _corr_kernel(shift_ref, sharp_ref, pres_ref, f0_ref, frev_hbm, out_ref, win_ref, acc_ref, sems):
    rows = f0_ref.shape[0]
    half = f0_ref.shape[1] // 4
    copies = []
    for t in range(2):
        for q in range(2):
            start = 196 - 128 * t - half * q - shift_ref[0, t]
            cp = pltpu.make_async_copy(frev_hbm.at[:, pl.ds(start, 128), :], win_ref.at[2 * t + q],
                                       sems.at[2 * t + q])
            cp.start()
            copies.append(cp)
    lane = lax.broadcasted_iota(jnp.int32, (half, 128), 1)
    band = lane // 9
    li = lax.broadcasted_iota(jnp.int32, (128, 1), 0)
    valid = li < DISP
    row_d = jnp.where(valid, li // 9 - 4, 0).astype(jnp.float32)
    col_d = jnp.where(valid, 4 - li % 9, 0).astype(jnp.float32)
    for t in range(2):
        shift_t = shift_ref[0, t].astype(jnp.float32)
        scale = sharp_ref[0, t] / 128.0
        present = pres_ref[0, t].astype(jnp.float32)
        for q in range(2):
            cols = slice(128 * t + half * q, 128 * t + half * (q + 1))
            copies[2 * t + q].wait()
            acc_ref[...] = jnp.zeros_like(acc_ref)
            for hp in range(rows + 8):
                lo, hi = max(0, hp - 8), min(rows - 1, hp)
                lhs = f0_ref[lo:hi + 1, cols, :].reshape((hi - lo + 1) * half, 128)
                w = win_ref[2 * t + q, hp].astype(jnp.bfloat16)
                s = lax.dot_general(lhs, w, (((1,), (1,)), ((), ())), preferred_element_type=jnp.float32)
                for h in range(lo, hi + 1):
                    a = hp - h
                    blk = s[(h - lo) * half:(h - lo + 1) * half]
                    rolled = pltpu.roll(blk, 9 + 9 * a, 1, stride=1, stride_axis=0)
                    acc_ref[h] = jnp.where(band == a, rolled, acc_ref[h])
            for i in range(rows // 2):
                pair = acc_ref[2 * i:2 * i + 2].reshape(2 * half, 128)
                energy = jnp.transpose(pair) * scale
                energy = jnp.where(valid, energy, -jnp.inf)
                top = jnp.max(energy, axis=0, keepdims=True)
                p = jnp.exp(energy - top)
                inv = 1.0 / jnp.sum(p, axis=0, keepdims=True)
                fy = jnp.sum(p * row_d, axis=0, keepdims=True) * inv * present
                fx = (jnp.sum(p * col_d, axis=0, keepdims=True) * inv + shift_t) * present
                for k in range(2):
                    out_ref[0, 2 * i + k:2 * i + k + 1, cols] = fy[:, k * half:(k + 1) * half]
                    out_ref[1, 2 * i + k:2 * i + k + 1, cols] = fx[:, k * half:(k + 1) * half]


def correlation(f0, f1rev_ext, shift, presence, sharp):
    rows, width, depth = f0.shape
    frev = f1rev_ext
    return pl.pallas_call(
        _corr_kernel,
        out_shape=jax.ShapeDtypeStruct((2, rows, width), jnp.float32),
        in_specs=[pl.BlockSpec(memory_space=pltpu.SMEM)] * 3
        + [pl.BlockSpec(memory_space=pltpu.VMEM), pl.BlockSpec(memory_space=pl.ANY)],
        out_specs=pl.BlockSpec(memory_space=pltpu.VMEM),
        scratch_shapes=[
            pltpu.VMEM((4, rows + 8, 128, depth), jnp.float32),
            pltpu.VMEM((rows, 64, 128), jnp.float32),
            pltpu.SemaphoreType.DMA((4,)),
        ],
    )(shift, sharp, presence, f0, frev)


def extended(array, sides, width):
    for axis, dim in sides:
        size, length = (lax.axis_size(axis), array.shape[dim])
        up = [(i, (i + 1) % size) for i in range(size - 1)]
        down = [(j, i) for i, j in up]
        last = lax.slice_in_dim(array, length - width, length, axis=dim)
        initial = lax.slice_in_dim(array, 0, width, axis=dim)
        before = lax.ppermute(last, axis, up)
        after = lax.ppermute(initial, axis, down)
        array = jnp.concatenate([before, array, after], axis=dim)
    return array


def butterfly_sum(x, axis, held):
    size = lax.axis_size(axis)
    if size & (size - 1):
        return lax.psum(x, axis), held
    step = 1
    while step < size:
        x = x + lax.ppermute(x, axis, [(i, i ^ step) for i in range(size)])
        if step == 1:
            x, held = lax.optimization_barrier((x, held))
        step *= 2
    return x, held


def _conv_kernel(*refs, finish, lead, trail, flips):
    if finish:
        where_ref, x_ref, k_ref, bias_ref, o_ref, w_ref = refs
    else:
        x_ref, k_ref, o_ref, w_ref = refs
    count, rows_out, _, depth = o_ref.shape
    width = x_ref.shape[2]
    for n, flip in enumerate(flips):
        for dr in range(3):
            for dc in range(3):
                w_ref[n, dr * depth:(dr + 1) * depth, dc * depth:(dc + 1) * depth] = k_ref[
                    dr, 2 - dc if flip else dc
                ]
    if lead:
        o_ref[:, :, :lead] = jnp.zeros((count, rows_out, lead, depth), o_ref.dtype)
    if trail:
        o_ref[:, :, lead + width:] = jnp.zeros((count, rows_out, trail, depth), o_ref.dtype)
    chunk = 4 if rows_out % 4 == 0 else (2 if rows_out % 2 == 0 else 1)
    m = chunk * width
    flat = lax.broadcasted_iota(jnp.int32, (m, depth), 0)
    left = flat % width != 0
    right = flat % width != width - 1
    for n in range(count):
        for r0 in range(0, rows_out, chunk):
            lhs = jnp.concatenate(
                [x_ref[n, r0 + dr:r0 + dr + chunk].reshape(m, depth) for dr in range(3)], axis=1
            )
            y = jnp.dot(lhs, w_ref[n], preferred_element_type=jnp.float32)
            out = (
                y[:, depth:2 * depth]
                + jnp.where(left, pltpu.roll(y[:, :depth], 1, 0), 0.0)
                + jnp.where(right, pltpu.roll(y[:, 2 * depth:], m - 1, 0), 0.0)
            )
            if finish:
                out = out + bias_ref[...]
                ms = jnp.mean(out * out, axis=1, keepdims=True)
                out = out * lax.rsqrt(ms + 1e-06)
                row = where_ref[0] + r0 + flat[:, 0:1] // width
                out = jnp.where((row >= 0) & (row < where_ref[1]), out, 0.0)
            o_ref[n, r0:r0 + chunk, lead:lead + width] = out.reshape(chunk, width, depth).astype(o_ref.dtype)


def conv_rows(field, kernel, flips, bias=None, first_row=None, total_rows=None, pad=(0, 0), dtype=jnp.bfloat16):
    count, rows_in, width, depth = field.shape
    vmem = pl.BlockSpec(memory_space=pltpu.VMEM)
    finish = bias is not None
    args = [field, kernel.astype(field.dtype)]
    specs = [vmem, vmem]
    if finish:
        where = jnp.stack([first_row, total_rows]).astype(jnp.int32)
        args = [where] + args + [bias.astype(jnp.float32).reshape(1, -1)]
        specs = [pl.BlockSpec(memory_space=pltpu.SMEM)] + specs + [vmem]
    return pl.pallas_call(
        functools.partial(_conv_kernel, finish=finish, lead=pad[0], trail=pad[1], flips=flips),
        out_shape=jax.ShapeDtypeStruct(
            (count, rows_in - 2, pad[0] + width + pad[1], kernel.shape[3]), dtype if finish else jnp.float32
        ),
        in_specs=specs,
        out_specs=vmem,
        scratch_shapes=[pltpu.VMEM((count, 3 * depth, 3 * kernel.shape[3]), field.dtype)],
    )(*args)


def finish_features(second_out, latter_kernel_intercept):
    shifted = second_out + latter_kernel_intercept
    return (
        shifted * lax.rsqrt(jnp.mean(shifted * shifted, axis=-1, keepdims=True) + 1e-06)
    ).astype(jnp.bfloat16)


def in_map(rows_from, count, rows_dev):
    total = rows_dev * lax.axis_size("rows")
    first = lax.axis_index("rows") * rows_dev + rows_from
    row = first + lax.broadcasted_iota(jnp.int32, (count, 1, 1), 0)
    return (row >= 0) & (row < total)


def local(
    specimen_pair_inputs,
    initial_kernel_tensor,
    latter_kernel_tensor,
    latter_kernel_intercept,
    patch_horizontal_shift,
    specimen_presence,
    softmax_sharpening,
):
    x0 = specimen_pair_inputs[0]
    x1 = specimen_pair_inputs[1, :, ::-1]
    k1 = initial_kernel_tensor
    rows_dev = x0.shape[0]
    width = x0.shape[1]
    size = lax.axis_size("rows")
    cells_all = rows_dev * size * width
    near, far = 2, 6
    up = [(i, i + 1) for i in range(size - 1)]
    down = [(i + 1, i) for i in range(size - 1)]
    before = lax.ppermute(
        jnp.concatenate([x0[rows_dev - near:], x1[rows_dev - far:]], axis=0), "rows", up
    )
    after = lax.ppermute(jnp.concatenate([x0[:near], x1[:far]], axis=0), "rows", down)
    b0, b1 = before[:near], before[near:]
    a0, a1 = after[:near], after[near:]
    interior = conv_rows(jnp.stack([x0, x1]), k1, (False, True))
    boundary = conv_rows(
        jnp.stack(
            [
                jnp.concatenate([b0[-1:], x0[:2]]),
                jnp.concatenate([x0[rows_dev - 2:], a0[:1]]),
                jnp.concatenate([b1[-1:], x1[:2]]),
                jnp.concatenate([x1[rows_dev - 2:], a1[:1]]),
            ]
        ),
        k1,
        (False, False, True, True),
    )
    stats = jnp.concatenate(
        [
            jnp.sum(interior, axis=(1, 2)) + jnp.sum(boundary.reshape(2, 2, width, -1), axis=(1, 2)),
            jnp.sum(interior * interior, axis=(1, 2))
            + jnp.sum(jnp.square(boundary).reshape(2, 2, width, -1), axis=(1, 2)),
        ],
        axis=0,
    )
    halo_in = (
        jnp.stack([jnp.concatenate([b0, x0[:1]]), jnp.concatenate([x0[rows_dev - 1:], a0])]),
        jnp.stack([jnp.concatenate([b1, x1[:1]]), jnp.concatenate([x1[rows_dev - 1:], a1])]),
    )
    stats, halo_in = butterfly_sum(stats, "rows", halo_in)
    average = stats[0:2] / cells_all
    variance = stats[2:4] / cells_all - average * average
    inv_scale = lax.rsqrt(variance + 1e-05)
    edge0 = conv_rows(halo_in[0], k1, (False, False))
    edge1 = conv_rows(halo_in[1], k1, (True, True))
    first0 = jnp.concatenate([edge0[0], boundary[0], interior[0], boundary[1], edge0[1]], axis=0)
    first1 = jnp.concatenate([edge1[0], boundary[2], interior[1], boundary[3], edge1[1]], axis=0)

    def hidden_of(field, which, rows_from):
        value = jax.nn.relu((field - average[which]) * inv_scale[which])
        value = jnp.where(in_map(rows_from, field.shape[0], rows_dev), value, 0.0)
        return value.astype(jnp.bfloat16)

    hidden0 = hidden_of(first0, 0, -1)
    hidden1 = hidden_of(first1, 1, 1 - far)
    total = rows_dev * size
    first = lax.axis_index("rows") * rows_dev
    source = conv_rows(
        hidden0[None], latter_kernel_tensor, (False,), latter_kernel_intercept, first, total
    )[0]
    target_reversed = conv_rows(
        hidden1[None],
        latter_kernel_tensor,
        (True,),
        latter_kernel_intercept,
        first + 2 - far,
        total,
        pad=(64, 8),
        dtype=jnp.float32,
    )[0]
    return correlation(
        source,
        target_reversed,
        patch_horizontal_shift,
        specimen_presence,
        softmax_sharpening,
    )


def solution(mesh):
    return jax.shard_map(
        local,
        mesh=mesh,
        in_specs=(
            P(None, ("pairs", "rows"), None, None),
            P(),
            P(),
            P(),
            P(("pairs", "rows"), None),
            P(("pairs", "rows"), None),
            P(("pairs", "rows"), None),
        ),
        out_specs=P(None, ("pairs", "rows"), None),
        check_vma=False,
    )
```

```python
import functools

import jax
import jax.numpy as jnp
from jax import lax
from jax.sharding import PartitionSpec as P
from jax.experimental import pallas as pl
from jax.experimental.pallas import tpu as pltpu

DISP = 81


def _corr_kernel(shift_ref, sharp_ref, pres_ref, f0_ref, frev_hbm, out_ref, win_ref, acc_ref, sems):
    rows = f0_ref.shape[0]
    half = f0_ref.shape[1] // 4
    copies = []
    for t in range(2):
        for q in range(2):
            start = 196 - 128 * t - half * q - shift_ref[0, t]
            cp = pltpu.make_async_copy(frev_hbm.at[:, pl.ds(start, 128), :], win_ref.at[2 * t + q],
                                       sems.at[2 * t + q])
            cp.start()
            copies.append(cp)
    lane = lax.broadcasted_iota(jnp.int32, (half, 128), 1)
    band = lane // 9
    li = lax.broadcasted_iota(jnp.int32, (128, 1), 0)
    valid = li < DISP
    row_d = jnp.where(valid, li // 9 - 4, 0).astype(jnp.float32)
    col_d = jnp.where(valid, 4 - li % 9, 0).astype(jnp.float32)
    for t in range(2):
        shift_t = shift_ref[0, t].astype(jnp.float32)
        scale = sharp_ref[0, t] / 128.0
        present = pres_ref[0, t].astype(jnp.float32)
        for q in range(2):
            cols = slice(128 * t + half * q, 128 * t + half * (q + 1))
            copies[2 * t + q].wait()
            acc_ref[...] = jnp.zeros_like(acc_ref)
            for hp in range(rows + 8):
                lo, hi = max(0, hp - 8), min(rows - 1, hp)
                lhs = f0_ref[lo:hi + 1, cols, :].reshape((hi - lo + 1) * half, 128)
                w = win_ref[2 * t + q, hp].astype(jnp.bfloat16)
                s = lax.dot_general(lhs, w, (((1,), (1,)), ((), ())), preferred_element_type=jnp.float32)
                for h in range(lo, hi + 1):
                    a = hp - h
                    blk = s[(h - lo) * half:(h - lo + 1) * half]
                    rolled = pltpu.roll(blk, 9 + 9 * a, 1, stride=1, stride_axis=0)
                    acc_ref[h] = jnp.where(band == a, rolled, acc_ref[h])
            for i in range(rows // 2):
                pair = acc_ref[2 * i:2 * i + 2].reshape(2 * half, 128)
                energy = jnp.transpose(pair) * scale
                energy = jnp.where(valid, energy, -jnp.inf)
                top = jnp.max(energy, axis=0, keepdims=True)
                p = jnp.exp(energy - top)
                inv = 1.0 / jnp.sum(p, axis=0, keepdims=True)
                fy = jnp.sum(p * row_d, axis=0, keepdims=True) * inv * present
                fx = (jnp.sum(p * col_d, axis=0, keepdims=True) * inv + shift_t) * present
                for k in range(2):
                    out_ref[0, 2 * i + k:2 * i + k + 1, cols] = fy[:, k * half:(k + 1) * half]
                    out_ref[1, 2 * i + k:2 * i + k + 1, cols] = fx[:, k * half:(k + 1) * half]


def correlation(f0, f1rev_ext, shift, presence, sharp):
    rows, width, depth = f0.shape
    frev = f1rev_ext
    return pl.pallas_call(
        _corr_kernel,
        out_shape=jax.ShapeDtypeStruct((2, rows, width), jnp.float32),
        in_specs=[pl.BlockSpec(memory_space=pltpu.SMEM)] * 3
        + [pl.BlockSpec(memory_space=pltpu.VMEM), pl.BlockSpec(memory_space=pl.ANY)],
        out_specs=pl.BlockSpec(memory_space=pltpu.VMEM),
        scratch_shapes=[
            pltpu.VMEM((4, rows + 8, 128, depth), jnp.float32),
            pltpu.VMEM((rows, 64, 128), jnp.float32),
            pltpu.SemaphoreType.DMA((4,)),
        ],
    )(shift, sharp, presence, f0, frev)


def extended(array, sides, width):
    for axis, dim in sides:
        size, length = (lax.axis_size(axis), array.shape[dim])
        up = [(i, (i + 1) % size) for i in range(size - 1)]
        down = [(j, i) for i, j in up]
        last = lax.slice_in_dim(array, length - width, length, axis=dim)
        initial = lax.slice_in_dim(array, 0, width, axis=dim)
        before = lax.ppermute(last, axis, up)
        after = lax.ppermute(initial, axis, down)
        array = jnp.concatenate([before, array, after], axis=dim)
    return array


def butterfly_sum(x, axis, held):
    size = lax.axis_size(axis)
    if size & (size - 1):
        return lax.psum(x, axis), held
    step = 1
    while step < size:
        x = x + lax.ppermute(x, axis, [(i, i ^ step) for i in range(size)])
        if step == 1:
            x, held = lax.optimization_barrier((x, held))
        step *= 2
    return x, held


def _conv_kernel(*refs, finish, lead, trail, flips, plan):
    if plan:
        where_ref, *sources, mean_ref, inv_ref, k_ref, bias_ref, o_ref, w_ref, x_ref = refs
        for r, (which, n, row) in enumerate(plan):
            value = jnp.maximum((sources[which][n, row] - mean_ref[...]) * inv_ref[...], 0.0)
            g = where_ref[2] + r
            keep = (g >= 0) & (g < where_ref[1])
            x_ref[0, r] = jnp.where(keep, value, 0.0).astype(x_ref.dtype)
    elif finish:
        where_ref, x_ref, k_ref, bias_ref, o_ref, w_ref = refs
    else:
        x_ref, k_ref, o_ref, w_ref = refs
    count, rows_out, _, depth = o_ref.shape
    width = x_ref.shape[2]
    for n, flip in enumerate(flips):
        for dr in range(3):
            for dc in range(3):
                w_ref[n, dr * depth:(dr + 1) * depth, dc * depth:(dc + 1) * depth] = k_ref[
                    dr, 2 - dc if flip else dc
                ]
    if lead:
        o_ref[:, :, :lead] = jnp.zeros((count, rows_out, lead, depth), o_ref.dtype)
    if trail:
        o_ref[:, :, lead + width:] = jnp.zeros((count, rows_out, trail, depth), o_ref.dtype)
    chunk = 4 if rows_out % 4 == 0 else (2 if rows_out % 2 == 0 else 1)
    m = chunk * width
    flat = lax.broadcasted_iota(jnp.int32, (m, depth), 0)
    left = flat % width != 0
    right = flat % width != width - 1
    for n in range(count):
        for r0 in range(0, rows_out, chunk):
            lhs = jnp.concatenate(
                [x_ref[n, r0 + dr:r0 + dr + chunk].reshape(m, depth) for dr in range(3)], axis=1
            )
            y = jnp.dot(lhs, w_ref[n], preferred_element_type=jnp.float32)
            out = (
                y[:, depth:2 * depth]
                + jnp.where(left, pltpu.roll(y[:, :depth], 1, 0), 0.0)
                + jnp.where(right, pltpu.roll(y[:, 2 * depth:], m - 1, 0), 0.0)
            )
            if finish:
                out = out + bias_ref[...]
                ms = jnp.mean(out * out, axis=1, keepdims=True)
                out = out * lax.rsqrt(ms + 1e-06)
                row = where_ref[0] + r0 + flat[:, 0:1] // width
                out = jnp.where((row >= 0) & (row < where_ref[1]), out, 0.0)
            o_ref[n, r0:r0 + chunk, lead:lead + width] = out.reshape(chunk, width, depth).astype(o_ref.dtype)


def conv_rows(field, kernel, flips, bias=None, first_row=None, total_rows=None, pad=(0, 0), dtype=jnp.bfloat16):
    count, rows_in, width, depth = field.shape
    vmem = pl.BlockSpec(memory_space=pltpu.VMEM)
    finish = bias is not None
    args = [field, kernel.astype(field.dtype)]
    specs = [vmem, vmem]
    if finish:
        where = jnp.stack([first_row, total_rows]).astype(jnp.int32)
        args = [where] + args + [bias.astype(jnp.float32).reshape(1, -1)]
        specs = [pl.BlockSpec(memory_space=pltpu.SMEM)] + specs + [vmem]
    return pl.pallas_call(
        functools.partial(_conv_kernel, finish=finish, lead=pad[0], trail=pad[1], flips=flips, plan=None),
        out_shape=jax.ShapeDtypeStruct(
            (count, rows_in - 2, pad[0] + width + pad[1], kernel.shape[3]), dtype if finish else jnp.float32
        ),
        in_specs=specs,
        out_specs=vmem,
        scratch_shapes=[pltpu.VMEM((count, 3 * depth, 3 * kernel.shape[3]), field.dtype)],
    )(*args)


def conv_hidden(sources, plan, mean, inv_scale, kernel, flips, bias, first_in, total_rows, pad=(0, 0),
                dtype=jnp.bfloat16):
    rows_in = len(plan)
    width, depth = sources[0].shape[2], sources[0].shape[3]
    vmem = pl.BlockSpec(memory_space=pltpu.VMEM)
    where = jnp.stack([first_in + 1, total_rows, first_in]).astype(jnp.int32)
    args = [where, *sources, mean.reshape(1, -1), inv_scale.reshape(1, -1),
            kernel.astype(jnp.bfloat16), bias.astype(jnp.float32).reshape(1, -1)]
    specs = [pl.BlockSpec(memory_space=pltpu.SMEM)] + [vmem] * (len(sources) + 4)
    return pl.pallas_call(
        functools.partial(_conv_kernel, finish=True, lead=pad[0], trail=pad[1], flips=flips, plan=plan),
        out_shape=jax.ShapeDtypeStruct((1, rows_in - 2, pad[0] + width + pad[1], kernel.shape[3]), dtype),
        in_specs=specs,
        out_specs=vmem,
        scratch_shapes=[
            pltpu.VMEM((1, 3 * depth, 3 * kernel.shape[3]), jnp.bfloat16),
            pltpu.VMEM((1, rows_in, width, depth), jnp.bfloat16),
        ],
    )(*args)


def finish_features(second_out, latter_kernel_intercept):
    shifted = second_out + latter_kernel_intercept
    return (
        shifted * lax.rsqrt(jnp.mean(shifted * shifted, axis=-1, keepdims=True) + 1e-06)
    ).astype(jnp.bfloat16)


def in_map(rows_from, count, rows_dev):
    total = rows_dev * lax.axis_size("rows")
    first = lax.axis_index("rows") * rows_dev + rows_from
    row = first + lax.broadcasted_iota(jnp.int32, (count, 1, 1), 0)
    return (row >= 0) & (row < total)


def local(
    specimen_pair_inputs,
    initial_kernel_tensor,
    latter_kernel_tensor,
    latter_kernel_intercept,
    patch_horizontal_shift,
    specimen_presence,
    softmax_sharpening,
):
    x0 = specimen_pair_inputs[0]
    x1 = specimen_pair_inputs[1, :, ::-1]
    k1 = initial_kernel_tensor
    rows_dev = x0.shape[0]
    width = x0.shape[1]
    size = lax.axis_size("rows")
    cells_all = rows_dev * size * width
    near, far = 2, 6
    up = [(i, i + 1) for i in range(size - 1)]
    down = [(i + 1, i) for i in range(size - 1)]
    before = lax.ppermute(
        jnp.concatenate([x0[rows_dev - near:], x1[rows_dev - far:]], axis=0), "rows", up
    )
    after = lax.ppermute(jnp.concatenate([x0[:near], x1[:far]], axis=0), "rows", down)
    b0, b1 = before[:near], before[near:]
    a0, a1 = after[:near], after[near:]
    interior = conv_rows(jnp.stack([x0, x1]), k1, (False, True))
    boundary = conv_rows(
        jnp.stack(
            [
                jnp.concatenate([b0[-1:], x0[:2]]),
                jnp.concatenate([x0[rows_dev - 2:], a0[:1]]),
                jnp.concatenate([b1[-1:], x1[:2]]),
                jnp.concatenate([x1[rows_dev - 2:], a1[:1]]),
            ]
        ),
        k1,
        (False, False, True, True),
    )
    stats = jnp.concatenate(
        [
            jnp.sum(interior, axis=(1, 2)) + jnp.sum(boundary.reshape(2, 2, width, -1), axis=(1, 2)),
            jnp.sum(interior * interior, axis=(1, 2))
            + jnp.sum(jnp.square(boundary).reshape(2, 2, width, -1), axis=(1, 2)),
        ],
        axis=0,
    )
    halo_in = (
        jnp.stack([jnp.concatenate([b0, x0[:1]]), jnp.concatenate([x0[rows_dev - 1:], a0])]),
        jnp.stack([jnp.concatenate([b1, x1[:1]]), jnp.concatenate([x1[rows_dev - 1:], a1])]),
    )
    stats, halo_in = butterfly_sum(stats, "rows", halo_in)
    average = stats[0:2] / cells_all
    variance = stats[2:4] / cells_all - average * average
    inv_scale = lax.rsqrt(variance + 1e-05)
    edge0 = conv_rows(halo_in[0], k1, (False, False))
    edge1 = conv_rows(halo_in[1], k1, (True, True))
    sources = (edge0, boundary, interior, edge1)
    plan0 = ((0, 0, 0), (1, 0, 0)) + tuple((2, 0, r) for r in range(rows_dev - 2)) + ((1, 1, 0), (0, 1, 0))
    halo = far - 1
    plan1 = (
        tuple((3, 0, r) for r in range(halo))
        + ((1, 2, 0),)
        + tuple((2, 1, r) for r in range(rows_dev - 2))
        + ((1, 3, 0),)
        + tuple((3, 1, r) for r in range(halo))
    )
    total = rows_dev * size
    first = lax.axis_index("rows") * rows_dev
    source = conv_hidden(
        sources, plan0, average[0], inv_scale[0], latter_kernel_tensor, (False,),
        latter_kernel_intercept, first - 1, total,
    )[0]
    target_reversed = conv_hidden(
        sources, plan1, average[1], inv_scale[1], latter_kernel_tensor, (True,),
        latter_kernel_intercept, first - halo, total, pad=(64, 8), dtype=jnp.float32,
    )[0]
    return correlation(
        source,
        target_reversed,
        patch_horizontal_shift,
        specimen_presence,
        softmax_sharpening,
    )


def solution(mesh):
    return jax.shard_map(
        local,
        mesh=mesh,
        in_specs=(
            P(None, ("pairs", "rows"), None, None),
            P(),
            P(),
            P(),
            P(("pairs", "rows"), None),
            P(("pairs", "rows"), None),
            P(("pairs", "rows"), None),
        ),
        out_specs=P(None, ("pairs", "rows"), None),
        check_vma=False,
    )
```

```python
import functools

import jax
import jax.numpy as jnp
from jax import lax
from jax.sharding import PartitionSpec as P
from jax.experimental import pallas as pl
from jax.experimental.pallas import tpu as pltpu

DISP = 81


def _corr_kernel(shift_ref, sharp_ref, pres_ref, f0_ref, frev_hbm, out_ref, win_ref, acc_ref, sems):
    rows = f0_ref.shape[0]
    half = f0_ref.shape[1] // 4
    copies = []
    for t in range(2):
        for q in range(2):
            start = 196 - 128 * t - half * q - shift_ref[0, t]
            cp = pltpu.make_async_copy(frev_hbm.at[:, pl.ds(start, 128), :], win_ref.at[2 * t + q],
                                       sems.at[2 * t + q])
            cp.start()
            copies.append(cp)
    lane = lax.broadcasted_iota(jnp.int32, (half, 128), 1)
    band = lane // 9
    li = lax.broadcasted_iota(jnp.int32, (128, 1), 0)
    valid = li < DISP
    row_d = jnp.where(valid, li // 9 - 4, 0).astype(jnp.float32)
    col_d = jnp.where(valid, 4 - li % 9, 0).astype(jnp.float32)
    for t in range(2):
        shift_t = shift_ref[0, t].astype(jnp.float32)
        scale = sharp_ref[0, t] / 128.0
        present = pres_ref[0, t].astype(jnp.float32)
        for q in range(2):
            cols = slice(128 * t + half * q, 128 * t + half * (q + 1))
            copies[2 * t + q].wait()
            acc_ref[...] = jnp.zeros_like(acc_ref)
            for hp in range(rows + 8):
                lo, hi = max(0, hp - 8), min(rows - 1, hp)
                lhs = f0_ref[lo:hi + 1, cols, :].reshape((hi - lo + 1) * half, 128)
                w = win_ref[2 * t + q, hp].astype(jnp.bfloat16)
                s = lax.dot_general(lhs, w, (((1,), (1,)), ((), ())), preferred_element_type=jnp.float32)
                for h in range(lo, hi + 1):
                    a = hp - h
                    blk = s[(h - lo) * half:(h - lo + 1) * half]
                    rolled = pltpu.roll(blk, 9 + 9 * a, 1, stride=1, stride_axis=0)
                    acc_ref[h] = jnp.where(band == a, rolled, acc_ref[h])
            for i in range(rows // 2):
                pair = acc_ref[2 * i:2 * i + 2].reshape(2 * half, 128)
                energy = jnp.transpose(pair) * scale
                energy = jnp.where(valid, energy, -jnp.inf)
                top = jnp.max(energy, axis=0, keepdims=True)
                p = jnp.exp(energy - top)
                inv = 1.0 / jnp.sum(p, axis=0, keepdims=True)
                fy = jnp.sum(p * row_d, axis=0, keepdims=True) * inv * present
                fx = (jnp.sum(p * col_d, axis=0, keepdims=True) * inv + shift_t) * present
                for k in range(2):
                    out_ref[0, 2 * i + k:2 * i + k + 1, cols] = fy[:, k * half:(k + 1) * half]
                    out_ref[1, 2 * i + k:2 * i + k + 1, cols] = fx[:, k * half:(k + 1) * half]


def correlation(f0, f1rev_ext, shift, presence, sharp):
    rows, width, depth = f0.shape
    frev = f1rev_ext
    return pl.pallas_call(
        _corr_kernel,
        out_shape=jax.ShapeDtypeStruct((2, rows, width), jnp.float32),
        in_specs=[pl.BlockSpec(memory_space=pltpu.SMEM)] * 3
        + [pl.BlockSpec(memory_space=pltpu.VMEM), pl.BlockSpec(memory_space=pl.ANY)],
        out_specs=pl.BlockSpec(memory_space=pltpu.VMEM),
        scratch_shapes=[
            pltpu.VMEM((4, rows + 8, 128, depth), jnp.float32),
            pltpu.VMEM((rows, 64, 128), jnp.float32),
            pltpu.SemaphoreType.DMA((4,)),
        ],
    )(shift, sharp, presence, f0, frev)


def extended(array, sides, width):
    for axis, dim in sides:
        size, length = (lax.axis_size(axis), array.shape[dim])
        up = [(i, (i + 1) % size) for i in range(size - 1)]
        down = [(j, i) for i, j in up]
        last = lax.slice_in_dim(array, length - width, length, axis=dim)
        initial = lax.slice_in_dim(array, 0, width, axis=dim)
        before = lax.ppermute(last, axis, up)
        after = lax.ppermute(initial, axis, down)
        array = jnp.concatenate([before, array, after], axis=dim)
    return array


def butterfly_sum(x, axis, held):
    size = lax.axis_size(axis)
    if size & (size - 1):
        return lax.psum(x, axis), held
    step = 1
    while step < size:
        x = x + lax.ppermute(x, axis, [(i, i ^ step) for i in range(size)])
        if step == 1:
            x, held = lax.optimization_barrier((x, held))
        step *= 2
    return x, held


def _conv_kernel(*refs, finish, lead, trail, flips, plan, gather=None):
    if gather:
        *sources, k_ref, o_ref, w_ref, x_ref = refs
        for n, rows in enumerate(gather):
            for r, (which, index) in enumerate(rows):
                x_ref[n, r] = sources[which][index]
    elif plan:
        where_ref, *sources, mean_ref, inv_ref, k_ref, bias_ref, o_ref, w_ref, x_ref = refs
        for r, (which, n, row) in enumerate(plan):
            value = jnp.maximum((sources[which][n, row] - mean_ref[...]) * inv_ref[...], 0.0)
            g = where_ref[2] + r
            keep = (g >= 0) & (g < where_ref[1])
            x_ref[0, r] = jnp.where(keep, value, 0.0).astype(x_ref.dtype)
    elif finish:
        where_ref, x_ref, k_ref, bias_ref, o_ref, w_ref = refs
    else:
        x_ref, k_ref, o_ref, w_ref = refs
    count, rows_out, _, depth = o_ref.shape
    width = x_ref.shape[2]
    for n, flip in enumerate(flips):
        for dr in range(3):
            for dc in range(3):
                w_ref[n, dr * depth:(dr + 1) * depth, dc * depth:(dc + 1) * depth] = k_ref[
                    dr, 2 - dc if flip else dc
                ]
    if lead:
        o_ref[:, :, :lead] = jnp.zeros((count, rows_out, lead, depth), o_ref.dtype)
    if trail:
        o_ref[:, :, lead + width:] = jnp.zeros((count, rows_out, trail, depth), o_ref.dtype)
    chunk = 4 if rows_out % 4 == 0 else (2 if rows_out % 2 == 0 else 1)
    m = chunk * width
    flat = lax.broadcasted_iota(jnp.int32, (m, depth), 0)
    left = flat % width != 0
    right = flat % width != width - 1
    for n in range(count):
        for r0 in range(0, rows_out, chunk):
            lhs = jnp.concatenate(
                [x_ref[n, r0 + dr:r0 + dr + chunk].reshape(m, depth) for dr in range(3)], axis=1
            )
            y = jnp.dot(lhs, w_ref[n], preferred_element_type=jnp.float32)
            out = (
                y[:, depth:2 * depth]
                + jnp.where(left, pltpu.roll(y[:, :depth], 1, 0), 0.0)
                + jnp.where(right, pltpu.roll(y[:, 2 * depth:], m - 1, 0), 0.0)
            )
            if finish:
                out = out + bias_ref[...]
                ms = jnp.mean(out * out, axis=1, keepdims=True)
                out = out * lax.rsqrt(ms + 1e-06)
                row = where_ref[0] + r0 + flat[:, 0:1] // width
                out = jnp.where((row >= 0) & (row < where_ref[1]), out, 0.0)
            o_ref[n, r0:r0 + chunk, lead:lead + width] = out.reshape(chunk, width, depth).astype(o_ref.dtype)


def conv_rows(field, kernel, flips, bias=None, first_row=None, total_rows=None, pad=(0, 0), dtype=jnp.bfloat16):
    count, rows_in, width, depth = field.shape
    vmem = pl.BlockSpec(memory_space=pltpu.VMEM)
    finish = bias is not None
    args = [field, kernel.astype(field.dtype)]
    specs = [vmem, vmem]
    if finish:
        where = jnp.stack([first_row, total_rows]).astype(jnp.int32)
        args = [where] + args + [bias.astype(jnp.float32).reshape(1, -1)]
        specs = [pl.BlockSpec(memory_space=pltpu.SMEM)] + specs + [vmem]
    return pl.pallas_call(
        functools.partial(_conv_kernel, finish=finish, lead=pad[0], trail=pad[1], flips=flips, plan=None),
        out_shape=jax.ShapeDtypeStruct(
            (count, rows_in - 2, pad[0] + width + pad[1], kernel.shape[3]), dtype if finish else jnp.float32
        ),
        in_specs=specs,
        out_specs=vmem,
        scratch_shapes=[pltpu.VMEM((count, 3 * depth, 3 * kernel.shape[3]), field.dtype)],
    )(*args)


def conv_gather(sources, gather, kernel, flips):
    count, rows_in = len(gather), len(gather[0])
    width, depth = sources[0].shape[-2], sources[0].shape[-1]
    vmem = pl.BlockSpec(memory_space=pltpu.VMEM)
    return pl.pallas_call(
        functools.partial(_conv_kernel, finish=False, lead=0, trail=0, flips=flips, plan=None, gather=gather),
        out_shape=jax.ShapeDtypeStruct((count, rows_in - 2, width, kernel.shape[3]), jnp.float32),
        in_specs=[vmem] * (len(sources) + 1),
        out_specs=vmem,
        scratch_shapes=[
            pltpu.VMEM((count, 3 * depth, 3 * kernel.shape[3]), jnp.bfloat16),
            pltpu.VMEM((count, rows_in, width, depth), jnp.bfloat16),
        ],
    )(*sources, kernel.astype(jnp.bfloat16))


def conv_hidden(sources, plan, mean, inv_scale, kernel, flips, bias, first_in, total_rows, pad=(0, 0),
                dtype=jnp.bfloat16):
    rows_in = len(plan)
    width, depth = sources[0].shape[2], sources[0].shape[3]
    vmem = pl.BlockSpec(memory_space=pltpu.VMEM)
    where = jnp.stack([first_in + 1, total_rows, first_in]).astype(jnp.int32)
    args = [where, *sources, mean.reshape(1, -1), inv_scale.reshape(1, -1),
            kernel.astype(jnp.bfloat16), bias.astype(jnp.float32).reshape(1, -1)]
    specs = [pl.BlockSpec(memory_space=pltpu.SMEM)] + [vmem] * (len(sources) + 4)
    return pl.pallas_call(
        functools.partial(_conv_kernel, finish=True, lead=pad[0], trail=pad[1], flips=flips, plan=plan),
        out_shape=jax.ShapeDtypeStruct((1, rows_in - 2, pad[0] + width + pad[1], kernel.shape[3]), dtype),
        in_specs=specs,
        out_specs=vmem,
        scratch_shapes=[
            pltpu.VMEM((1, 3 * depth, 3 * kernel.shape[3]), jnp.bfloat16),
            pltpu.VMEM((1, rows_in, width, depth), jnp.bfloat16),
        ],
    )(*args)


def finish_features(second_out, latter_kernel_intercept):
    shifted = second_out + latter_kernel_intercept
    return (
        shifted * lax.rsqrt(jnp.mean(shifted * shifted, axis=-1, keepdims=True) + 1e-06)
    ).astype(jnp.bfloat16)


def in_map(rows_from, count, rows_dev):
    total = rows_dev * lax.axis_size("rows")
    first = lax.axis_index("rows") * rows_dev + rows_from
    row = first + lax.broadcasted_iota(jnp.int32, (count, 1, 1), 0)
    return (row >= 0) & (row < total)


def local(
    specimen_pair_inputs,
    initial_kernel_tensor,
    latter_kernel_tensor,
    latter_kernel_intercept,
    patch_horizontal_shift,
    specimen_presence,
    softmax_sharpening,
):
    x0 = specimen_pair_inputs[0]
    x1 = specimen_pair_inputs[1, :, ::-1]
    k1 = initial_kernel_tensor
    rows_dev = x0.shape[0]
    width = x0.shape[1]
    size = lax.axis_size("rows")
    cells_all = rows_dev * size * width
    near, far = 2, 6
    up = [(i, i + 1) for i in range(size - 1)]
    down = [(i + 1, i) for i in range(size - 1)]
    before = lax.ppermute(
        jnp.concatenate([x0[rows_dev - near:], x1[rows_dev - far:]], axis=0), "rows", up
    )
    after = lax.ppermute(jnp.concatenate([x0[:near], x1[:far]], axis=0), "rows", down)

    def row0(r):
        if r < 0:
            return (2, (near + r,))
        if r >= rows_dev:
            return (3, (r - rows_dev,))
        return (0, (0, r))

    def row1(r):
        if r < 0:
            return (2, (near + far + r,))
        if r >= rows_dev:
            return (3, (near + r - rows_dev,))
        return (1, (r,))

    def rows_of(pick, lo, hi):
        return tuple(pick(r) for r in range(lo, hi))

    inputs = (specimen_pair_inputs, x1)
    halos = (specimen_pair_inputs, x1, before, after)
    interior = conv_gather(inputs, (rows_of(row0, 0, rows_dev), rows_of(row1, 0, rows_dev)), k1, (False, True))
    boundary = conv_gather(
        halos,
        (
            rows_of(row0, -1, 2),
            rows_of(row0, rows_dev - 2, rows_dev + 1),
            rows_of(row1, -1, 2),
            rows_of(row1, rows_dev - 2, rows_dev + 1),
        ),
        k1,
        (False, False, True, True),
    )
    stats = jnp.concatenate(
        [
            jnp.sum(interior, axis=(1, 2)) + jnp.sum(boundary.reshape(2, 2, width, -1), axis=(1, 2)),
            jnp.sum(interior * interior, axis=(1, 2))
            + jnp.sum(jnp.square(boundary).reshape(2, 2, width, -1), axis=(1, 2)),
        ],
        axis=0,
    )
    stats, halos = butterfly_sum(stats, "rows", halos)
    average = stats[0:2] / cells_all
    variance = stats[2:4] / cells_all - average * average
    inv_scale = lax.rsqrt(variance + 1e-05)
    edge0 = conv_gather(
        halos, (rows_of(row0, -near, 1), rows_of(row0, rows_dev - 1, rows_dev + near)), k1, (False, False)
    )
    edge1 = conv_gather(
        halos, (rows_of(row1, -far, 1), rows_of(row1, rows_dev - 1, rows_dev + far)), k1, (True, True)
    )
    sources = (edge0, boundary, interior, edge1)
    plan0 = ((0, 0, 0), (1, 0, 0)) + tuple((2, 0, r) for r in range(rows_dev - 2)) + ((1, 1, 0), (0, 1, 0))
    halo = far - 1
    plan1 = (
        tuple((3, 0, r) for r in range(halo))
        + ((1, 2, 0),)
        + tuple((2, 1, r) for r in range(rows_dev - 2))
        + ((1, 3, 0),)
        + tuple((3, 1, r) for r in range(halo))
    )
    total = rows_dev * size
    first = lax.axis_index("rows") * rows_dev
    source = conv_hidden(
        sources, plan0, average[0], inv_scale[0], latter_kernel_tensor, (False,),
        latter_kernel_intercept, first - 1, total,
    )[0]
    target_reversed = conv_hidden(
        sources, plan1, average[1], inv_scale[1], latter_kernel_tensor, (True,),
        latter_kernel_intercept, first - halo, total, pad=(64, 8), dtype=jnp.float32,
    )[0]
    return correlation(
        source,
        target_reversed,
        patch_horizontal_shift,
        specimen_presence,
        softmax_sharpening,
    )


def solution(mesh):
    return jax.shard_map(
        local,
        mesh=mesh,
        in_specs=(
            P(None, ("pairs", "rows"), None, None),
            P(),
            P(),
            P(),
            P(("pairs", "rows"), None),
            P(("pairs", "rows"), None),
            P(("pairs", "rows"), None),
        ),
        out_specs=P(None, ("pairs", "rows"), None),
        check_vma=False,
    )
```

```python
import functools

import jax
import jax.numpy as jnp
from jax import lax
from jax.sharding import PartitionSpec as P
from jax.experimental import pallas as pl
from jax.experimental.pallas import tpu as pltpu

DISP = 81


def _corr_kernel(shift_ref, sharp_ref, pres_ref, f0_ref, frev_hbm, out_ref, win_ref, acc_ref, sems):
    rows = f0_ref.shape[0]
    half = f0_ref.shape[1] // 4
    copies = []
    for t in range(2):
        for q in range(2):
            start = 196 - 128 * t - half * q - shift_ref[0, t]
            cp = pltpu.make_async_copy(frev_hbm.at[:, pl.ds(start, 128), :], win_ref.at[2 * t + q],
                                       sems.at[2 * t + q])
            cp.start()
            copies.append(cp)
    lane = lax.broadcasted_iota(jnp.int32, (half, 128), 1)
    band = lane // 9
    li = lax.broadcasted_iota(jnp.int32, (128, 1), 0)
    valid = li < DISP
    row_d = jnp.where(valid, li // 9 - 4, 0).astype(jnp.float32)
    col_d = jnp.where(valid, 4 - li % 9, 0).astype(jnp.float32)
    for t in range(2):
        shift_t = shift_ref[0, t].astype(jnp.float32)
        scale = sharp_ref[0, t] / 128.0
        present = pres_ref[0, t].astype(jnp.float32)
        for q in range(2):
            cols = slice(128 * t + half * q, 128 * t + half * (q + 1))
            copies[2 * t + q].wait()
            acc_ref[...] = jnp.zeros_like(acc_ref)
            for hp in range(rows + 8):
                lo, hi = max(0, hp - 8), min(rows - 1, hp)
                lhs = f0_ref[lo:hi + 1, cols, :].reshape((hi - lo + 1) * half, 128)
                w = win_ref[2 * t + q, hp].astype(jnp.bfloat16)
                s = lax.dot_general(lhs, w, (((1,), (1,)), ((), ())), preferred_element_type=jnp.float32)
                for h in range(lo, hi + 1):
                    a = hp - h
                    blk = s[(h - lo) * half:(h - lo + 1) * half]
                    rolled = pltpu.roll(blk, 9 + 9 * a, 1, stride=1, stride_axis=0)
                    acc_ref[h] = jnp.where(band == a, rolled, acc_ref[h])
            for i in range(rows // 2):
                pair = acc_ref[2 * i:2 * i + 2].reshape(2 * half, 128)
                energy = jnp.transpose(pair) * scale
                energy = jnp.where(valid, energy, -jnp.inf)
                top = jnp.max(energy, axis=0, keepdims=True)
                p = jnp.exp(energy - top)
                inv = 1.0 / jnp.sum(p, axis=0, keepdims=True)
                fy = jnp.sum(p * row_d, axis=0, keepdims=True) * inv * present
                fx = (jnp.sum(p * col_d, axis=0, keepdims=True) * inv + shift_t) * present
                for k in range(2):
                    out_ref[0, 2 * i + k:2 * i + k + 1, cols] = fy[:, k * half:(k + 1) * half]
                    out_ref[1, 2 * i + k:2 * i + k + 1, cols] = fx[:, k * half:(k + 1) * half]


def correlation(f0, f1rev_ext, shift, presence, sharp):
    rows, width, depth = f0.shape
    frev = f1rev_ext
    return pl.pallas_call(
        _corr_kernel,
        out_shape=jax.ShapeDtypeStruct((2, rows, width), jnp.float32),
        in_specs=[pl.BlockSpec(memory_space=pltpu.SMEM)] * 3
        + [pl.BlockSpec(memory_space=pltpu.VMEM), pl.BlockSpec(memory_space=pl.ANY)],
        out_specs=pl.BlockSpec(memory_space=pltpu.VMEM),
        scratch_shapes=[
            pltpu.VMEM((4, rows + 8, 128, depth), jnp.float32),
            pltpu.VMEM((rows, 64, 128), jnp.float32),
            pltpu.SemaphoreType.DMA((4,)),
        ],
    )(shift, sharp, presence, f0, frev)


def extended(array, sides, width):
    for axis, dim in sides:
        size, length = (lax.axis_size(axis), array.shape[dim])
        up = [(i, (i + 1) % size) for i in range(size - 1)]
        down = [(j, i) for i, j in up]
        last = lax.slice_in_dim(array, length - width, length, axis=dim)
        initial = lax.slice_in_dim(array, 0, width, axis=dim)
        before = lax.ppermute(last, axis, up)
        after = lax.ppermute(initial, axis, down)
        array = jnp.concatenate([before, array, after], axis=dim)
    return array


def butterfly_sum(x, axis, held):
    size = lax.axis_size(axis)
    if size & (size - 1):
        return lax.psum(x, axis), held
    step = 1
    while step < size:
        x = x + lax.ppermute(x, axis, [(i, i ^ step) for i in range(size)])
        if step == 1:
            x, held = lax.optimization_barrier((x, held))
        step *= 2
    return x, held


def _conv_kernel(*refs, finish, lead, trail, flips, plan, gather=None):
    if gather:
        *sources, k_ref, o_ref, w_ref, x_ref = refs
        for n, rows in enumerate(gather):
            for r, (which, index) in enumerate(rows):
                x_ref[n, r] = sources[which][index].astype(x_ref.dtype)
    elif plan:
        where_ref, *sources, mean_ref, inv_ref, k_ref, bias_ref, o_ref, w_ref, x_ref = refs
        for r, (which, n, row) in enumerate(plan):
            value = jnp.maximum((sources[which][n, row] - mean_ref[...]) * inv_ref[...], 0.0)
            g = where_ref[2] + r
            keep = (g >= 0) & (g < where_ref[1])
            x_ref[0, r] = jnp.where(keep, value, 0.0).astype(x_ref.dtype)
    elif finish:
        where_ref, x_ref, k_ref, bias_ref, o_ref, w_ref = refs
    else:
        x_ref, k_ref, o_ref, w_ref = refs
    count, rows_out, _, depth = o_ref.shape
    width = x_ref.shape[2]
    for n, flip in enumerate(flips):
        for dr in range(3):
            for dc in range(3):
                w_ref[n, dr * depth:(dr + 1) * depth, dc * depth:(dc + 1) * depth] = k_ref[
                    dr, 2 - dc if flip else dc
                ]
    if lead:
        o_ref[:, :, :lead] = jnp.zeros((count, rows_out, lead, depth), o_ref.dtype)
    if trail:
        o_ref[:, :, lead + width:] = jnp.zeros((count, rows_out, trail, depth), o_ref.dtype)
    chunk = 4 if rows_out % 4 == 0 else (2 if rows_out % 2 == 0 else 1)
    m = chunk * width
    flat = lax.broadcasted_iota(jnp.int32, (m, depth), 0)
    left = flat % width != 0
    right = flat % width != width - 1
    for n in range(count):
        for r0 in range(0, rows_out, chunk):
            lhs = jnp.concatenate(
                [x_ref[n, r0 + dr:r0 + dr + chunk].reshape(m, depth) for dr in range(3)], axis=1
            )
            y = jnp.dot(lhs, w_ref[n], preferred_element_type=jnp.float32)
            out = (
                y[:, depth:2 * depth]
                + jnp.where(left, pltpu.roll(y[:, :depth], 1, 0), 0.0)
                + jnp.where(right, pltpu.roll(y[:, 2 * depth:], m - 1, 0), 0.0)
            )
            if finish:
                out = out + bias_ref[...]
                ms = jnp.mean(out * out, axis=1, keepdims=True)
                out = out * lax.rsqrt(ms + 1e-06)
                row = where_ref[0] + r0 + flat[:, 0:1] // width
                out = jnp.where((row >= 0) & (row < where_ref[1]), out, 0.0)
            o_ref[n, r0:r0 + chunk, lead:lead + width] = out.reshape(chunk, width, depth).astype(o_ref.dtype)


def conv_rows(field, kernel, flips, bias=None, first_row=None, total_rows=None, pad=(0, 0), dtype=jnp.bfloat16):
    count, rows_in, width, depth = field.shape
    vmem = pl.BlockSpec(memory_space=pltpu.VMEM)
    finish = bias is not None
    args = [field, kernel.astype(field.dtype)]
    specs = [vmem, vmem]
    if finish:
        where = jnp.stack([first_row, total_rows]).astype(jnp.int32)
        args = [where] + args + [bias.astype(jnp.float32).reshape(1, -1)]
        specs = [pl.BlockSpec(memory_space=pltpu.SMEM)] + specs + [vmem]
    return pl.pallas_call(
        functools.partial(_conv_kernel, finish=finish, lead=pad[0], trail=pad[1], flips=flips, plan=None),
        out_shape=jax.ShapeDtypeStruct(
            (count, rows_in - 2, pad[0] + width + pad[1], kernel.shape[3]), dtype if finish else jnp.float32
        ),
        in_specs=specs,
        out_specs=vmem,
        scratch_shapes=[pltpu.VMEM((count, 3 * depth, 3 * kernel.shape[3]), field.dtype)],
    )(*args)


def conv_gather(sources, gather, kernel, flips):
    count, rows_in = len(gather), len(gather[0])
    width, depth = sources[0].shape[-2], sources[0].shape[-1]
    vmem = pl.BlockSpec(memory_space=pltpu.VMEM)
    return pl.pallas_call(
        functools.partial(_conv_kernel, finish=False, lead=0, trail=0, flips=flips, plan=None, gather=gather),
        out_shape=jax.ShapeDtypeStruct((count, rows_in - 2, width, kernel.shape[3]), jnp.float32),
        in_specs=[vmem] * (len(sources) + 1),
        out_specs=vmem,
        scratch_shapes=[
            pltpu.VMEM((count, 3 * depth, 3 * kernel.shape[3]), jnp.bfloat16),
            pltpu.VMEM((count, rows_in, width, depth), jnp.bfloat16),
        ],
    )(*sources, kernel.astype(jnp.bfloat16))


def conv_hidden(sources, plan, mean, inv_scale, kernel, flips, bias, first_in, total_rows, pad=(0, 0),
                dtype=jnp.bfloat16):
    rows_in = len(plan)
    width, depth = sources[0].shape[2], sources[0].shape[3]
    vmem = pl.BlockSpec(memory_space=pltpu.VMEM)
    where = jnp.stack([first_in + 1, total_rows, first_in]).astype(jnp.int32)
    args = [where, *sources, mean.reshape(1, -1), inv_scale.reshape(1, -1),
            kernel.astype(jnp.bfloat16), bias.astype(jnp.float32).reshape(1, -1)]
    specs = [pl.BlockSpec(memory_space=pltpu.SMEM)] + [vmem] * (len(sources) + 4)
    return pl.pallas_call(
        functools.partial(_conv_kernel, finish=True, lead=pad[0], trail=pad[1], flips=flips, plan=plan),
        out_shape=jax.ShapeDtypeStruct((1, rows_in - 2, pad[0] + width + pad[1], kernel.shape[3]), dtype),
        in_specs=specs,
        out_specs=vmem,
        scratch_shapes=[
            pltpu.VMEM((1, 3 * depth, 3 * kernel.shape[3]), jnp.bfloat16),
            pltpu.VMEM((1, rows_in, width, depth), jnp.bfloat16),
        ],
    )(*args)


def finish_features(second_out, latter_kernel_intercept):
    shifted = second_out + latter_kernel_intercept
    return (
        shifted * lax.rsqrt(jnp.mean(shifted * shifted, axis=-1, keepdims=True) + 1e-06)
    ).astype(jnp.bfloat16)


def in_map(rows_from, count, rows_dev):
    total = rows_dev * lax.axis_size("rows")
    first = lax.axis_index("rows") * rows_dev + rows_from
    row = first + lax.broadcasted_iota(jnp.int32, (count, 1, 1), 0)
    return (row >= 0) & (row < total)


def local(
    specimen_pair_inputs,
    initial_kernel_tensor,
    latter_kernel_tensor,
    latter_kernel_intercept,
    patch_horizontal_shift,
    specimen_presence,
    softmax_sharpening,
):
    x0 = specimen_pair_inputs[0]
    x1 = specimen_pair_inputs[1].astype(jnp.float32)[:, ::-1]
    k1 = initial_kernel_tensor
    rows_dev = x0.shape[0]
    width = x0.shape[1]
    size = lax.axis_size("rows")
    cells_all = rows_dev * size * width
    near, far = 2, 6
    up = [(i, i + 1) for i in range(size - 1)]
    down = [(i + 1, i) for i in range(size - 1)]
    before = lax.ppermute(
        jnp.concatenate([x0[rows_dev - near:], x1[rows_dev - far:].astype(x0.dtype)], axis=0), "rows", up
    )
    after = lax.ppermute(
        jnp.concatenate([x0[:near], x1[:far].astype(x0.dtype)], axis=0), "rows", down
    )

    def row0(r):
        if r < 0:
            return (2, (near + r,))
        if r >= rows_dev:
            return (3, (r - rows_dev,))
        return (0, (0, r))

    def row1(r):
        if r < 0:
            return (2, (near + far + r,))
        if r >= rows_dev:
            return (3, (near + r - rows_dev,))
        return (1, (r,))

    def rows_of(pick, lo, hi):
        return tuple(pick(r) for r in range(lo, hi))

    inputs = (specimen_pair_inputs, x1)
    halos = (specimen_pair_inputs, x1, before, after)
    interior = conv_gather(inputs, (rows_of(row0, 0, rows_dev), rows_of(row1, 0, rows_dev)), k1, (False, True))
    boundary = conv_gather(
        halos,
        (
            rows_of(row0, -1, 2),
            rows_of(row0, rows_dev - 2, rows_dev + 1),
            rows_of(row1, -1, 2),
            rows_of(row1, rows_dev - 2, rows_dev + 1),
        ),
        k1,
        (False, False, True, True),
    )
    stats = jnp.concatenate(
        [
            jnp.sum(interior, axis=(1, 2)) + jnp.sum(boundary.reshape(2, 2, width, -1), axis=(1, 2)),
            jnp.sum(interior * interior, axis=(1, 2))
            + jnp.sum(jnp.square(boundary).reshape(2, 2, width, -1), axis=(1, 2)),
        ],
        axis=0,
    )
    stats, halos = butterfly_sum(stats, "rows", halos)
    average = stats[0:2] / cells_all
    variance = stats[2:4] / cells_all - average * average
    inv_scale = lax.rsqrt(variance + 1e-05)
    edge0 = conv_gather(
        halos, (rows_of(row0, -near, 1), rows_of(row0, rows_dev - 1, rows_dev + near)), k1, (False, False)
    )
    edge1 = conv_gather(
        halos, (rows_of(row1, -far, 1), rows_of(row1, rows_dev - 1, rows_dev + far)), k1, (True, True)
    )
    sources = (edge0, boundary, interior, edge1)
    plan0 = ((0, 0, 0), (1, 0, 0)) + tuple((2, 0, r) for r in range(rows_dev - 2)) + ((1, 1, 0), (0, 1, 0))
    halo = far - 1
    plan1 = (
        tuple((3, 0, r) for r in range(halo))
        + ((1, 2, 0),)
        + tuple((2, 1, r) for r in range(rows_dev - 2))
        + ((1, 3, 0),)
        + tuple((3, 1, r) for r in range(halo))
    )
    total = rows_dev * size
    first = lax.axis_index("rows") * rows_dev
    source = conv_hidden(
        sources, plan0, average[0], inv_scale[0], latter_kernel_tensor, (False,),
        latter_kernel_intercept, first - 1, total,
    )[0]
    target_reversed = conv_hidden(
        sources, plan1, average[1], inv_scale[1], latter_kernel_tensor, (True,),
        latter_kernel_intercept, first - halo, total, pad=(64, 8), dtype=jnp.float32,
    )[0]
    return correlation(
        source,
        target_reversed,
        patch_horizontal_shift,
        specimen_presence,
        softmax_sharpening,
    )


def solution(mesh):
    return jax.shard_map(
        local,
        mesh=mesh,
        in_specs=(
            P(None, ("pairs", "rows"), None, None),
            P(),
            P(),
            P(),
            P(("pairs", "rows"), None),
            P(("pairs", "rows"), None),
            P(("pairs", "rows"), None),
        ),
        out_specs=P(None, ("pairs", "rows"), None),
        check_vma=False,
    )
```

```python
import functools

import jax
import jax.numpy as jnp
from jax import lax
from jax.sharding import PartitionSpec as P
from jax.experimental import pallas as pl
from jax.experimental.pallas import tpu as pltpu

DISP = 81


def _corr_kernel(shift_ref, sharp_ref, pres_ref, f0_ref, frev_hbm, out_ref, win_ref, acc_ref, sems):
    rows = f0_ref.shape[0]
    half = f0_ref.shape[1] // 4
    copies = []
    for t in range(2):
        for q in range(2):
            start = 196 - 128 * t - half * q - shift_ref[0, t]
            cp = pltpu.make_async_copy(frev_hbm.at[:, pl.ds(start, 128), :], win_ref.at[2 * t + q],
                                       sems.at[2 * t + q])
            cp.start()
            copies.append(cp)
    lane = lax.broadcasted_iota(jnp.int32, (half, 128), 1)
    band = lane // 9
    li = lax.broadcasted_iota(jnp.int32, (128, 1), 0)
    valid = li < DISP
    row_d = jnp.where(valid, li // 9 - 4, 0).astype(jnp.float32)
    col_d = jnp.where(valid, 4 - li % 9, 0).astype(jnp.float32)
    for t in range(2):
        shift_t = shift_ref[0, t].astype(jnp.float32)
        scale = sharp_ref[0, t] / 128.0
        present = pres_ref[0, t].astype(jnp.float32)
        for q in range(2):
            cols = slice(128 * t + half * q, 128 * t + half * (q + 1))
            copies[2 * t + q].wait()
            acc_ref[...] = jnp.zeros_like(acc_ref)
            for hp in range(rows + 8):
                lo, hi = max(0, hp - 8), min(rows - 1, hp)
                lhs = f0_ref[lo:hi + 1, cols, :].reshape((hi - lo + 1) * half, 128)
                w = win_ref[2 * t + q, hp].astype(jnp.bfloat16)
                s = lax.dot_general(lhs, w, (((1,), (1,)), ((), ())), preferred_element_type=jnp.float32)
                for h in range(lo, hi + 1):
                    a = hp - h
                    blk = s[(h - lo) * half:(h - lo + 1) * half]
                    rolled = pltpu.roll(blk, 9 + 9 * a, 1, stride=1, stride_axis=0)
                    acc_ref[h] = jnp.where(band == a, rolled, acc_ref[h])
            for i in range(rows // 2):
                pair = acc_ref[2 * i:2 * i + 2].reshape(2 * half, 128)
                energy = jnp.transpose(pair) * scale
                energy = jnp.where(valid, energy, -jnp.inf)
                top = jnp.max(energy, axis=0, keepdims=True)
                p = jnp.exp(energy - top)
                inv = 1.0 / jnp.sum(p, axis=0, keepdims=True)
                fy = jnp.sum(p * row_d, axis=0, keepdims=True) * inv * present
                fx = (jnp.sum(p * col_d, axis=0, keepdims=True) * inv + shift_t) * present
                for k in range(2):
                    out_ref[0, 2 * i + k:2 * i + k + 1, cols] = fy[:, k * half:(k + 1) * half]
                    out_ref[1, 2 * i + k:2 * i + k + 1, cols] = fx[:, k * half:(k + 1) * half]


def correlation(f0, f1rev_ext, shift, presence, sharp):
    rows, width, depth = f0.shape
    frev = f1rev_ext
    return pl.pallas_call(
        _corr_kernel,
        out_shape=jax.ShapeDtypeStruct((2, rows, width), jnp.float32),
        in_specs=[pl.BlockSpec(memory_space=pltpu.SMEM)] * 3
        + [pl.BlockSpec(memory_space=pltpu.VMEM), pl.BlockSpec(memory_space=pl.ANY)],
        out_specs=pl.BlockSpec(memory_space=pltpu.VMEM),
        scratch_shapes=[
            pltpu.VMEM((4, rows + 8, 128, depth), jnp.float32),
            pltpu.VMEM((rows, 64, 128), jnp.float32),
            pltpu.SemaphoreType.DMA((4,)),
        ],
    )(shift, sharp, presence, f0, frev)


def extended(array, sides, width):
    for axis, dim in sides:
        size, length = (lax.axis_size(axis), array.shape[dim])
        up = [(i, (i + 1) % size) for i in range(size - 1)]
        down = [(j, i) for i, j in up]
        last = lax.slice_in_dim(array, length - width, length, axis=dim)
        initial = lax.slice_in_dim(array, 0, width, axis=dim)
        before = lax.ppermute(last, axis, up)
        after = lax.ppermute(initial, axis, down)
        array = jnp.concatenate([before, array, after], axis=dim)
    return array


def butterfly_sum(x, axis, held):
    size = lax.axis_size(axis)
    if size & (size - 1):
        return lax.psum(x, axis), held
    step = 1
    while step < size:
        x = x + lax.ppermute(x, axis, [(i, i ^ step) for i in range(size)])
        if step == 1:
            x, held = lax.optimization_barrier((x, held))
        step *= 2
    return x, held


def _reverse_rows(value):
    tiles = value.shape[0] // 8
    v = value.reshape(tiles, 8, value.shape[1])
    v = jnp.concatenate([v[i:i + 1] for i in reversed(range(tiles))], axis=0)
    sub = lax.broadcasted_iota(jnp.int32, v.shape, 1)
    for step in (1, 2, 4):
        v = jnp.where((sub & step) != 0, pltpu.roll(v, step, 1), pltpu.roll(v, 8 - step, 1))
    return v.reshape(value.shape)


def _conv_kernel(*refs, finish, lead, trail, flips, plan, gather=None, reverse=False):
    if gather:
        *sources, k_ref, o_ref, w_ref, x_ref = refs
        for n, rows in enumerate(gather):
            for r, (which, index) in enumerate(rows):
                x_ref[n, r] = sources[which][index].astype(x_ref.dtype)
    elif plan:
        where_ref, *sources, mean_ref, inv_ref, k_ref, bias_ref, o_ref, w_ref, x_ref = refs
        for r, (which, n, row) in enumerate(plan):
            value = jnp.maximum((sources[which][n, row] - mean_ref[...]) * inv_ref[...], 0.0)
            g = where_ref[2] + r
            keep = (g >= 0) & (g < where_ref[1])
            value = jnp.where(keep, value, 0.0)
            if reverse:
                value = _reverse_rows(value)
            x_ref[0, r] = value.astype(x_ref.dtype)
    elif finish:
        where_ref, x_ref, k_ref, bias_ref, o_ref, w_ref = refs
    else:
        x_ref, k_ref, o_ref, w_ref = refs
    count, rows_out, _, depth = o_ref.shape
    width = x_ref.shape[2]
    for n, flip in enumerate(flips):
        for dr in range(3):
            for dc in range(3):
                w_ref[n, dr * depth:(dr + 1) * depth, dc * depth:(dc + 1) * depth] = k_ref[
                    dr, 2 - dc if flip else dc
                ]
    if lead:
        o_ref[:, :, :lead] = jnp.zeros((count, rows_out, lead, depth), o_ref.dtype)
    if trail:
        o_ref[:, :, lead + width:] = jnp.zeros((count, rows_out, trail, depth), o_ref.dtype)
    chunk = 4 if rows_out % 4 == 0 else (2 if rows_out % 2 == 0 else 1)
    m = chunk * width
    flat = lax.broadcasted_iota(jnp.int32, (m, depth), 0)
    left = flat % width != 0
    right = flat % width != width - 1
    for n in range(count):
        for r0 in range(0, rows_out, chunk):
            lhs = jnp.concatenate(
                [x_ref[n, r0 + dr:r0 + dr + chunk].reshape(m, depth) for dr in range(3)], axis=1
            )
            y = jnp.dot(lhs, w_ref[n], preferred_element_type=jnp.float32)
            out = (
                y[:, depth:2 * depth]
                + jnp.where(left, pltpu.roll(y[:, :depth], 1, 0), 0.0)
                + jnp.where(right, pltpu.roll(y[:, 2 * depth:], m - 1, 0), 0.0)
            )
            if finish:
                out = out + bias_ref[...]
                ms = jnp.mean(out * out, axis=1, keepdims=True)
                out = out * lax.rsqrt(ms + 1e-06)
                row = where_ref[0] + r0 + flat[:, 0:1] // width
                out = jnp.where((row >= 0) & (row < where_ref[1]), out, 0.0)
            o_ref[n, r0:r0 + chunk, lead:lead + width] = out.reshape(chunk, width, depth).astype(o_ref.dtype)


def conv_rows(field, kernel, flips, bias=None, first_row=None, total_rows=None, pad=(0, 0), dtype=jnp.bfloat16):
    count, rows_in, width, depth = field.shape
    vmem = pl.BlockSpec(memory_space=pltpu.VMEM)
    finish = bias is not None
    args = [field, kernel.astype(field.dtype)]
    specs = [vmem, vmem]
    if finish:
        where = jnp.stack([first_row, total_rows]).astype(jnp.int32)
        args = [where] + args + [bias.astype(jnp.float32).reshape(1, -1)]
        specs = [pl.BlockSpec(memory_space=pltpu.SMEM)] + specs + [vmem]
    return pl.pallas_call(
        functools.partial(_conv_kernel, finish=finish, lead=pad[0], trail=pad[1], flips=flips, plan=None),
        out_shape=jax.ShapeDtypeStruct(
            (count, rows_in - 2, pad[0] + width + pad[1], kernel.shape[3]), dtype if finish else jnp.float32
        ),
        in_specs=specs,
        out_specs=vmem,
        scratch_shapes=[pltpu.VMEM((count, 3 * depth, 3 * kernel.shape[3]), field.dtype)],
    )(*args)


def conv_gather(sources, gather, kernel, flips):
    count, rows_in = len(gather), len(gather[0])
    width, depth = sources[0].shape[-2], sources[0].shape[-1]
    vmem = pl.BlockSpec(memory_space=pltpu.VMEM)
    return pl.pallas_call(
        functools.partial(_conv_kernel, finish=False, lead=0, trail=0, flips=flips, plan=None, gather=gather),
        out_shape=jax.ShapeDtypeStruct((count, rows_in - 2, width, kernel.shape[3]), jnp.float32),
        in_specs=[vmem] * (len(sources) + 1),
        out_specs=vmem,
        scratch_shapes=[
            pltpu.VMEM((count, 3 * depth, 3 * kernel.shape[3]), jnp.bfloat16),
            pltpu.VMEM((count, rows_in, width, depth), jnp.bfloat16),
        ],
    )(*sources, kernel.astype(jnp.bfloat16))


def conv_hidden(sources, plan, mean, inv_scale, kernel, flips, bias, first_in, total_rows, pad=(0, 0),
                dtype=jnp.bfloat16, reverse=False):
    rows_in = len(plan)
    width, depth = sources[0].shape[2], sources[0].shape[3]
    vmem = pl.BlockSpec(memory_space=pltpu.VMEM)
    where = jnp.stack([first_in + 1, total_rows, first_in]).astype(jnp.int32)
    args = [where, *sources, mean.reshape(1, -1), inv_scale.reshape(1, -1),
            kernel.astype(jnp.bfloat16), bias.astype(jnp.float32).reshape(1, -1)]
    specs = [pl.BlockSpec(memory_space=pltpu.SMEM)] + [vmem] * (len(sources) + 4)
    return pl.pallas_call(
        functools.partial(
            _conv_kernel, finish=True, lead=pad[0], trail=pad[1], flips=flips, plan=plan, reverse=reverse
        ),
        out_shape=jax.ShapeDtypeStruct((1, rows_in - 2, pad[0] + width + pad[1], kernel.shape[3]), dtype),
        in_specs=specs,
        out_specs=vmem,
        scratch_shapes=[
            pltpu.VMEM((1, 3 * depth, 3 * kernel.shape[3]), jnp.bfloat16),
            pltpu.VMEM((1, rows_in, width, depth), jnp.bfloat16),
        ],
    )(*args)


def finish_features(second_out, latter_kernel_intercept):
    shifted = second_out + latter_kernel_intercept
    return (
        shifted * lax.rsqrt(jnp.mean(shifted * shifted, axis=-1, keepdims=True) + 1e-06)
    ).astype(jnp.bfloat16)


def in_map(rows_from, count, rows_dev):
    total = rows_dev * lax.axis_size("rows")
    first = lax.axis_index("rows") * rows_dev + rows_from
    row = first + lax.broadcasted_iota(jnp.int32, (count, 1, 1), 0)
    return (row >= 0) & (row < total)


def local(
    specimen_pair_inputs,
    initial_kernel_tensor,
    latter_kernel_tensor,
    latter_kernel_intercept,
    patch_horizontal_shift,
    specimen_presence,
    softmax_sharpening,
):
    x0 = specimen_pair_inputs[0]
    x1 = specimen_pair_inputs[1]
    k1 = initial_kernel_tensor
    rows_dev = x0.shape[0]
    width = x0.shape[1]
    size = lax.axis_size("rows")
    cells_all = rows_dev * size * width
    near, far = 2, 6
    up = [(i, i + 1) for i in range(size - 1)]
    down = [(i + 1, i) for i in range(size - 1)]
    before = lax.ppermute(
        jnp.concatenate([x0[rows_dev - near:], x1[rows_dev - far:]], axis=0), "rows", up
    )
    after = lax.ppermute(
        jnp.concatenate([x0[:near], x1[:far]], axis=0), "rows", down
    )

    def row0(r):
        if r < 0:
            return (2, (near + r,))
        if r >= rows_dev:
            return (3, (r - rows_dev,))
        return (0, (0, r))

    def row1(r):
        if r < 0:
            return (2, (near + far + r,))
        if r >= rows_dev:
            return (3, (near + r - rows_dev,))
        return (1, (r,))

    def rows_of(pick, lo, hi):
        return tuple(pick(r) for r in range(lo, hi))

    inputs = (specimen_pair_inputs, x1)
    halos = (specimen_pair_inputs, x1, before, after)
    interior = conv_gather(inputs, (rows_of(row0, 0, rows_dev), rows_of(row1, 0, rows_dev)), k1, (False, False))
    boundary = conv_gather(
        halos,
        (
            rows_of(row0, -1, 2),
            rows_of(row0, rows_dev - 2, rows_dev + 1),
            rows_of(row1, -1, 2),
            rows_of(row1, rows_dev - 2, rows_dev + 1),
        ),
        k1,
        (False, False, False, False),
    )
    stats = jnp.concatenate(
        [
            jnp.sum(interior, axis=(1, 2)) + jnp.sum(boundary.reshape(2, 2, width, -1), axis=(1, 2)),
            jnp.sum(interior * interior, axis=(1, 2))
            + jnp.sum(jnp.square(boundary).reshape(2, 2, width, -1), axis=(1, 2)),
        ],
        axis=0,
    )
    stats, halos = butterfly_sum(stats, "rows", halos)
    average = stats[0:2] / cells_all
    variance = stats[2:4] / cells_all - average * average
    inv_scale = lax.rsqrt(variance + 1e-05)
    edge0 = conv_gather(
        halos, (rows_of(row0, -near, 1), rows_of(row0, rows_dev - 1, rows_dev + near)), k1, (False, False)
    )
    edge1 = conv_gather(
        halos, (rows_of(row1, -far, 1), rows_of(row1, rows_dev - 1, rows_dev + far)), k1, (False, False)
    )
    sources = (edge0, boundary, interior, edge1)
    plan0 = ((0, 0, 0), (1, 0, 0)) + tuple((2, 0, r) for r in range(rows_dev - 2)) + ((1, 1, 0), (0, 1, 0))
    halo = far - 1
    plan1 = (
        tuple((3, 0, r) for r in range(halo))
        + ((1, 2, 0),)
        + tuple((2, 1, r) for r in range(rows_dev - 2))
        + ((1, 3, 0),)
        + tuple((3, 1, r) for r in range(halo))
    )
    total = rows_dev * size
    first = lax.axis_index("rows") * rows_dev
    source = conv_hidden(
        sources, plan0, average[0], inv_scale[0], latter_kernel_tensor, (False,),
        latter_kernel_intercept, first - 1, total,
    )[0]
    target_reversed = conv_hidden(
        sources, plan1, average[1], inv_scale[1], latter_kernel_tensor, (True,),
        latter_kernel_intercept, first - halo, total, pad=(64, 8), dtype=jnp.float32, reverse=True,
    )[0]
    return correlation(
        source,
        target_reversed,
        patch_horizontal_shift,
        specimen_presence,
        softmax_sharpening,
    )


def solution(mesh):
    return jax.shard_map(
        local,
        mesh=mesh,
        in_specs=(
            P(None, ("pairs", "rows"), None, None),
            P(),
            P(),
            P(),
            P(("pairs", "rows"), None),
            P(("pairs", "rows"), None),
            P(("pairs", "rows"), None),
        ),
        out_specs=P(None, ("pairs", "rows"), None),
        check_vma=False,
    )
```

```python
import functools

import jax
import jax.numpy as jnp
from jax import lax
from jax.sharding import PartitionSpec as P
from jax.experimental import pallas as pl
from jax.experimental.pallas import tpu as pltpu

DISP = 81


def _corr_kernel(shift_ref, sharp_ref, pres_ref, f0_ref, frev_hbm, out_ref, win_ref, acc_ref, sems):
    rows = f0_ref.shape[0]
    half = f0_ref.shape[1] // 4
    copies = []
    for t in range(2):
        for q in range(2):
            start = 196 - 128 * t - half * q - shift_ref[0, t]
            cp = pltpu.make_async_copy(frev_hbm.at[:, pl.ds(start, 128), :], win_ref.at[2 * t + q],
                                       sems.at[2 * t + q])
            cp.start()
            copies.append(cp)
    lane = lax.broadcasted_iota(jnp.int32, (half, 128), 1)
    band = lane // 9
    li = lax.broadcasted_iota(jnp.int32, (128, 1), 0)
    valid = li < DISP
    row_d = jnp.where(valid, li // 9 - 4, 0).astype(jnp.float32)
    col_d = jnp.where(valid, 4 - li % 9, 0).astype(jnp.float32)
    for t in range(2):
        shift_t = shift_ref[0, t].astype(jnp.float32)
        scale = sharp_ref[0, t] / 128.0
        present = pres_ref[0, t].astype(jnp.float32)
        for q in range(2):
            cols = slice(128 * t + half * q, 128 * t + half * (q + 1))
            copies[2 * t + q].wait()
            acc_ref[...] = jnp.zeros_like(acc_ref)
            for hp in range(rows + 8):
                lo, hi = max(0, hp - 8), min(rows - 1, hp)
                lhs = f0_ref[lo:hi + 1, cols, :].reshape((hi - lo + 1) * half, 128)
                w = win_ref[2 * t + q, hp].astype(jnp.bfloat16)
                s = lax.dot_general(lhs, w, (((1,), (1,)), ((), ())), preferred_element_type=jnp.float32)
                for h in range(lo, hi + 1):
                    a = hp - h
                    blk = s[(h - lo) * half:(h - lo + 1) * half]
                    rolled = pltpu.roll(blk, 9 + 9 * a, 1, stride=1, stride_axis=0)
                    acc_ref[h] = jnp.where(band == a, rolled, acc_ref[h])
            for i in range(rows // 2):
                pair = acc_ref[2 * i:2 * i + 2].reshape(2 * half, 128)
                energy = jnp.transpose(pair) * scale
                energy = jnp.where(valid, energy, -jnp.inf)
                top = jnp.max(energy, axis=0, keepdims=True)
                p = jnp.exp(energy - top)
                inv = 1.0 / jnp.sum(p, axis=0, keepdims=True)
                fy = jnp.sum(p * row_d, axis=0, keepdims=True) * inv * present
                fx = (jnp.sum(p * col_d, axis=0, keepdims=True) * inv + shift_t) * present
                for k in range(2):
                    out_ref[0, 2 * i + k:2 * i + k + 1, cols] = fy[:, k * half:(k + 1) * half]
                    out_ref[1, 2 * i + k:2 * i + k + 1, cols] = fx[:, k * half:(k + 1) * half]


def correlation(f0, f1rev_ext, shift, presence, sharp):
    rows, width, depth = f0.shape
    frev = f1rev_ext
    return pl.pallas_call(
        _corr_kernel,
        out_shape=jax.ShapeDtypeStruct((2, rows, width), jnp.float32),
        in_specs=[pl.BlockSpec(memory_space=pltpu.SMEM)] * 3
        + [pl.BlockSpec(memory_space=pltpu.VMEM), pl.BlockSpec(memory_space=pl.ANY)],
        out_specs=pl.BlockSpec(memory_space=pltpu.VMEM),
        scratch_shapes=[
            pltpu.VMEM((4, rows + 8, 128, depth), jnp.float32),
            pltpu.VMEM((rows, 64, 128), jnp.float32),
            pltpu.SemaphoreType.DMA((4,)),
        ],
    )(shift, sharp, presence, f0, frev)


def extended(array, sides, width):
    for axis, dim in sides:
        size, length = (lax.axis_size(axis), array.shape[dim])
        up = [(i, (i + 1) % size) for i in range(size - 1)]
        down = [(j, i) for i, j in up]
        last = lax.slice_in_dim(array, length - width, length, axis=dim)
        initial = lax.slice_in_dim(array, 0, width, axis=dim)
        before = lax.ppermute(last, axis, up)
        after = lax.ppermute(initial, axis, down)
        array = jnp.concatenate([before, array, after], axis=dim)
    return array


def butterfly_sum(x, axis, held):
    size = lax.axis_size(axis)
    if size & (size - 1):
        return lax.psum(x, axis), held
    step = 1
    while step < size:
        x = x + lax.ppermute(x, axis, [(i, i ^ step) for i in range(size)])
        if step == 1:
            x, held = lax.optimization_barrier((x, held))
        step *= 2
    return x, held


def _reverse_rows(value):
    tiles = value.shape[0] // 8
    v = value.reshape(tiles, 8, value.shape[1])
    v = jnp.concatenate([v[i:i + 1] for i in reversed(range(tiles))], axis=0)
    sub = lax.broadcasted_iota(jnp.int32, v.shape, 1)
    for step in (1, 2, 4):
        v = jnp.where((sub & step) != 0, pltpu.roll(v, step, 1), pltpu.roll(v, 8 - step, 1))
    return v.reshape(value.shape)


def _conv_kernel(*refs, finish, lead, trail, flips, plan, gather=None, reverse=False):
    if gather:
        *sources, k_ref, o_ref, w_ref, x_ref = refs
        for n, rows in enumerate(gather):
            for r, (which, index) in enumerate(rows):
                x_ref[n, r] = sources[which][index].astype(x_ref.dtype)
    elif plan:
        where_ref, *sources, mean_ref, inv_ref, k_ref, bias_ref, o_ref, w_ref, x_ref = refs
        for r, (which, n, row) in enumerate(plan):
            value = jnp.maximum((sources[which][n, row] - mean_ref[...]) * inv_ref[...], 0.0)
            g = where_ref[2] + r
            keep = (g >= 0) & (g < where_ref[1])
            value = jnp.where(keep, value, 0.0)
            if reverse:
                value = _reverse_rows(value)
            x_ref[0, r] = value.astype(x_ref.dtype)
    elif finish:
        where_ref, x_ref, k_ref, bias_ref, o_ref, w_ref = refs
    else:
        x_ref, k_ref, o_ref, w_ref = refs
    count, rows_out, _, depth = o_ref.shape
    width = x_ref.shape[2]
    for n, flip in enumerate(flips):
        for dr in range(3):
            for dc in range(3):
                w_ref[n, dr * depth:(dr + 1) * depth, dc * depth:(dc + 1) * depth] = k_ref[
                    dr, 2 - dc if flip else dc
                ]
    if lead:
        o_ref[:, :, :lead] = jnp.zeros((count, rows_out, lead, depth), o_ref.dtype)
    if trail:
        o_ref[:, :, lead + width:] = jnp.zeros((count, rows_out, trail, depth), o_ref.dtype)
    chunk = 4 if rows_out % 4 == 0 else (2 if rows_out % 2 == 0 else 1)
    m = chunk * width
    flat = lax.broadcasted_iota(jnp.int32, (m, depth), 0)
    left = flat % width != 0
    right = flat % width != width - 1
    if len(set(flips)) == 1 and chunk < 4 and count > 1:
        cells = [(n, r) for n in range(count) for r in range(rows_out)]
        group = max(1, min(len(cells), 1024 // width))
        while len(cells) % group:
            group -= 1
        m = group * width
        flat = lax.broadcasted_iota(jnp.int32, (m, depth), 0)
        left = flat % width != 0
        right = flat % width != width - 1
        for g0 in range(0, len(cells), group):
            part = cells[g0:g0 + group]
            lhs = jnp.concatenate(
                [jnp.concatenate([x_ref[n, r + dr] for n, r in part], axis=0) for dr in range(3)], axis=1
            )
            y = jnp.dot(lhs, w_ref[0], preferred_element_type=jnp.float32)
            out = (
                y[:, depth:2 * depth]
                + jnp.where(left, pltpu.roll(y[:, :depth], 1, 0), 0.0)
                + jnp.where(right, pltpu.roll(y[:, 2 * depth:], m - 1, 0), 0.0)
            )
            for k, (n, r) in enumerate(part):
                o_ref[n, r] = out[k * width:(k + 1) * width].astype(o_ref.dtype)
        return
    for n in range(count):
        for r0 in range(0, rows_out, chunk):
            lhs = jnp.concatenate(
                [x_ref[n, r0 + dr:r0 + dr + chunk].reshape(m, depth) for dr in range(3)], axis=1
            )
            y = jnp.dot(lhs, w_ref[n], preferred_element_type=jnp.float32)
            out = (
                y[:, depth:2 * depth]
                + jnp.where(left, pltpu.roll(y[:, :depth], 1, 0), 0.0)
                + jnp.where(right, pltpu.roll(y[:, 2 * depth:], m - 1, 0), 0.0)
            )
            if finish:
                out = out + bias_ref[...]
                ms = jnp.mean(out * out, axis=1, keepdims=True)
                out = out * lax.rsqrt(ms + 1e-06)
                row = where_ref[0] + r0 + flat[:, 0:1] // width
                out = jnp.where((row >= 0) & (row < where_ref[1]), out, 0.0)
            o_ref[n, r0:r0 + chunk, lead:lead + width] = out.reshape(chunk, width, depth).astype(o_ref.dtype)


def conv_rows(field, kernel, flips, bias=None, first_row=None, total_rows=None, pad=(0, 0), dtype=jnp.bfloat16):
    count, rows_in, width, depth = field.shape
    vmem = pl.BlockSpec(memory_space=pltpu.VMEM)
    finish = bias is not None
    args = [field, kernel.astype(field.dtype)]
    specs = [vmem, vmem]
    if finish:
        where = jnp.stack([first_row, total_rows]).astype(jnp.int32)
        args = [where] + args + [bias.astype(jnp.float32).reshape(1, -1)]
        specs = [pl.BlockSpec(memory_space=pltpu.SMEM)] + specs + [vmem]
    return pl.pallas_call(
        functools.partial(_conv_kernel, finish=finish, lead=pad[0], trail=pad[1], flips=flips, plan=None),
        out_shape=jax.ShapeDtypeStruct(
            (count, rows_in - 2, pad[0] + width + pad[1], kernel.shape[3]), dtype if finish else jnp.float32
        ),
        in_specs=specs,
        out_specs=vmem,
        scratch_shapes=[pltpu.VMEM((count, 3 * depth, 3 * kernel.shape[3]), field.dtype)],
    )(*args)


def conv_gather(sources, gather, kernel, flips):
    count, rows_in = len(gather), len(gather[0])
    width, depth = sources[0].shape[-2], sources[0].shape[-1]
    vmem = pl.BlockSpec(memory_space=pltpu.VMEM)
    return pl.pallas_call(
        functools.partial(_conv_kernel, finish=False, lead=0, trail=0, flips=flips, plan=None, gather=gather),
        out_shape=jax.ShapeDtypeStruct((count, rows_in - 2, width, kernel.shape[3]), jnp.float32),
        in_specs=[vmem] * (len(sources) + 1),
        out_specs=vmem,
        scratch_shapes=[
            pltpu.VMEM((count, 3 * depth, 3 * kernel.shape[3]), jnp.bfloat16),
            pltpu.VMEM((count, rows_in, width, depth), jnp.bfloat16),
        ],
    )(*sources, kernel.astype(jnp.bfloat16))


def conv_hidden(sources, plan, mean, inv_scale, kernel, flips, bias, first_in, total_rows, pad=(0, 0),
                dtype=jnp.bfloat16, reverse=False):
    rows_in = len(plan)
    width, depth = sources[0].shape[2], sources[0].shape[3]
    vmem = pl.BlockSpec(memory_space=pltpu.VMEM)
    where = jnp.stack([first_in + 1, total_rows, first_in]).astype(jnp.int32)
    args = [where, *sources, mean.reshape(1, -1), inv_scale.reshape(1, -1),
            kernel.astype(jnp.bfloat16), bias.astype(jnp.float32).reshape(1, -1)]
    specs = [pl.BlockSpec(memory_space=pltpu.SMEM)] + [vmem] * (len(sources) + 4)
    return pl.pallas_call(
        functools.partial(
            _conv_kernel, finish=True, lead=pad[0], trail=pad[1], flips=flips, plan=plan, reverse=reverse
        ),
        out_shape=jax.ShapeDtypeStruct((1, rows_in - 2, pad[0] + width + pad[1], kernel.shape[3]), dtype),
        in_specs=specs,
        out_specs=vmem,
        scratch_shapes=[
            pltpu.VMEM((1, 3 * depth, 3 * kernel.shape[3]), jnp.bfloat16),
            pltpu.VMEM((1, rows_in, width, depth), jnp.bfloat16),
        ],
    )(*args)


def finish_features(second_out, latter_kernel_intercept):
    shifted = second_out + latter_kernel_intercept
    return (
        shifted * lax.rsqrt(jnp.mean(shifted * shifted, axis=-1, keepdims=True) + 1e-06)
    ).astype(jnp.bfloat16)


def in_map(rows_from, count, rows_dev):
    total = rows_dev * lax.axis_size("rows")
    first = lax.axis_index("rows") * rows_dev + rows_from
    row = first + lax.broadcasted_iota(jnp.int32, (count, 1, 1), 0)
    return (row >= 0) & (row < total)


def local(
    specimen_pair_inputs,
    initial_kernel_tensor,
    latter_kernel_tensor,
    latter_kernel_intercept,
    patch_horizontal_shift,
    specimen_presence,
    softmax_sharpening,
):
    x0 = specimen_pair_inputs[0]
    x1 = specimen_pair_inputs[1]
    k1 = initial_kernel_tensor
    rows_dev = x0.shape[0]
    width = x0.shape[1]
    size = lax.axis_size("rows")
    cells_all = rows_dev * size * width
    near, far = 2, 6
    up = [(i, i + 1) for i in range(size - 1)]
    down = [(i + 1, i) for i in range(size - 1)]
    before = lax.ppermute(
        jnp.concatenate([x0[rows_dev - near:], x1[rows_dev - far:]], axis=0), "rows", up
    )
    after = lax.ppermute(
        jnp.concatenate([x0[:near], x1[:far]], axis=0), "rows", down
    )

    def row0(r):
        if r < 0:
            return (2, (near + r,))
        if r >= rows_dev:
            return (3, (r - rows_dev,))
        return (0, (0, r))

    def row1(r):
        if r < 0:
            return (2, (near + far + r,))
        if r >= rows_dev:
            return (3, (near + r - rows_dev,))
        return (1, (r,))

    def rows_of(pick, lo, hi):
        return tuple(pick(r) for r in range(lo, hi))

    inputs = (specimen_pair_inputs, x1)
    halos = (specimen_pair_inputs, x1, before, after)
    interior = conv_gather(inputs, (rows_of(row0, 0, rows_dev), rows_of(row1, 0, rows_dev)), k1, (False, False))
    boundary = conv_gather(
        halos,
        (
            rows_of(row0, -1, 2),
            rows_of(row0, rows_dev - 2, rows_dev + 1),
            rows_of(row1, -1, 2),
            rows_of(row1, rows_dev - 2, rows_dev + 1),
        ),
        k1,
        (False, False, False, False),
    )
    stats = jnp.concatenate(
        [
            jnp.sum(interior, axis=(1, 2)) + jnp.sum(boundary.reshape(2, 2, width, -1), axis=(1, 2)),
            jnp.sum(interior * interior, axis=(1, 2))
            + jnp.sum(jnp.square(boundary).reshape(2, 2, width, -1), axis=(1, 2)),
        ],
        axis=0,
    )
    stats, halos = butterfly_sum(stats, "rows", halos)
    average = stats[0:2] / cells_all
    variance = stats[2:4] / cells_all - average * average
    inv_scale = lax.rsqrt(variance + 1e-05)
    edge0 = conv_gather(
        halos, (rows_of(row0, -near, 1), rows_of(row0, rows_dev - 1, rows_dev + near)), k1, (False, False)
    )
    edge1 = conv_gather(
        halos, (rows_of(row1, -far, 1), rows_of(row1, rows_dev - 1, rows_dev + far)), k1, (False, False)
    )
    sources = (edge0, boundary, interior, edge1)
    plan0 = ((0, 0, 0), (1, 0, 0)) + tuple((2, 0, r) for r in range(rows_dev - 2)) + ((1, 1, 0), (0, 1, 0))
    halo = far - 1
    plan1 = (
        tuple((3, 0, r) for r in range(halo))
        + ((1, 2, 0),)
        + tuple((2, 1, r) for r in range(rows_dev - 2))
        + ((1, 3, 0),)
        + tuple((3, 1, r) for r in range(halo))
    )
    total = rows_dev * size
    first = lax.axis_index("rows") * rows_dev
    source = conv_hidden(
        sources, plan0, average[0], inv_scale[0], latter_kernel_tensor, (False,),
        latter_kernel_intercept, first - 1, total,
    )[0]
    target_reversed = conv_hidden(
        sources, plan1, average[1], inv_scale[1], latter_kernel_tensor, (True,),
        latter_kernel_intercept, first - halo, total, pad=(64, 8), dtype=jnp.float32, reverse=True,
    )[0]
    return correlation(
        source,
        target_reversed,
        patch_horizontal_shift,
        specimen_presence,
        softmax_sharpening,
    )


def solution(mesh):
    return jax.shard_map(
        local,
        mesh=mesh,
        in_specs=(
            P(None, ("pairs", "rows"), None, None),
            P(),
            P(),
            P(),
            P(("pairs", "rows"), None),
            P(("pairs", "rows"), None),
            P(("pairs", "rows"), None),
        ),
        out_specs=P(None, ("pairs", "rows"), None),
        check_vma=False,
    )
```

```python
import functools

import jax
import jax.numpy as jnp
from jax import lax
from jax.sharding import PartitionSpec as P
from jax.experimental import pallas as pl
from jax.experimental.pallas import tpu as pltpu

DISP = 81


def _corr_kernel(shift_ref, sharp_ref, pres_ref, f0_ref, frev_hbm, out_ref, win_ref, acc_ref, sems):
    rows = f0_ref.shape[0]
    half = f0_ref.shape[1] // 4
    copies = []
    for t in range(2):
        for q in range(2):
            start = 196 - 128 * t - half * q - shift_ref[0, t]
            cp = pltpu.make_async_copy(frev_hbm.at[:, pl.ds(start, 128), :], win_ref.at[2 * t + q],
                                       sems.at[2 * t + q])
            cp.start()
            copies.append(cp)
    lane = lax.broadcasted_iota(jnp.int32, (half, 128), 1)
    band = lane // 9
    li = lax.broadcasted_iota(jnp.int32, (128, 1), 0)
    valid = li < DISP
    row_d = jnp.where(valid, li // 9 - 4, 0).astype(jnp.float32)
    col_d = jnp.where(valid, 4 - li % 9, 0).astype(jnp.float32)
    for t in range(2):
        shift_t = shift_ref[0, t].astype(jnp.float32)
        scale = sharp_ref[0, t] / 128.0
        present = pres_ref[0, t].astype(jnp.float32)
        for q in range(2):
            cols = slice(128 * t + half * q, 128 * t + half * (q + 1))
            copies[2 * t + q].wait()
            acc_ref[...] = jnp.zeros_like(acc_ref)
            for hp in range(rows + 8):
                lo, hi = max(0, hp - 8), min(rows - 1, hp)
                lhs = f0_ref[lo:hi + 1, cols, :].reshape((hi - lo + 1) * half, 128)
                w = win_ref[2 * t + q, hp].astype(jnp.bfloat16)
                s = lax.dot_general(lhs, w, (((1,), (1,)), ((), ())), preferred_element_type=jnp.float32)
                for h in range(lo, hi + 1):
                    a = hp - h
                    blk = s[(h - lo) * half:(h - lo + 1) * half]
                    rolled = pltpu.roll(blk, 9 + 9 * a, 1, stride=1, stride_axis=0)
                    acc_ref[h] = jnp.where(band == a, rolled, acc_ref[h])
            for i in range(rows // 2):
                pair = acc_ref[2 * i:2 * i + 2].reshape(2 * half, 128)
                energy = jnp.transpose(pair) * scale
                energy = jnp.where(valid, energy, -jnp.inf)
                top = jnp.max(energy, axis=0, keepdims=True)
                p = jnp.exp(energy - top)
                inv = 1.0 / jnp.sum(p, axis=0, keepdims=True)
                fy = jnp.sum(p * row_d, axis=0, keepdims=True) * inv * present
                fx = (jnp.sum(p * col_d, axis=0, keepdims=True) * inv + shift_t) * present
                for k in range(2):
                    out_ref[0, 2 * i + k:2 * i + k + 1, cols] = fy[:, k * half:(k + 1) * half]
                    out_ref[1, 2 * i + k:2 * i + k + 1, cols] = fx[:, k * half:(k + 1) * half]


def correlation(f0, f1rev_ext, shift, presence, sharp):
    rows, width, depth = f0.shape
    frev = f1rev_ext
    return pl.pallas_call(
        _corr_kernel,
        out_shape=jax.ShapeDtypeStruct((2, rows, width), jnp.float32),
        in_specs=[pl.BlockSpec(memory_space=pltpu.SMEM)] * 3
        + [pl.BlockSpec(memory_space=pltpu.VMEM), pl.BlockSpec(memory_space=pl.ANY)],
        out_specs=pl.BlockSpec(memory_space=pltpu.VMEM),
        scratch_shapes=[
            pltpu.VMEM((4, rows + 8, 128, depth), jnp.float32),
            pltpu.VMEM((rows, 64, 128), jnp.float32),
            pltpu.SemaphoreType.DMA((4,)),
        ],
    )(shift, sharp, presence, f0, frev)


def extended(array, sides, width):
    for axis, dim in sides:
        size, length = (lax.axis_size(axis), array.shape[dim])
        up = [(i, (i + 1) % size) for i in range(size - 1)]
        down = [(j, i) for i, j in up]
        last = lax.slice_in_dim(array, length - width, length, axis=dim)
        initial = lax.slice_in_dim(array, 0, width, axis=dim)
        before = lax.ppermute(last, axis, up)
        after = lax.ppermute(initial, axis, down)
        array = jnp.concatenate([before, array, after], axis=dim)
    return array


def butterfly_sum(x, axis, held):
    size = lax.axis_size(axis)
    if size & (size - 1):
        return lax.psum(x, axis), held
    step = 1
    while step < size:
        x = x + lax.ppermute(x, axis, [(i, i ^ step) for i in range(size)])
        if step == 1:
            x, held = lax.optimization_barrier((x, held))
        step *= 2
    return x, held


def _reverse_rows(value):
    tiles = value.shape[0] // 8
    v = value.reshape(tiles, 8, value.shape[1])
    v = jnp.concatenate([v[i:i + 1] for i in reversed(range(tiles))], axis=0)
    sub = lax.broadcasted_iota(jnp.int32, v.shape, 1)
    for step in (1, 2, 4):
        v = jnp.where((sub & step) != 0, pltpu.roll(v, step, 1), pltpu.roll(v, 8 - step, 1))
    return v.reshape(value.shape)


def _conv_kernel(*refs, finish, lead, trail, flips, plan, gather=None, reverse=False):
    if gather:
        *sources, k_ref, o_ref, w_ref, x_ref, sems = refs
        copies = []
        for n, rows in enumerate(gather):
            for r, (which, index) in enumerate(rows):
                copy = pltpu.make_async_copy(sources[which].at[index], x_ref.at[n, r], sems.at[len(copies)])
                copy.start()
                copies.append(copy)
        for copy in copies:
            copy.wait()
    elif plan:
        where_ref, *sources, mean_ref, inv_ref, k_ref, bias_ref, o_ref, w_ref, x_ref, stage_ref, sems = refs
        copies = []
        for r, (which, n, row) in enumerate(plan):
            copy = pltpu.make_async_copy(sources[which].at[n, row], stage_ref.at[r], sems.at[r])
            copy.start()
            copies.append(copy)
        for copy in copies:
            copy.wait()
        for r in range(len(plan)):
            value = jnp.maximum((stage_ref[r] - mean_ref[...]) * inv_ref[...], 0.0)
            g = where_ref[2] + r
            keep = (g >= 0) & (g < where_ref[1])
            value = jnp.where(keep, value, 0.0)
            if reverse:
                value = _reverse_rows(value)
            x_ref[0, r] = value.astype(x_ref.dtype)
    elif finish:
        where_ref, x_ref, k_ref, bias_ref, o_ref, w_ref = refs
    else:
        x_ref, k_ref, o_ref, w_ref = refs
    count, rows_out, _, depth = o_ref.shape
    width = x_ref.shape[2]
    for n, flip in enumerate(flips):
        for dr in range(3):
            for dc in range(3):
                w_ref[n, dr * depth:(dr + 1) * depth, dc * depth:(dc + 1) * depth] = k_ref[
                    dr, 2 - dc if flip else dc
                ]
    if lead:
        o_ref[:, :, :lead] = jnp.zeros((count, rows_out, lead, depth), o_ref.dtype)
    if trail:
        o_ref[:, :, lead + width:] = jnp.zeros((count, rows_out, trail, depth), o_ref.dtype)
    chunk = 4 if rows_out % 4 == 0 else (2 if rows_out % 2 == 0 else 1)
    m = chunk * width
    flat = lax.broadcasted_iota(jnp.int32, (m, depth), 0)
    left = flat % width != 0
    right = flat % width != width - 1
    if len(set(flips)) == 1 and chunk < 4 and count > 1:
        cells = [(n, r) for n in range(count) for r in range(rows_out)]
        group = max(1, min(len(cells), 1024 // width))
        while len(cells) % group:
            group -= 1
        m = group * width
        flat = lax.broadcasted_iota(jnp.int32, (m, depth), 0)
        left = flat % width != 0
        right = flat % width != width - 1
        for g0 in range(0, len(cells), group):
            part = cells[g0:g0 + group]
            lhs = jnp.concatenate(
                [jnp.concatenate([x_ref[n, r + dr] for n, r in part], axis=0) for dr in range(3)], axis=1
            )
            y = jnp.dot(lhs, w_ref[0], preferred_element_type=jnp.float32)
            out = (
                y[:, depth:2 * depth]
                + jnp.where(left, pltpu.roll(y[:, :depth], 1, 0), 0.0)
                + jnp.where(right, pltpu.roll(y[:, 2 * depth:], m - 1, 0), 0.0)
            )
            for k, (n, r) in enumerate(part):
                o_ref[n, r] = out[k * width:(k + 1) * width].astype(o_ref.dtype)
        return
    for n in range(count):
        for r0 in range(0, rows_out, chunk):
            lhs = jnp.concatenate(
                [x_ref[n, r0 + dr:r0 + dr + chunk].reshape(m, depth) for dr in range(3)], axis=1
            )
            y = jnp.dot(lhs, w_ref[n], preferred_element_type=jnp.float32)
            out = (
                y[:, depth:2 * depth]
                + jnp.where(left, pltpu.roll(y[:, :depth], 1, 0), 0.0)
                + jnp.where(right, pltpu.roll(y[:, 2 * depth:], m - 1, 0), 0.0)
            )
            if finish:
                out = out + bias_ref[...]
                ms = jnp.mean(out * out, axis=1, keepdims=True)
                out = out * lax.rsqrt(ms + 1e-06)
                row = where_ref[0] + r0 + flat[:, 0:1] // width
                out = jnp.where((row >= 0) & (row < where_ref[1]), out, 0.0)
            o_ref[n, r0:r0 + chunk, lead:lead + width] = out.reshape(chunk, width, depth).astype(o_ref.dtype)


def conv_rows(field, kernel, flips, bias=None, first_row=None, total_rows=None, pad=(0, 0), dtype=jnp.bfloat16):
    count, rows_in, width, depth = field.shape
    vmem = pl.BlockSpec(memory_space=pltpu.VMEM)
    finish = bias is not None
    args = [field, kernel.astype(field.dtype)]
    specs = [vmem, vmem]
    if finish:
        where = jnp.stack([first_row, total_rows]).astype(jnp.int32)
        args = [where] + args + [bias.astype(jnp.float32).reshape(1, -1)]
        specs = [pl.BlockSpec(memory_space=pltpu.SMEM)] + specs + [vmem]
    return pl.pallas_call(
        functools.partial(_conv_kernel, finish=finish, lead=pad[0], trail=pad[1], flips=flips, plan=None),
        out_shape=jax.ShapeDtypeStruct(
            (count, rows_in - 2, pad[0] + width + pad[1], kernel.shape[3]), dtype if finish else jnp.float32
        ),
        in_specs=specs,
        out_specs=vmem,
        scratch_shapes=[pltpu.VMEM((count, 3 * depth, 3 * kernel.shape[3]), field.dtype)],
    )(*args)


def conv_gather(sources, gather, kernel, flips):
    count, rows_in = len(gather), len(gather[0])
    width, depth = sources[0].shape[-2], sources[0].shape[-1]
    vmem = pl.BlockSpec(memory_space=pltpu.VMEM)
    return pl.pallas_call(
        functools.partial(_conv_kernel, finish=False, lead=0, trail=0, flips=flips, plan=None, gather=gather),
        out_shape=jax.ShapeDtypeStruct((count, rows_in - 2, width, kernel.shape[3]), jnp.float32),
        in_specs=[pl.BlockSpec(memory_space=pl.ANY)] * len(sources) + [vmem],
        out_specs=vmem,
        scratch_shapes=[
            pltpu.VMEM((count, 3 * depth, 3 * kernel.shape[3]), jnp.bfloat16),
            pltpu.VMEM((count, rows_in, width, depth), jnp.bfloat16),
            pltpu.SemaphoreType.DMA((count * rows_in,)),
        ],
    )(*sources, kernel.astype(jnp.bfloat16))


def conv_hidden(sources, plan, mean, inv_scale, kernel, flips, bias, first_in, total_rows, pad=(0, 0),
                dtype=jnp.bfloat16, reverse=False):
    rows_in = len(plan)
    width, depth = sources[0].shape[2], sources[0].shape[3]
    vmem = pl.BlockSpec(memory_space=pltpu.VMEM)
    where = jnp.stack([first_in + 1, total_rows, first_in]).astype(jnp.int32)
    args = [where, *sources, mean.reshape(1, -1), inv_scale.reshape(1, -1),
            kernel.astype(jnp.bfloat16), bias.astype(jnp.float32).reshape(1, -1)]
    specs = (
        [pl.BlockSpec(memory_space=pltpu.SMEM)]
        + [pl.BlockSpec(memory_space=pl.ANY)] * len(sources)
        + [vmem] * 4
    )
    return pl.pallas_call(
        functools.partial(
            _conv_kernel, finish=True, lead=pad[0], trail=pad[1], flips=flips, plan=plan, reverse=reverse
        ),
        out_shape=jax.ShapeDtypeStruct((1, rows_in - 2, pad[0] + width + pad[1], kernel.shape[3]), dtype),
        in_specs=specs,
        out_specs=vmem,
        scratch_shapes=[
            pltpu.VMEM((1, 3 * depth, 3 * kernel.shape[3]), jnp.bfloat16),
            pltpu.VMEM((1, rows_in, width, depth), jnp.bfloat16),
            pltpu.VMEM((rows_in, width, depth), jnp.float32),
            pltpu.SemaphoreType.DMA((rows_in,)),
        ],
    )(*args)


def finish_features(second_out, latter_kernel_intercept):
    shifted = second_out + latter_kernel_intercept
    return (
        shifted * lax.rsqrt(jnp.mean(shifted * shifted, axis=-1, keepdims=True) + 1e-06)
    ).astype(jnp.bfloat16)


def in_map(rows_from, count, rows_dev):
    total = rows_dev * lax.axis_size("rows")
    first = lax.axis_index("rows") * rows_dev + rows_from
    row = first + lax.broadcasted_iota(jnp.int32, (count, 1, 1), 0)
    return (row >= 0) & (row < total)


def local(
    specimen_pair_inputs,
    initial_kernel_tensor,
    latter_kernel_tensor,
    latter_kernel_intercept,
    patch_horizontal_shift,
    specimen_presence,
    softmax_sharpening,
):
    x0 = specimen_pair_inputs[0]
    x1 = specimen_pair_inputs[1]
    k1 = initial_kernel_tensor
    rows_dev = x0.shape[0]
    width = x0.shape[1]
    size = lax.axis_size("rows")
    cells_all = rows_dev * size * width
    near, far = 2, 6
    up = [(i, i + 1) for i in range(size - 1)]
    down = [(i + 1, i) for i in range(size - 1)]
    before = lax.ppermute(
        jnp.concatenate([x0[rows_dev - near:], x1[rows_dev - far:]], axis=0), "rows", up
    )
    after = lax.ppermute(
        jnp.concatenate([x0[:near], x1[:far]], axis=0), "rows", down
    )

    def row0(r):
        if r < 0:
            return (2, (near + r,))
        if r >= rows_dev:
            return (3, (r - rows_dev,))
        return (0, (0, r))

    def row1(r):
        if r < 0:
            return (2, (near + far + r,))
        if r >= rows_dev:
            return (3, (near + r - rows_dev,))
        return (1, (r,))

    def rows_of(pick, lo, hi):
        return tuple(pick(r) for r in range(lo, hi))

    inputs = (specimen_pair_inputs, x1)
    halos = (specimen_pair_inputs, x1, before, after)
    interior = conv_gather(inputs, (rows_of(row0, 0, rows_dev), rows_of(row1, 0, rows_dev)), k1, (False, False))
    boundary = conv_gather(
        halos,
        (
            rows_of(row0, -1, 2),
            rows_of(row0, rows_dev - 2, rows_dev + 1),
            rows_of(row1, -1, 2),
            rows_of(row1, rows_dev - 2, rows_dev + 1),
        ),
        k1,
        (False, False, False, False),
    )
    stats = jnp.concatenate(
        [
            jnp.sum(interior, axis=(1, 2)) + jnp.sum(boundary.reshape(2, 2, width, -1), axis=(1, 2)),
            jnp.sum(interior * interior, axis=(1, 2))
            + jnp.sum(jnp.square(boundary).reshape(2, 2, width, -1), axis=(1, 2)),
        ],
        axis=0,
    )
    stats, halos = butterfly_sum(stats, "rows", halos)
    average = stats[0:2] / cells_all
    variance = stats[2:4] / cells_all - average * average
    inv_scale = lax.rsqrt(variance + 1e-05)
    edge0 = conv_gather(
        halos, (rows_of(row0, -near, 1), rows_of(row0, rows_dev - 1, rows_dev + near)), k1, (False, False)
    )
    edge1 = conv_gather(
        halos, (rows_of(row1, -far, 1), rows_of(row1, rows_dev - 1, rows_dev + far)), k1, (False, False)
    )
    sources = (edge0, boundary, interior, edge1)
    plan0 = ((0, 0, 0), (1, 0, 0)) + tuple((2, 0, r) for r in range(rows_dev - 2)) + ((1, 1, 0), (0, 1, 0))
    halo = far - 1
    plan1 = (
        tuple((3, 0, r) for r in range(halo))
        + ((1, 2, 0),)
        + tuple((2, 1, r) for r in range(rows_dev - 2))
        + ((1, 3, 0),)
        + tuple((3, 1, r) for r in range(halo))
    )
    total = rows_dev * size
    first = lax.axis_index("rows") * rows_dev
    source = conv_hidden(
        sources, plan0, average[0], inv_scale[0], latter_kernel_tensor, (False,),
        latter_kernel_intercept, first - 1, total,
    )[0]
    target_reversed = conv_hidden(
        sources, plan1, average[1], inv_scale[1], latter_kernel_tensor, (True,),
        latter_kernel_intercept, first - halo, total, pad=(64, 8), dtype=jnp.float32, reverse=True,
    )[0]
    return correlation(
        source,
        target_reversed,
        patch_horizontal_shift,
        specimen_presence,
        softmax_sharpening,
    )


def solution(mesh):
    return jax.shard_map(
        local,
        mesh=mesh,
        in_specs=(
            P(None, ("pairs", "rows"), None, None),
            P(),
            P(),
            P(),
            P(("pairs", "rows"), None),
            P(("pairs", "rows"), None),
            P(("pairs", "rows"), None),
        ),
        out_specs=P(None, ("pairs", "rows"), None),
        check_vma=False,
    )
```

```python
import functools

import jax
import jax.numpy as jnp
from jax import lax
from jax.sharding import PartitionSpec as P
from jax.experimental import pallas as pl
from jax.experimental.pallas import tpu as pltpu

DISP = 81


def _corr_kernel(shift_ref, sharp_ref, pres_ref, f0_ref, frev_hbm, out_ref, win_ref, acc_ref, sems):
    rows = f0_ref.shape[0]
    half = f0_ref.shape[1] // 4
    copies = []
    for t in range(2):
        for q in range(2):
            start = 196 - 128 * t - half * q - shift_ref[0, t]
            cp = pltpu.make_async_copy(frev_hbm.at[:, pl.ds(start, 128), :], win_ref.at[2 * t + q],
                                       sems.at[2 * t + q])
            cp.start()
            copies.append(cp)
    lane = lax.broadcasted_iota(jnp.int32, (half, 128), 1)
    band = lane // 9
    li = lax.broadcasted_iota(jnp.int32, (128, 1), 0)
    valid = li < DISP
    row_d = jnp.where(valid, li // 9 - 4, 0).astype(jnp.float32)
    col_d = jnp.where(valid, 4 - li % 9, 0).astype(jnp.float32)
    for t in range(2):
        shift_t = shift_ref[0, t].astype(jnp.float32)
        scale = sharp_ref[0, t] / 128.0
        present = pres_ref[0, t].astype(jnp.float32)
        for q in range(2):
            cols = slice(128 * t + half * q, 128 * t + half * (q + 1))
            copies[2 * t + q].wait()
            acc_ref[...] = jnp.zeros_like(acc_ref)
            for hp in range(rows + 8):
                lo, hi = max(0, hp - 8), min(rows - 1, hp)
                lhs = f0_ref[lo:hi + 1, cols, :].reshape((hi - lo + 1) * half, 128)
                w = win_ref[2 * t + q, hp].astype(jnp.bfloat16)
                s = lax.dot_general(lhs, w, (((1,), (1,)), ((), ())), preferred_element_type=jnp.float32)
                for h in range(lo, hi + 1):
                    a = hp - h
                    blk = s[(h - lo) * half:(h - lo + 1) * half]
                    rolled = pltpu.roll(blk, 9 + 9 * a, 1, stride=1, stride_axis=0)
                    acc_ref[h] = jnp.where(band == a, rolled, acc_ref[h])
            for i in range(rows // 2):
                pair = acc_ref[2 * i:2 * i + 2].reshape(2 * half, 128)
                energy = jnp.transpose(pair) * scale
                energy = jnp.where(valid, energy, -jnp.inf)
                top = jnp.max(energy, axis=0, keepdims=True)
                p = jnp.exp(energy - top)
                inv = 1.0 / jnp.sum(p, axis=0, keepdims=True)
                fy = jnp.sum(p * row_d, axis=0, keepdims=True) * inv * present
                fx = (jnp.sum(p * col_d, axis=0, keepdims=True) * inv + shift_t) * present
                for k in range(2):
                    out_ref[0, 2 * i + k:2 * i + k + 1, cols] = fy[:, k * half:(k + 1) * half]
                    out_ref[1, 2 * i + k:2 * i + k + 1, cols] = fx[:, k * half:(k + 1) * half]


def correlation(f0, f1rev_ext, shift, presence, sharp):
    rows, width, depth = f0.shape
    frev = f1rev_ext
    return pl.pallas_call(
        _corr_kernel,
        out_shape=jax.ShapeDtypeStruct((2, rows, width), jnp.float32),
        in_specs=[pl.BlockSpec(memory_space=pltpu.SMEM)] * 3
        + [pl.BlockSpec(memory_space=pltpu.VMEM), pl.BlockSpec(memory_space=pl.ANY)],
        out_specs=pl.BlockSpec(memory_space=pltpu.VMEM),
        scratch_shapes=[
            pltpu.VMEM((4, rows + 8, 128, depth), jnp.float32),
            pltpu.VMEM((rows, 64, 128), jnp.float32),
            pltpu.SemaphoreType.DMA((4,)),
        ],
    )(shift, sharp, presence, f0, frev)


def extended(array, sides, width):
    for axis, dim in sides:
        size, length = (lax.axis_size(axis), array.shape[dim])
        up = [(i, (i + 1) % size) for i in range(size - 1)]
        down = [(j, i) for i, j in up]
        last = lax.slice_in_dim(array, length - width, length, axis=dim)
        initial = lax.slice_in_dim(array, 0, width, axis=dim)
        before = lax.ppermute(last, axis, up)
        after = lax.ppermute(initial, axis, down)
        array = jnp.concatenate([before, array, after], axis=dim)
    return array


def butterfly_sum(x, axis, held):
    size = lax.axis_size(axis)
    if size & (size - 1):
        return lax.psum(x, axis), held
    step = 1
    while step < size:
        x = x + lax.ppermute(x, axis, [(i, i ^ step) for i in range(size)])
        if step == 1:
            x, held = lax.optimization_barrier((x, held))
        step *= 2
    return x, held


def _reverse_rows(value):
    tiles = value.shape[0] // 8
    v = value.reshape(tiles, 8, value.shape[1])
    v = jnp.concatenate([v[i:i + 1] for i in reversed(range(tiles))], axis=0)
    sub = lax.broadcasted_iota(jnp.int32, v.shape, 1)
    for step in (1, 2, 4):
        v = jnp.where((sub & step) != 0, pltpu.roll(v, step, 1), pltpu.roll(v, 8 - step, 1))
    return v.reshape(value.shape)


def _conv_kernel(*refs, finish, lead, trail, flips, plan, gather=None, reverse=False):
    sums_ref = None
    if gather:
        *sources, k_ref, o_ref, sums_ref, w_ref, x_ref = refs
        for n, rows in enumerate(gather):
            for r, (which, index) in enumerate(rows):
                x_ref[n, r] = sources[which][index].astype(x_ref.dtype)
    elif plan:
        where_ref, *sources, mean_ref, inv_ref, k_ref, bias_ref, o_ref, w_ref, x_ref = refs
        for r, (which, n, row) in enumerate(plan):
            value = jnp.maximum((sources[which][n, row] - mean_ref[...]) * inv_ref[...], 0.0)
            g = where_ref[2] + r
            keep = (g >= 0) & (g < where_ref[1])
            value = jnp.where(keep, value, 0.0)
            if reverse:
                value = _reverse_rows(value)
            x_ref[0, r] = value.astype(x_ref.dtype)
    elif finish:
        where_ref, x_ref, k_ref, bias_ref, o_ref, w_ref = refs
    else:
        x_ref, k_ref, o_ref, w_ref = refs
    count, rows_out, _, depth = o_ref.shape
    width = x_ref.shape[2]
    for n, flip in enumerate(flips):
        for dr in range(3):
            for dc in range(3):
                w_ref[n, dr * depth:(dr + 1) * depth, dc * depth:(dc + 1) * depth] = k_ref[
                    dr, 2 - dc if flip else dc
                ]
    if lead:
        o_ref[:, :, :lead] = jnp.zeros((count, rows_out, lead, depth), o_ref.dtype)
    if trail:
        o_ref[:, :, lead + width:] = jnp.zeros((count, rows_out, trail, depth), o_ref.dtype)
    chunk = 4 if rows_out % 4 == 0 else (2 if rows_out % 2 == 0 else 1)
    m = chunk * width
    flat = lax.broadcasted_iota(jnp.int32, (m, depth), 0)
    left = flat % width != 0
    right = flat % width != width - 1
    if len(set(flips)) == 1 and chunk < 4 and count > 1:
        cells = [(n, r) for n in range(count) for r in range(rows_out)]
        group = max(1, min(len(cells), 1024 // width))
        while len(cells) % group:
            group -= 1
        m = group * width
        flat = lax.broadcasted_iota(jnp.int32, (m, depth), 0)
        left = flat % width != 0
        right = flat % width != width - 1
        totals = {}
        for g0 in range(0, len(cells), group):
            part = cells[g0:g0 + group]
            lhs = jnp.concatenate(
                [jnp.concatenate([x_ref[n, r + dr] for n, r in part], axis=0) for dr in range(3)], axis=1
            )
            y = jnp.dot(lhs, w_ref[0], preferred_element_type=jnp.float32)
            out = (
                y[:, depth:2 * depth]
                + jnp.where(left, pltpu.roll(y[:, :depth], 1, 0), 0.0)
                + jnp.where(right, pltpu.roll(y[:, 2 * depth:], m - 1, 0), 0.0)
            )
            for k, (n, r) in enumerate(part):
                segment = out[k * width:(k + 1) * width]
                o_ref[n, r] = segment.astype(o_ref.dtype)
                if sums_ref is not None:
                    both = jnp.concatenate(
                        [jnp.sum(segment, axis=0, keepdims=True),
                         jnp.sum(segment * segment, axis=0, keepdims=True)], axis=0
                    )
                    totals[n] = both if n not in totals else totals[n] + both
        if sums_ref is not None:
            for n in range(count):
                sums_ref[n] = totals[n]
        return
    assert sums_ref is None
    for n in range(count):
        for r0 in range(0, rows_out, chunk):
            lhs = jnp.concatenate(
                [x_ref[n, r0 + dr:r0 + dr + chunk].reshape(m, depth) for dr in range(3)], axis=1
            )
            y = jnp.dot(lhs, w_ref[n], preferred_element_type=jnp.float32)
            out = (
                y[:, depth:2 * depth]
                + jnp.where(left, pltpu.roll(y[:, :depth], 1, 0), 0.0)
                + jnp.where(right, pltpu.roll(y[:, 2 * depth:], m - 1, 0), 0.0)
            )
            if finish:
                out = out + bias_ref[...]
                ms = jnp.mean(out * out, axis=1, keepdims=True)
                out = out * lax.rsqrt(ms + 1e-06)
                row = where_ref[0] + r0 + flat[:, 0:1] // width
                out = jnp.where((row >= 0) & (row < where_ref[1]), out, 0.0)
            o_ref[n, r0:r0 + chunk, lead:lead + width] = out.reshape(chunk, width, depth).astype(o_ref.dtype)


def conv_rows(field, kernel, flips, bias=None, first_row=None, total_rows=None, pad=(0, 0), dtype=jnp.bfloat16):
    count, rows_in, width, depth = field.shape
    vmem = pl.BlockSpec(memory_space=pltpu.VMEM)
    finish = bias is not None
    args = [field, kernel.astype(field.dtype)]
    specs = [vmem, vmem]
    if finish:
        where = jnp.stack([first_row, total_rows]).astype(jnp.int32)
        args = [where] + args + [bias.astype(jnp.float32).reshape(1, -1)]
        specs = [pl.BlockSpec(memory_space=pltpu.SMEM)] + specs + [vmem]
    return pl.pallas_call(
        functools.partial(_conv_kernel, finish=finish, lead=pad[0], trail=pad[1], flips=flips, plan=None),
        out_shape=jax.ShapeDtypeStruct(
            (count, rows_in - 2, pad[0] + width + pad[1], kernel.shape[3]), dtype if finish else jnp.float32
        ),
        in_specs=specs,
        out_specs=vmem,
        scratch_shapes=[pltpu.VMEM((count, 3 * depth, 3 * kernel.shape[3]), field.dtype)],
    )(*args)


def conv_gather(sources, gather, kernel, flips):
    count, rows_in = len(gather), len(gather[0])
    width, depth = sources[0].shape[-2], sources[0].shape[-1]
    vmem = pl.BlockSpec(memory_space=pltpu.VMEM)
    return pl.pallas_call(
        functools.partial(_conv_kernel, finish=False, lead=0, trail=0, flips=flips, plan=None, gather=gather),
        out_shape=(
            jax.ShapeDtypeStruct((count, rows_in - 2, width, kernel.shape[3]), jnp.float32),
            jax.ShapeDtypeStruct((count, 2, kernel.shape[3]), jnp.float32),
        ),
        in_specs=[vmem] * (len(sources) + 1),
        out_specs=(vmem, vmem),
        scratch_shapes=[
            pltpu.VMEM((count, 3 * depth, 3 * kernel.shape[3]), jnp.bfloat16),
            pltpu.VMEM((count, rows_in, width, depth), jnp.bfloat16),
        ],
    )(*sources, kernel.astype(jnp.bfloat16))


def conv_hidden(sources, plan, mean, inv_scale, kernel, flips, bias, first_in, total_rows, pad=(0, 0),
                dtype=jnp.bfloat16, reverse=False):
    rows_in = len(plan)
    width, depth = sources[0].shape[2], sources[0].shape[3]
    vmem = pl.BlockSpec(memory_space=pltpu.VMEM)
    where = jnp.stack([first_in + 1, total_rows, first_in]).astype(jnp.int32)
    args = [where, *sources, mean.reshape(1, -1), inv_scale.reshape(1, -1),
            kernel.astype(jnp.bfloat16), bias.astype(jnp.float32).reshape(1, -1)]
    specs = [pl.BlockSpec(memory_space=pltpu.SMEM)] + [vmem] * (len(sources) + 4)
    return pl.pallas_call(
        functools.partial(
            _conv_kernel, finish=True, lead=pad[0], trail=pad[1], flips=flips, plan=plan, reverse=reverse
        ),
        out_shape=jax.ShapeDtypeStruct((1, rows_in - 2, pad[0] + width + pad[1], kernel.shape[3]), dtype),
        in_specs=specs,
        out_specs=vmem,
        scratch_shapes=[
            pltpu.VMEM((1, 3 * depth, 3 * kernel.shape[3]), jnp.bfloat16),
            pltpu.VMEM((1, rows_in, width, depth), jnp.bfloat16),
        ],
    )(*args)


def finish_features(second_out, latter_kernel_intercept):
    shifted = second_out + latter_kernel_intercept
    return (
        shifted * lax.rsqrt(jnp.mean(shifted * shifted, axis=-1, keepdims=True) + 1e-06)
    ).astype(jnp.bfloat16)


def in_map(rows_from, count, rows_dev):
    total = rows_dev * lax.axis_size("rows")
    first = lax.axis_index("rows") * rows_dev + rows_from
    row = first + lax.broadcasted_iota(jnp.int32, (count, 1, 1), 0)
    return (row >= 0) & (row < total)


def local(
    specimen_pair_inputs,
    initial_kernel_tensor,
    latter_kernel_tensor,
    latter_kernel_intercept,
    patch_horizontal_shift,
    specimen_presence,
    softmax_sharpening,
):
    x0 = specimen_pair_inputs[0]
    x1 = specimen_pair_inputs[1]
    k1 = initial_kernel_tensor
    rows_dev = x0.shape[0]
    width = x0.shape[1]
    size = lax.axis_size("rows")
    cells_all = rows_dev * size * width
    near, far = 2, 6
    up = [(i, i + 1) for i in range(size - 1)]
    down = [(i + 1, i) for i in range(size - 1)]
    before = lax.ppermute(
        jnp.concatenate([x0[rows_dev - near:], x1[rows_dev - far:]], axis=0), "rows", up
    )
    after = lax.ppermute(
        jnp.concatenate([x0[:near], x1[:far]], axis=0), "rows", down
    )

    def row0(r):
        if r < 0:
            return (2, (near + r,))
        if r >= rows_dev:
            return (3, (r - rows_dev,))
        return (0, (0, r))

    def row1(r):
        if r < 0:
            return (2, (near + far + r,))
        if r >= rows_dev:
            return (3, (near + r - rows_dev,))
        return (1, (r,))

    def rows_of(pick, lo, hi):
        return tuple(pick(r) for r in range(lo, hi))

    inputs = (specimen_pair_inputs, x1)
    halos = (specimen_pair_inputs, x1, before, after)
    interior, inner_sums = conv_gather(inputs, (rows_of(row0, 0, rows_dev), rows_of(row1, 0, rows_dev)), k1, (False, False))
    boundary, edge_sums = conv_gather(
        halos,
        (
            rows_of(row0, -1, 2),
            rows_of(row0, rows_dev - 2, rows_dev + 1),
            rows_of(row1, -1, 2),
            rows_of(row1, rows_dev - 2, rows_dev + 1),
        ),
        k1,
        (False, False, False, False),
    )
    per_slide = inner_sums + edge_sums[0::2] + edge_sums[1::2]
    stats = jnp.concatenate([per_slide[:, 0], per_slide[:, 1]], axis=0)
    stats, halos = butterfly_sum(stats, "rows", halos)
    average = stats[0:2] / cells_all
    variance = stats[2:4] / cells_all - average * average
    inv_scale = lax.rsqrt(variance + 1e-05)
    edge0, _ = conv_gather(
        halos, (rows_of(row0, -near, 1), rows_of(row0, rows_dev - 1, rows_dev + near)), k1, (False, False)
    )
    edge1, _ = conv_gather(
        halos, (rows_of(row1, -far, 1), rows_of(row1, rows_dev - 1, rows_dev + far)), k1, (False, False)
    )
    sources = (edge0, boundary, interior, edge1)
    plan0 = ((0, 0, 0), (1, 0, 0)) + tuple((2, 0, r) for r in range(rows_dev - 2)) + ((1, 1, 0), (0, 1, 0))
    halo = far - 1
    plan1 = (
        tuple((3, 0, r) for r in range(halo))
        + ((1, 2, 0),)
        + tuple((2, 1, r) for r in range(rows_dev - 2))
        + ((1, 3, 0),)
        + tuple((3, 1, r) for r in range(halo))
    )
    total = rows_dev * size
    first = lax.axis_index("rows") * rows_dev
    source = conv_hidden(
        sources, plan0, average[0], inv_scale[0], latter_kernel_tensor, (False,),
        latter_kernel_intercept, first - 1, total,
    )[0]
    target_reversed = conv_hidden(
        sources, plan1, average[1], inv_scale[1], latter_kernel_tensor, (True,),
        latter_kernel_intercept, first - halo, total, pad=(64, 8), dtype=jnp.float32, reverse=True,
    )[0]
    return correlation(
        source,
        target_reversed,
        patch_horizontal_shift,
        specimen_presence,
        softmax_sharpening,
    )


def solution(mesh):
    return jax.shard_map(
        local,
        mesh=mesh,
        in_specs=(
            P(None, ("pairs", "rows"), None, None),
            P(),
            P(),
            P(),
            P(("pairs", "rows"), None),
            P(("pairs", "rows"), None),
            P(("pairs", "rows"), None),
        ),
        out_specs=P(None, ("pairs", "rows"), None),
        check_vma=False,
    )
```

```python
import functools

import jax
import jax.numpy as jnp
from jax import lax
from jax.sharding import PartitionSpec as P
from jax.experimental import pallas as pl
from jax.experimental.pallas import tpu as pltpu

DISP = 81


def _corr_kernel(shift_ref, sharp_ref, pres_ref, f0_ref, frev_hbm, out_ref, win_ref, acc_ref, sems):
    rows = f0_ref.shape[0]
    half = f0_ref.shape[1] // 4
    copies = []
    for t in range(2):
        for q in range(2):
            start = 196 - 128 * t - half * q - shift_ref[0, t]
            cp = pltpu.make_async_copy(frev_hbm.at[:, pl.ds(start, 128), :], win_ref.at[2 * t + q],
                                       sems.at[2 * t + q])
            cp.start()
            copies.append(cp)
    lane = lax.broadcasted_iota(jnp.int32, (half, 128), 1)
    band = lane // 9
    li = lax.broadcasted_iota(jnp.int32, (128, 1), 0)
    valid = li < DISP
    row_d = jnp.where(valid, li // 9 - 4, 0).astype(jnp.float32)
    col_d = jnp.where(valid, 4 - li % 9, 0).astype(jnp.float32)
    for t in range(2):
        shift_t = shift_ref[0, t].astype(jnp.float32)
        scale = sharp_ref[0, t] / 128.0
        present = pres_ref[0, t].astype(jnp.float32)
        for q in range(2):
            cols = slice(128 * t + half * q, 128 * t + half * (q + 1))
            copies[2 * t + q].wait()
            acc_ref[...] = jnp.zeros_like(acc_ref)
            for hp in range(rows + 8):
                lo, hi = max(0, hp - 8), min(rows - 1, hp)
                lhs = f0_ref[lo:hi + 1, cols, :].reshape((hi - lo + 1) * half, 128)
                w = win_ref[2 * t + q, hp].astype(jnp.bfloat16)
                s = lax.dot_general(lhs, w, (((1,), (1,)), ((), ())), preferred_element_type=jnp.float32)
                for h in range(lo, hi + 1):
                    a = hp - h
                    blk = s[(h - lo) * half:(h - lo + 1) * half]
                    rolled = pltpu.roll(blk, 9 + 9 * a, 1, stride=1, stride_axis=0)
                    acc_ref[h] = jnp.where(band == a, rolled, acc_ref[h])
            for i in range(rows // 2):
                pair = acc_ref[2 * i:2 * i + 2].reshape(2 * half, 128)
                energy = jnp.transpose(pair) * scale
                energy = jnp.where(valid, energy, -jnp.inf)
                top = jnp.max(energy, axis=0, keepdims=True)
                p = jnp.exp(energy - top)
                inv = 1.0 / jnp.sum(p, axis=0, keepdims=True)
                fy = jnp.sum(p * row_d, axis=0, keepdims=True) * inv * present
                fx = (jnp.sum(p * col_d, axis=0, keepdims=True) * inv + shift_t) * present
                for k in range(2):
                    out_ref[0, 2 * i + k:2 * i + k + 1, cols] = fy[:, k * half:(k + 1) * half]
                    out_ref[1, 2 * i + k:2 * i + k + 1, cols] = fx[:, k * half:(k + 1) * half]


def correlation(f0, f1rev_ext, shift, presence, sharp):
    rows, width, depth = f0.shape
    frev = f1rev_ext
    return pl.pallas_call(
        _corr_kernel,
        out_shape=jax.ShapeDtypeStruct((2, rows, width), jnp.float32),
        in_specs=[pl.BlockSpec(memory_space=pltpu.SMEM)] * 3
        + [pl.BlockSpec(memory_space=pltpu.VMEM), pl.BlockSpec(memory_space=pl.ANY)],
        out_specs=pl.BlockSpec(memory_space=pltpu.VMEM),
        scratch_shapes=[
            pltpu.VMEM((4, rows + 8, 128, depth), jnp.float32),
            pltpu.VMEM((rows, 64, 128), jnp.float32),
            pltpu.SemaphoreType.DMA((4,)),
        ],
    )(shift, sharp, presence, f0, frev)


def extended(array, sides, width):
    for axis, dim in sides:
        size, length = (lax.axis_size(axis), array.shape[dim])
        up = [(i, (i + 1) % size) for i in range(size - 1)]
        down = [(j, i) for i, j in up]
        last = lax.slice_in_dim(array, length - width, length, axis=dim)
        initial = lax.slice_in_dim(array, 0, width, axis=dim)
        before = lax.ppermute(last, axis, up)
        after = lax.ppermute(initial, axis, down)
        array = jnp.concatenate([before, array, after], axis=dim)
    return array


def butterfly_sum(x, axis, fillers):
    size = lax.axis_size(axis)
    if size & (size - 1):
        return lax.psum(x, axis), [fill() for fill in fillers]
    done = []
    step = 1
    while step < size:
        moved = lax.ppermute(x, axis, [(i, i ^ step) for i in range(size)])
        if len(done) < len(fillers):
            value = fillers[len(done)]()
            x, value = lax.optimization_barrier((x + moved, value))
            done.append(value)
        else:
            x = x + moved
        step *= 2
    return x, done + [fill() for fill in fillers[len(done):]]


def _reverse_rows(value):
    tiles = value.shape[0] // 8
    v = value.reshape(tiles, 8, value.shape[1])
    v = jnp.concatenate([v[i:i + 1] for i in reversed(range(tiles))], axis=0)
    sub = lax.broadcasted_iota(jnp.int32, v.shape, 1)
    for step in (1, 2, 4):
        v = jnp.where((sub & step) != 0, pltpu.roll(v, step, 1), pltpu.roll(v, 8 - step, 1))
    return v.reshape(value.shape)


def _conv_kernel(*refs, finish, lead, trail, flips, plan, gather=None, reverse=False):
    sums_ref = None
    if gather:
        *sources, k_ref, o_ref, sums_ref, w_ref, x_ref = refs
        for n, rows in enumerate(gather):
            for r, (which, index) in enumerate(rows):
                x_ref[n, r] = sources[which][index].astype(x_ref.dtype)
    elif plan:
        where_ref, *sources, mean_ref, inv_ref, k_ref, bias_ref, o_ref, w_ref, x_ref = refs
        for r, (which, n, row) in enumerate(plan):
            value = jnp.maximum((sources[which][n, row] - mean_ref[...]) * inv_ref[...], 0.0)
            g = where_ref[2] + r
            keep = (g >= 0) & (g < where_ref[1])
            value = jnp.where(keep, value, 0.0)
            if reverse:
                value = _reverse_rows(value)
            x_ref[0, r] = value.astype(x_ref.dtype)
    elif finish:
        where_ref, x_ref, k_ref, bias_ref, o_ref, w_ref = refs
    else:
        x_ref, k_ref, o_ref, w_ref = refs
    count, rows_out, _, depth = o_ref.shape
    width = x_ref.shape[2]
    for n, flip in enumerate(flips):
        for dr in range(3):
            for dc in range(3):
                w_ref[n, dr * depth:(dr + 1) * depth, dc * depth:(dc + 1) * depth] = k_ref[
                    dr, 2 - dc if flip else dc
                ]
    if lead:
        o_ref[:, :, :lead] = jnp.zeros((count, rows_out, lead, depth), o_ref.dtype)
    if trail:
        o_ref[:, :, lead + width:] = jnp.zeros((count, rows_out, trail, depth), o_ref.dtype)
    chunk = 4 if rows_out % 4 == 0 else (2 if rows_out % 2 == 0 else 1)
    m = chunk * width
    flat = lax.broadcasted_iota(jnp.int32, (m, depth), 0)
    left = flat % width != 0
    right = flat % width != width - 1
    if len(set(flips)) == 1 and chunk < 4 and count > 1:
        cells = [(n, r) for n in range(count) for r in range(rows_out)]
        group = max(1, min(len(cells), 1024 // width))
        while len(cells) % group:
            group -= 1
        m = group * width
        flat = lax.broadcasted_iota(jnp.int32, (m, depth), 0)
        left = flat % width != 0
        right = flat % width != width - 1
        totals = {}
        for g0 in range(0, len(cells), group):
            part = cells[g0:g0 + group]
            lhs = jnp.concatenate(
                [jnp.concatenate([x_ref[n, r + dr] for n, r in part], axis=0) for dr in range(3)], axis=1
            )
            y = jnp.dot(lhs, w_ref[0], preferred_element_type=jnp.float32)
            out = (
                y[:, depth:2 * depth]
                + jnp.where(left, pltpu.roll(y[:, :depth], 1, 0), 0.0)
                + jnp.where(right, pltpu.roll(y[:, 2 * depth:], m - 1, 0), 0.0)
            )
            for k, (n, r) in enumerate(part):
                segment = out[k * width:(k + 1) * width]
                o_ref[n, r] = segment.astype(o_ref.dtype)
                if sums_ref is not None:
                    both = jnp.concatenate(
                        [jnp.sum(segment, axis=0, keepdims=True),
                         jnp.sum(segment * segment, axis=0, keepdims=True)], axis=0
                    )
                    totals[n] = both if n not in totals else totals[n] + both
        if sums_ref is not None:
            for n in range(count):
                sums_ref[n] = totals[n]
        return
    assert sums_ref is None
    for n in range(count):
        for r0 in range(0, rows_out, chunk):
            lhs = jnp.concatenate(
                [x_ref[n, r0 + dr:r0 + dr + chunk].reshape(m, depth) for dr in range(3)], axis=1
            )
            y = jnp.dot(lhs, w_ref[n], preferred_element_type=jnp.float32)
            out = (
                y[:, depth:2 * depth]
                + jnp.where(left, pltpu.roll(y[:, :depth], 1, 0), 0.0)
                + jnp.where(right, pltpu.roll(y[:, 2 * depth:], m - 1, 0), 0.0)
            )
            if finish:
                out = out + bias_ref[...]
                ms = jnp.mean(out * out, axis=1, keepdims=True)
                out = out * lax.rsqrt(ms + 1e-06)
                row = where_ref[0] + r0 + flat[:, 0:1] // width
                out = jnp.where((row >= 0) & (row < where_ref[1]), out, 0.0)
            o_ref[n, r0:r0 + chunk, lead:lead + width] = out.reshape(chunk, width, depth).astype(o_ref.dtype)


def conv_rows(field, kernel, flips, bias=None, first_row=None, total_rows=None, pad=(0, 0), dtype=jnp.bfloat16):
    count, rows_in, width, depth = field.shape
    vmem = pl.BlockSpec(memory_space=pltpu.VMEM)
    finish = bias is not None
    args = [field, kernel.astype(field.dtype)]
    specs = [vmem, vmem]
    if finish:
        where = jnp.stack([first_row, total_rows]).astype(jnp.int32)
        args = [where] + args + [bias.astype(jnp.float32).reshape(1, -1)]
        specs = [pl.BlockSpec(memory_space=pltpu.SMEM)] + specs + [vmem]
    return pl.pallas_call(
        functools.partial(_conv_kernel, finish=finish, lead=pad[0], trail=pad[1], flips=flips, plan=None),
        out_shape=jax.ShapeDtypeStruct(
            (count, rows_in - 2, pad[0] + width + pad[1], kernel.shape[3]), dtype if finish else jnp.float32
        ),
        in_specs=specs,
        out_specs=vmem,
        scratch_shapes=[pltpu.VMEM((count, 3 * depth, 3 * kernel.shape[3]), field.dtype)],
    )(*args)


def conv_gather(sources, gather, kernel, flips):
    count, rows_in = len(gather), len(gather[0])
    width, depth = sources[0].shape[-2], sources[0].shape[-1]
    vmem = pl.BlockSpec(memory_space=pltpu.VMEM)
    return pl.pallas_call(
        functools.partial(_conv_kernel, finish=False, lead=0, trail=0, flips=flips, plan=None, gather=gather),
        out_shape=(
            jax.ShapeDtypeStruct((count, rows_in - 2, width, kernel.shape[3]), jnp.float32),
            jax.ShapeDtypeStruct((count, 2, kernel.shape[3]), jnp.float32),
        ),
        in_specs=[vmem] * (len(sources) + 1),
        out_specs=(vmem, vmem),
        scratch_shapes=[
            pltpu.VMEM((count, 3 * depth, 3 * kernel.shape[3]), jnp.bfloat16),
            pltpu.VMEM((count, rows_in, width, depth), jnp.bfloat16),
        ],
    )(*sources, kernel.astype(jnp.bfloat16))


def conv_hidden(sources, plan, mean, inv_scale, kernel, flips, bias, first_in, total_rows, pad=(0, 0),
                dtype=jnp.bfloat16, reverse=False):
    rows_in = len(plan)
    width, depth = sources[0].shape[2], sources[0].shape[3]
    vmem = pl.BlockSpec(memory_space=pltpu.VMEM)
    where = jnp.stack([first_in + 1, total_rows, first_in]).astype(jnp.int32)
    args = [where, *sources, mean.reshape(1, -1), inv_scale.reshape(1, -1),
            kernel.astype(jnp.bfloat16), bias.astype(jnp.float32).reshape(1, -1)]
    specs = [pl.BlockSpec(memory_space=pltpu.SMEM)] + [vmem] * (len(sources) + 4)
    return pl.pallas_call(
        functools.partial(
            _conv_kernel, finish=True, lead=pad[0], trail=pad[1], flips=flips, plan=plan, reverse=reverse
        ),
        out_shape=jax.ShapeDtypeStruct((1, rows_in - 2, pad[0] + width + pad[1], kernel.shape[3]), dtype),
        in_specs=specs,
        out_specs=vmem,
        scratch_shapes=[
            pltpu.VMEM((1, 3 * depth, 3 * kernel.shape[3]), jnp.bfloat16),
            pltpu.VMEM((1, rows_in, width, depth), jnp.bfloat16),
        ],
    )(*args)


def finish_features(second_out, latter_kernel_intercept):
    shifted = second_out + latter_kernel_intercept
    return (
        shifted * lax.rsqrt(jnp.mean(shifted * shifted, axis=-1, keepdims=True) + 1e-06)
    ).astype(jnp.bfloat16)


def in_map(rows_from, count, rows_dev):
    total = rows_dev * lax.axis_size("rows")
    first = lax.axis_index("rows") * rows_dev + rows_from
    row = first + lax.broadcasted_iota(jnp.int32, (count, 1, 1), 0)
    return (row >= 0) & (row < total)


def local(
    specimen_pair_inputs,
    initial_kernel_tensor,
    latter_kernel_tensor,
    latter_kernel_intercept,
    patch_horizontal_shift,
    specimen_presence,
    softmax_sharpening,
):
    x0 = specimen_pair_inputs[0]
    x1 = specimen_pair_inputs[1]
    k1 = initial_kernel_tensor
    rows_dev = x0.shape[0]
    width = x0.shape[1]
    size = lax.axis_size("rows")
    cells_all = rows_dev * size * width
    near, far = 2, 6
    up = [(i, i + 1) for i in range(size - 1)]
    down = [(i + 1, i) for i in range(size - 1)]
    before = lax.ppermute(
        jnp.concatenate([x0[rows_dev - near:], x1[rows_dev - far:]], axis=0), "rows", up
    )
    after = lax.ppermute(
        jnp.concatenate([x0[:near], x1[:far]], axis=0), "rows", down
    )

    def row0(r):
        if r < 0:
            return (2, (near + r,))
        if r >= rows_dev:
            return (3, (r - rows_dev,))
        return (0, (0, r))

    def row1(r):
        if r < 0:
            return (2, (near + far + r,))
        if r >= rows_dev:
            return (3, (near + r - rows_dev,))
        return (1, (r,))

    def rows_of(pick, lo, hi):
        return tuple(pick(r) for r in range(lo, hi))

    inputs = (specimen_pair_inputs, x1)
    halos = (specimen_pair_inputs, x1, before, after)
    interior, inner_sums = conv_gather(inputs, (rows_of(row0, 0, rows_dev), rows_of(row1, 0, rows_dev)), k1, (False, False))
    boundary, edge_sums = conv_gather(
        halos,
        (
            rows_of(row0, -1, 2),
            rows_of(row0, rows_dev - 2, rows_dev + 1),
            rows_of(row1, -1, 2),
            rows_of(row1, rows_dev - 2, rows_dev + 1),
        ),
        k1,
        (False, False, False, False),
    )
    per_slide = inner_sums + edge_sums[0::2] + edge_sums[1::2]
    stats = jnp.concatenate([per_slide[:, 0], per_slide[:, 1]], axis=0)
    stats, (edge0, edge1) = butterfly_sum(
        stats,
        "rows",
        [
            lambda: conv_gather(
                halos, (rows_of(row0, -near, 1), rows_of(row0, rows_dev - 1, rows_dev + near)), k1, (False, False)
            )[0],
            lambda: conv_gather(
                halos, (rows_of(row1, -far, 1), rows_of(row1, rows_dev - 1, rows_dev + far)), k1, (False, False)
            )[0],
        ],
    )
    average = stats[0:2] / cells_all
    variance = stats[2:4] / cells_all - average * average
    inv_scale = lax.rsqrt(variance + 1e-05)
    sources = (edge0, boundary, interior, edge1)
    plan0 = ((0, 0, 0), (1, 0, 0)) + tuple((2, 0, r) for r in range(rows_dev - 2)) + ((1, 1, 0), (0, 1, 0))
    halo = far - 1
    plan1 = (
        tuple((3, 0, r) for r in range(halo))
        + ((1, 2, 0),)
        + tuple((2, 1, r) for r in range(rows_dev - 2))
        + ((1, 3, 0),)
        + tuple((3, 1, r) for r in range(halo))
    )
    total = rows_dev * size
    first = lax.axis_index("rows") * rows_dev
    source = conv_hidden(
        sources, plan0, average[0], inv_scale[0], latter_kernel_tensor, (False,),
        latter_kernel_intercept, first - 1, total,
    )[0]
    target_reversed = conv_hidden(
        sources, plan1, average[1], inv_scale[1], latter_kernel_tensor, (True,),
        latter_kernel_intercept, first - halo, total, pad=(64, 8), dtype=jnp.float32, reverse=True,
    )[0]
    return correlation(
        source,
        target_reversed,
        patch_horizontal_shift,
        specimen_presence,
        softmax_sharpening,
    )


def solution(mesh):
    return jax.shard_map(
        local,
        mesh=mesh,
        in_specs=(
            P(None, ("pairs", "rows"), None, None),
            P(),
            P(),
            P(),
            P(("pairs", "rows"), None),
            P(("pairs", "rows"), None),
            P(("pairs", "rows"), None),
        ),
        out_specs=P(None, ("pairs", "rows"), None),
        check_vma=False,
    )
```

```python
import functools

import jax
import jax.numpy as jnp
from jax import lax
from jax.sharding import PartitionSpec as P
from jax.experimental import pallas as pl
from jax.experimental.pallas import tpu as pltpu

DISP = 81


def _corr_kernel(shift_ref, sharp_ref, pres_ref, f0_ref, frev_hbm, out_ref, win_ref, acc_ref, sems):
    rows = f0_ref.shape[0]
    half = f0_ref.shape[1] // 4
    copies = []
    for t in range(2):
        for q in range(2):
            start = 196 - 128 * t - half * q - shift_ref[0, t]
            cp = pltpu.make_async_copy(frev_hbm.at[:, pl.ds(start, 128), :], win_ref.at[2 * t + q],
                                       sems.at[2 * t + q])
            cp.start()
            copies.append(cp)
    lane = lax.broadcasted_iota(jnp.int32, (half, 128), 1)
    band = lane // 9
    li = lax.broadcasted_iota(jnp.int32, (128, 1), 0)
    valid = li < DISP
    row_d = jnp.where(valid, li // 9 - 4, 0).astype(jnp.float32)
    col_d = jnp.where(valid, 4 - li % 9, 0).astype(jnp.float32)
    for t in range(2):
        shift_t = shift_ref[0, t].astype(jnp.float32)
        scale = sharp_ref[0, t] / 128.0
        present = pres_ref[0, t].astype(jnp.float32)
        for q in range(2):
            cols = slice(128 * t + half * q, 128 * t + half * (q + 1))
            copies[2 * t + q].wait()
            acc_ref[...] = jnp.zeros_like(acc_ref)
            for hp in range(rows + 8):
                lo, hi = max(0, hp - 8), min(rows - 1, hp)
                lhs = f0_ref[lo:hi + 1, cols, :].reshape((hi - lo + 1) * half, 128)
                w = win_ref[2 * t + q, hp].astype(jnp.bfloat16)
                s = lax.dot_general(lhs, w, (((1,), (1,)), ((), ())), preferred_element_type=jnp.float32)
                for h in range(lo, hi + 1):
                    a = hp - h
                    blk = s[(h - lo) * half:(h - lo + 1) * half]
                    rolled = pltpu.roll(blk, 9 + 9 * a, 1, stride=1, stride_axis=0)
                    acc_ref[h] = jnp.where(band == a, rolled, acc_ref[h])
            for i in range(rows // 2):
                pair = acc_ref[2 * i:2 * i + 2].reshape(2 * half, 128)
                energy = jnp.transpose(pair) * scale
                energy = jnp.where(valid, energy, -jnp.inf)
                top = jnp.max(energy, axis=0, keepdims=True)
                p = jnp.exp(energy - top)
                inv = 1.0 / jnp.sum(p, axis=0, keepdims=True)
                fy = jnp.sum(p * row_d, axis=0, keepdims=True) * inv * present
                fx = (jnp.sum(p * col_d, axis=0, keepdims=True) * inv + shift_t) * present
                for k in range(2):
                    out_ref[0, 2 * i + k:2 * i + k + 1, cols] = fy[:, k * half:(k + 1) * half]
                    out_ref[1, 2 * i + k:2 * i + k + 1, cols] = fx[:, k * half:(k + 1) * half]


def correlation(f0, f1rev_ext, shift, presence, sharp):
    rows, width, depth = f0.shape
    frev = f1rev_ext
    return pl.pallas_call(
        _corr_kernel,
        out_shape=jax.ShapeDtypeStruct((2, rows, width), jnp.float32),
        in_specs=[pl.BlockSpec(memory_space=pltpu.SMEM)] * 3
        + [pl.BlockSpec(memory_space=pltpu.VMEM), pl.BlockSpec(memory_space=pl.ANY)],
        out_specs=pl.BlockSpec(memory_space=pltpu.VMEM),
        scratch_shapes=[
            pltpu.VMEM((4, rows + 8, 128, depth), jnp.float32),
            pltpu.VMEM((rows, 64, 128), jnp.float32),
            pltpu.SemaphoreType.DMA((4,)),
        ],
    )(shift, sharp, presence, f0, frev)


def extended(array, sides, width):
    for axis, dim in sides:
        size, length = (lax.axis_size(axis), array.shape[dim])
        up = [(i, (i + 1) % size) for i in range(size - 1)]
        down = [(j, i) for i, j in up]
        last = lax.slice_in_dim(array, length - width, length, axis=dim)
        initial = lax.slice_in_dim(array, 0, width, axis=dim)
        before = lax.ppermute(last, axis, up)
        after = lax.ppermute(initial, axis, down)
        array = jnp.concatenate([before, array, after], axis=dim)
    return array


def butterfly_sum(x, axis, fillers):
    size = lax.axis_size(axis)
    if size & (size - 1):
        return lax.psum(x, axis), [fill() for fill in fillers]
    done = []
    step = 1
    while step < size:
        moved = lax.ppermute(x, axis, [(i, i ^ step) for i in range(size)])
        if len(done) < len(fillers):
            value = fillers[len(done)]()
            x, value = lax.optimization_barrier((x + moved, value))
            done.append(value)
        else:
            x = x + moved
        step *= 2
    return x, done + [fill() for fill in fillers[len(done):]]


def _reverse_rows(value):
    tiles = value.shape[0] // 8
    v = value.reshape(tiles, 8, value.shape[1])
    v = jnp.concatenate([v[i:i + 1] for i in reversed(range(tiles))], axis=0)
    sub = lax.broadcasted_iota(jnp.int32, v.shape, 1)
    for step in (1, 2, 4):
        v = jnp.where((sub & step) != 0, pltpu.roll(v, step, 1), pltpu.roll(v, 8 - step, 1))
    return v.reshape(value.shape)


def _conv_kernel(*refs, finish, lead, trail, flips, plan, gather=None, reverse=False):
    sums_ref = None
    if gather:
        *sources, k_ref, o_ref, sums_ref, w_ref, x_ref = refs
        for n, rows in enumerate(gather):
            for r, (which, index) in enumerate(rows):
                x_ref[n, r] = sources[which][index].astype(x_ref.dtype)
    elif plan:
        where_ref, *sources, mean_ref, inv_ref, k_ref, bias_ref, o_ref, w_ref, x_ref = refs
        for r, (which, n, row) in enumerate(plan):
            value = jnp.maximum((sources[which][n, row] - mean_ref[...]) * inv_ref[...], 0.0)
            g = where_ref[2] + r
            keep = (g >= 0) & (g < where_ref[1])
            value = jnp.where(keep, value, 0.0)
            if reverse:
                value = _reverse_rows(value)
            x_ref[0, r] = value.astype(x_ref.dtype)
    elif finish:
        where_ref, x_ref, k_ref, bias_ref, o_ref, w_ref = refs
    else:
        x_ref, k_ref, o_ref, w_ref = refs
    count, rows_out, _, depth = o_ref.shape
    width = x_ref.shape[2]
    for n, flip in enumerate(flips):
        for dr in range(3):
            for dc in range(3):
                w_ref[n, dr * depth:(dr + 1) * depth, dc * depth:(dc + 1) * depth] = k_ref[
                    dr, 2 - dc if flip else dc
                ]
    if lead:
        o_ref[:, :, :lead] = jnp.zeros((count, rows_out, lead, depth), o_ref.dtype)
    if trail:
        o_ref[:, :, lead + width:] = jnp.zeros((count, rows_out, trail, depth), o_ref.dtype)
    chunk = 4 if rows_out % 4 == 0 else (2 if rows_out % 2 == 0 else 1)
    m = chunk * width
    flat = lax.broadcasted_iota(jnp.int32, (m, depth), 0)
    left = flat % width != 0
    right = flat % width != width - 1
    if len(set(flips)) == 1 and chunk < 4 and count > 1:
        cells = [(n, r) for n in range(count) for r in range(rows_out)]
        group = max(1, min(len(cells), 1024 // width))
        while len(cells) % group:
            group -= 1
        m = group * width
        flat = lax.broadcasted_iota(jnp.int32, (m, depth), 0)
        left = flat % width != 0
        right = flat % width != width - 1
        totals = {}
        for g0 in range(0, len(cells), group):
            part = cells[g0:g0 + group]
            lhs = jnp.concatenate(
                [jnp.concatenate([x_ref[n, r + dr] for n, r in part], axis=0) for dr in range(3)], axis=1
            )
            y = jnp.dot(lhs, w_ref[0], preferred_element_type=jnp.float32)
            out = (
                y[:, depth:2 * depth]
                + jnp.where(left, pltpu.roll(y[:, :depth], 1, 0), 0.0)
                + jnp.where(right, pltpu.roll(y[:, 2 * depth:], m - 1, 0), 0.0)
            )
            for k, (n, r) in enumerate(part):
                segment = out[k * width:(k + 1) * width]
                o_ref[n, r] = segment.astype(o_ref.dtype)
                if sums_ref is not None:
                    both = jnp.concatenate(
                        [jnp.sum(segment, axis=0, keepdims=True),
                         jnp.sum(segment * segment, axis=0, keepdims=True)], axis=0
                    )
                    totals[n] = both if n not in totals else totals[n] + both
        if sums_ref is not None:
            for n in range(count):
                sums_ref[n] = totals[n]
        return
    assert sums_ref is None
    for n in range(count):
        for r0 in range(0, rows_out, chunk):
            lhs = jnp.concatenate(
                [x_ref[n, r0 + dr:r0 + dr + chunk].reshape(m, depth) for dr in range(3)], axis=1
            )
            y = jnp.dot(lhs, w_ref[n], preferred_element_type=jnp.float32)
            out = (
                y[:, depth:2 * depth]
                + jnp.where(left, pltpu.roll(y[:, :depth], 1, 0), 0.0)
                + jnp.where(right, pltpu.roll(y[:, 2 * depth:], m - 1, 0), 0.0)
            )
            if finish:
                out = out + bias_ref[...]
                ms = jnp.mean(out * out, axis=1, keepdims=True)
                out = out * lax.rsqrt(ms + 1e-06)
                row = where_ref[0] + r0 + flat[:, 0:1] // width
                out = jnp.where((row >= 0) & (row < where_ref[1]), out, 0.0)
            o_ref[n, r0:r0 + chunk, lead:lead + width] = out.reshape(chunk, width, depth).astype(o_ref.dtype)


def conv_rows(field, kernel, flips, bias=None, first_row=None, total_rows=None, pad=(0, 0), dtype=jnp.bfloat16):
    count, rows_in, width, depth = field.shape
    vmem = pl.BlockSpec(memory_space=pltpu.VMEM)
    finish = bias is not None
    args = [field, kernel.astype(field.dtype)]
    specs = [vmem, vmem]
    if finish:
        where = jnp.stack([first_row, total_rows]).astype(jnp.int32)
        args = [where] + args + [bias.astype(jnp.float32).reshape(1, -1)]
        specs = [pl.BlockSpec(memory_space=pltpu.SMEM)] + specs + [vmem]
    return pl.pallas_call(
        functools.partial(_conv_kernel, finish=finish, lead=pad[0], trail=pad[1], flips=flips, plan=None),
        out_shape=jax.ShapeDtypeStruct(
            (count, rows_in - 2, pad[0] + width + pad[1], kernel.shape[3]), dtype if finish else jnp.float32
        ),
        in_specs=specs,
        out_specs=vmem,
        scratch_shapes=[pltpu.VMEM((count, 3 * depth, 3 * kernel.shape[3]), field.dtype)],
    )(*args)


def conv_gather(sources, gather, kernel, flips):
    count, rows_in = len(gather), len(gather[0])
    width, depth = sources[0].shape[-2], sources[0].shape[-1]
    vmem = pl.BlockSpec(memory_space=pltpu.VMEM)
    return pl.pallas_call(
        functools.partial(_conv_kernel, finish=False, lead=0, trail=0, flips=flips, plan=None, gather=gather),
        out_shape=(
            jax.ShapeDtypeStruct((count, rows_in - 2, width, kernel.shape[3]), jnp.float32),
            jax.ShapeDtypeStruct((count, 2, kernel.shape[3]), jnp.float32),
        ),
        in_specs=[vmem] * (len(sources) + 1),
        out_specs=(vmem, vmem),
        scratch_shapes=[
            pltpu.VMEM((count, 3 * depth, 3 * kernel.shape[3]), jnp.bfloat16),
            pltpu.VMEM((count, rows_in, width, depth), jnp.bfloat16),
        ],
    )(*sources, kernel.astype(jnp.bfloat16))


def conv_hidden(sources, plan, mean, inv_scale, kernel, flips, bias, first_in, total_rows, pad=(0, 0),
                dtype=jnp.bfloat16, reverse=False):
    rows_in = len(plan)
    width, depth = sources[0].shape[2], sources[0].shape[3]
    vmem = pl.BlockSpec(memory_space=pltpu.VMEM)
    where = jnp.stack([first_in + 1, total_rows, first_in]).astype(jnp.int32)
    args = [where, *sources, mean.reshape(1, -1), inv_scale.reshape(1, -1),
            kernel.astype(jnp.bfloat16), bias.astype(jnp.float32).reshape(1, -1)]
    specs = [pl.BlockSpec(memory_space=pltpu.SMEM)] + [vmem] * (len(sources) + 4)
    return pl.pallas_call(
        functools.partial(
            _conv_kernel, finish=True, lead=pad[0], trail=pad[1], flips=flips, plan=plan, reverse=reverse
        ),
        out_shape=jax.ShapeDtypeStruct((1, rows_in - 2, pad[0] + width + pad[1], kernel.shape[3]), dtype),
        in_specs=specs,
        out_specs=vmem,
        scratch_shapes=[
            pltpu.VMEM((1, 3 * depth, 3 * kernel.shape[3]), jnp.bfloat16),
            pltpu.VMEM((1, rows_in, width, depth), jnp.bfloat16),
        ],
    )(*args)


def finish_features(second_out, latter_kernel_intercept):
    shifted = second_out + latter_kernel_intercept
    return (
        shifted * lax.rsqrt(jnp.mean(shifted * shifted, axis=-1, keepdims=True) + 1e-06)
    ).astype(jnp.bfloat16)


def in_map(rows_from, count, rows_dev):
    total = rows_dev * lax.axis_size("rows")
    first = lax.axis_index("rows") * rows_dev + rows_from
    row = first + lax.broadcasted_iota(jnp.int32, (count, 1, 1), 0)
    return (row >= 0) & (row < total)


def local(
    specimen_pair_inputs,
    initial_kernel_tensor,
    latter_kernel_tensor,
    latter_kernel_intercept,
    patch_horizontal_shift,
    specimen_presence,
    softmax_sharpening,
):
    x0 = specimen_pair_inputs[0]
    x1 = specimen_pair_inputs[1]
    k1 = initial_kernel_tensor
    rows_dev = x0.shape[0]
    width = x0.shape[1]
    size = lax.axis_size("rows")
    cells_all = rows_dev * size * width
    near, far = 2, 6
    up = [(i, i + 1) for i in range(size - 1)]
    down = [(i + 1, i) for i in range(size - 1)]
    last = rows_dev - 1
    before = lax.ppermute(jnp.concatenate([x0[last:], x1[last:]], axis=0), "rows", up)
    after = lax.ppermute(jnp.concatenate([x0[:1], x1[:1]], axis=0), "rows", down)
    before_far = lax.ppermute(
        jnp.concatenate([x0[rows_dev - near:last], x1[rows_dev - far:last]], axis=0), "rows", up
    )
    after_far = lax.ppermute(jnp.concatenate([x0[1:near], x1[1:far]], axis=0), "rows", down)

    def row0(r):
        if r == -1:
            return (2, (0,))
        if r < -1:
            return (4, (near - 1 + r + 1,))
        if r == rows_dev:
            return (3, (0,))
        if r > rows_dev:
            return (5, (r - rows_dev - 1,))
        return (0, (0, r))

    def row1(r):
        if r == -1:
            return (2, (1,))
        if r < -1:
            return (4, (near - 1 + far + r,))
        if r == rows_dev:
            return (3, (1,))
        if r > rows_dev:
            return (5, (near - 1 + r - rows_dev - 1,))
        return (1, (r,))

    def rows_of(pick, lo, hi):
        return tuple(pick(r) for r in range(lo, hi))

    inputs = (specimen_pair_inputs, x1)
    nearby = (specimen_pair_inputs, x1, before, after)
    halos = (specimen_pair_inputs, x1, before, after, before_far, after_far)
    interior, inner_sums = conv_gather(inputs, (rows_of(row0, 0, rows_dev), rows_of(row1, 0, rows_dev)), k1, (False, False))
    boundary, edge_sums = conv_gather(
        nearby,
        (
            rows_of(row0, -1, 2),
            rows_of(row0, rows_dev - 2, rows_dev + 1),
            rows_of(row1, -1, 2),
            rows_of(row1, rows_dev - 2, rows_dev + 1),
        ),
        k1,
        (False, False, False, False),
    )
    per_slide = inner_sums + edge_sums[0::2] + edge_sums[1::2]
    stats = jnp.concatenate([per_slide[:, 0], per_slide[:, 1]], axis=0)
    stats, (edge0, edge1) = butterfly_sum(
        stats,
        "rows",
        [
            lambda: conv_gather(
                halos, (rows_of(row0, -near, 1), rows_of(row0, rows_dev - 1, rows_dev + near)), k1, (False, False)
            )[0],
            lambda: conv_gather(
                halos, (rows_of(row1, -far, 1), rows_of(row1, rows_dev - 1, rows_dev + far)), k1, (False, False)
            )[0],
        ],
    )
    average = stats[0:2] / cells_all
    variance = stats[2:4] / cells_all - average * average
    inv_scale = lax.rsqrt(variance + 1e-05)
    sources = (edge0, boundary, interior, edge1)
    plan0 = ((0, 0, 0), (1, 0, 0)) + tuple((2, 0, r) for r in range(rows_dev - 2)) + ((1, 1, 0), (0, 1, 0))
    halo = far - 1
    plan1 = (
        tuple((3, 0, r) for r in range(halo))
        + ((1, 2, 0),)
        + tuple((2, 1, r) for r in range(rows_dev - 2))
        + ((1, 3, 0),)
        + tuple((3, 1, r) for r in range(halo))
    )
    total = rows_dev * size
    first = lax.axis_index("rows") * rows_dev
    source = conv_hidden(
        sources, plan0, average[0], inv_scale[0], latter_kernel_tensor, (False,),
        latter_kernel_intercept, first - 1, total,
    )[0]
    target_reversed = conv_hidden(
        sources, plan1, average[1], inv_scale[1], latter_kernel_tensor, (True,),
        latter_kernel_intercept, first - halo, total, pad=(64, 8), dtype=jnp.float32, reverse=True,
    )[0]
    return correlation(
        source,
        target_reversed,
        patch_horizontal_shift,
        specimen_presence,
        softmax_sharpening,
    )


def solution(mesh):
    return jax.shard_map(
        local,
        mesh=mesh,
        in_specs=(
            P(None, ("pairs", "rows"), None, None),
            P(),
            P(),
            P(),
            P(("pairs", "rows"), None),
            P(("pairs", "rows"), None),
            P(("pairs", "rows"), None),
        ),
        out_specs=P(None, ("pairs", "rows"), None),
        check_vma=False,
    )
```

```python
import functools

import jax
import jax.numpy as jnp
from jax import lax
from jax.sharding import PartitionSpec as P
from jax.experimental import pallas as pl
from jax.experimental.pallas import tpu as pltpu

DISP = 81


def _corr_kernel(shift_ref, sharp_ref, pres_ref, f0_ref, frev_hbm, out_ref, win_ref, acc_ref, sems):
    rows = f0_ref.shape[0]
    half = f0_ref.shape[1] // 4
    copies = []
    for t in range(2):
        for q in range(2):
            start = 196 - 128 * t - half * q - shift_ref[0, t]
            cp = pltpu.make_async_copy(frev_hbm.at[:, pl.ds(start, 128), :], win_ref.at[2 * t + q],
                                       sems.at[2 * t + q])
            cp.start()
            copies.append(cp)
    lane = lax.broadcasted_iota(jnp.int32, (half, 128), 1)
    band = lane // 9
    li = lax.broadcasted_iota(jnp.int32, (128, 1), 0)
    valid = li < DISP
    row_d = jnp.where(valid, li // 9 - 4, 0).astype(jnp.float32)
    col_d = jnp.where(valid, 4 - li % 9, 0).astype(jnp.float32)
    for t in range(2):
        shift_t = shift_ref[0, t].astype(jnp.float32)
        scale = sharp_ref[0, t] / 128.0
        present = pres_ref[0, t].astype(jnp.float32)
        for q in range(2):
            cols = slice(128 * t + half * q, 128 * t + half * (q + 1))
            copies[2 * t + q].wait()
            acc_ref[...] = jnp.zeros_like(acc_ref)
            for hp in range(rows + 8):
                lo, hi = max(0, hp - 8), min(rows - 1, hp)
                lhs = f0_ref[lo:hi + 1, cols, :].reshape((hi - lo + 1) * half, 128)
                w = win_ref[2 * t + q, hp].astype(jnp.bfloat16)
                s = lax.dot_general(lhs, w, (((1,), (1,)), ((), ())), preferred_element_type=jnp.float32)
                for h in range(lo, hi + 1):
                    a = hp - h
                    blk = s[(h - lo) * half:(h - lo + 1) * half]
                    rolled = pltpu.roll(blk, 9 + 9 * a, 1, stride=1, stride_axis=0)
                    acc_ref[h] = jnp.where(band == a, rolled, acc_ref[h])
            for i in range(rows // 2):
                pair = acc_ref[2 * i:2 * i + 2].reshape(2 * half, 128)
                energy = jnp.transpose(pair) * scale
                energy = jnp.where(valid, energy, -jnp.inf)
                top = jnp.max(energy, axis=0, keepdims=True)
                p = jnp.exp(energy - top)
                inv = 1.0 / jnp.sum(p, axis=0, keepdims=True)
                fy = jnp.sum(p * row_d, axis=0, keepdims=True) * inv * present
                fx = (jnp.sum(p * col_d, axis=0, keepdims=True) * inv + shift_t) * present
                for k in range(2):
                    out_ref[0, 2 * i + k:2 * i + k + 1, cols] = fy[:, k * half:(k + 1) * half]
                    out_ref[1, 2 * i + k:2 * i + k + 1, cols] = fx[:, k * half:(k + 1) * half]


def correlation(f0, f1rev_ext, shift, presence, sharp):
    rows, width, depth = f0.shape
    frev = f1rev_ext
    return pl.pallas_call(
        _corr_kernel,
        out_shape=jax.ShapeDtypeStruct((2, rows, width), jnp.float32),
        in_specs=[pl.BlockSpec(memory_space=pltpu.SMEM)] * 3
        + [pl.BlockSpec(memory_space=pltpu.VMEM), pl.BlockSpec(memory_space=pl.ANY)],
        out_specs=pl.BlockSpec(memory_space=pltpu.VMEM),
        scratch_shapes=[
            pltpu.VMEM((4, rows + 8, 128, depth), jnp.float32),
            pltpu.VMEM((rows, 64, 128), jnp.float32),
            pltpu.SemaphoreType.DMA((4,)),
        ],
    )(shift, sharp, presence, f0, frev)


def extended(array, sides, width):
    for axis, dim in sides:
        size, length = (lax.axis_size(axis), array.shape[dim])
        up = [(i, (i + 1) % size) for i in range(size - 1)]
        down = [(j, i) for i, j in up]
        last = lax.slice_in_dim(array, length - width, length, axis=dim)
        initial = lax.slice_in_dim(array, 0, width, axis=dim)
        before = lax.ppermute(last, axis, up)
        after = lax.ppermute(initial, axis, down)
        array = jnp.concatenate([before, array, after], axis=dim)
    return array


def butterfly_sum(x, axis, fillers):
    size = lax.axis_size(axis)
    if size & (size - 1):
        return lax.psum(x, axis), [fill() for fill in fillers]
    done = []
    step = 1
    while step < size:
        moved = lax.ppermute(x, axis, [(i, i ^ step) for i in range(size)])
        if len(done) < len(fillers):
            value = fillers[len(done)]()
            x, value = lax.optimization_barrier((x + moved, value))
            done.append(value)
        else:
            x = x + moved
        step *= 2
    return x, done + [fill() for fill in fillers[len(done):]]


def _reverse_rows(value):
    tiles = value.shape[0] // 8
    v = value.reshape(tiles, 8, value.shape[1])
    v = jnp.concatenate([v[i:i + 1] for i in reversed(range(tiles))], axis=0)
    sub = lax.broadcasted_iota(jnp.int32, v.shape, 1)
    for step in (1, 2, 4):
        v = jnp.where((sub & step) != 0, pltpu.roll(v, step, 1), pltpu.roll(v, 8 - step, 1))
    return v.reshape(value.shape)


def _conv_kernel(*refs, finish, lead, trail, flips, plan, gather=None, reverse=False):
    sums_ref = None
    if gather:
        *sources, k_ref, o_ref, sums_ref, w_ref, x_ref = refs
        for n, rows in enumerate(gather):
            for r, (which, index) in enumerate(rows):
                x_ref[n, r] = sources[which][index].astype(x_ref.dtype)
    elif plan:
        where_ref, *sources, mean_ref, inv_ref, k_ref, bias_ref, o_ref, w_ref, x_ref = refs
        for r, (which, n, row) in enumerate(plan):
            value = jnp.maximum((sources[which][n, row] - mean_ref[...]) * inv_ref[...], 0.0)
            g = where_ref[2] + r
            keep = (g >= 0) & (g < where_ref[1])
            value = jnp.where(keep, value, 0.0)
            if reverse:
                value = _reverse_rows(value)
            x_ref[0, r] = value.astype(x_ref.dtype)
    elif finish:
        where_ref, x_ref, k_ref, bias_ref, o_ref, w_ref = refs
    else:
        x_ref, k_ref, o_ref, w_ref = refs
    count, rows_out, _, depth = o_ref.shape
    width = x_ref.shape[2]
    for n, flip in enumerate(flips):
        for dr in range(3):
            for dc in range(3):
                w_ref[n, dr * depth:(dr + 1) * depth, dc * depth:(dc + 1) * depth] = k_ref[
                    dr, 2 - dc if flip else dc
                ]
    if lead:
        o_ref[:, :, :lead] = jnp.zeros((count, rows_out, lead, depth), o_ref.dtype)
    if trail:
        o_ref[:, :, lead + width:] = jnp.zeros((count, rows_out, trail, depth), o_ref.dtype)
    chunk = 4 if rows_out % 4 == 0 else (2 if rows_out % 2 == 0 else 1)
    m = chunk * width
    flat = lax.broadcasted_iota(jnp.int32, (m, depth), 0)
    left = flat % width != 0
    right = flat % width != width - 1
    if len(set(flips)) == 1 and chunk < 4 and count > 1:
        cells = [(n, r) for n in range(count) for r in range(rows_out)]
        group = max(1, min(len(cells), 1024 // width))
        while len(cells) % group:
            group -= 1
        m = group * width
        flat = lax.broadcasted_iota(jnp.int32, (m, depth), 0)
        left = flat % width != 0
        right = flat % width != width - 1
        totals = {}
        for g0 in range(0, len(cells), group):
            part = cells[g0:g0 + group]
            lhs = jnp.concatenate(
                [jnp.concatenate([x_ref[n, r + dr] for n, r in part], axis=0) for dr in range(3)], axis=1
            )
            y = jnp.dot(lhs, w_ref[0], preferred_element_type=jnp.float32)
            out = (
                y[:, depth:2 * depth]
                + jnp.where(left, pltpu.roll(y[:, :depth], 1, 0), 0.0)
                + jnp.where(right, pltpu.roll(y[:, 2 * depth:], m - 1, 0), 0.0)
            )
            for k, (n, r) in enumerate(part):
                segment = out[k * width:(k + 1) * width]
                o_ref[n, r] = segment.astype(o_ref.dtype)
                if sums_ref is not None:
                    both = jnp.concatenate(
                        [jnp.sum(segment, axis=0, keepdims=True),
                         jnp.sum(segment * segment, axis=0, keepdims=True)], axis=0
                    )
                    totals[n] = both if n not in totals else totals[n] + both
        if sums_ref is not None:
            for n in range(count):
                sums_ref[n] = totals[n]
        return
    assert sums_ref is None
    for n in range(count):
        for r0 in range(0, rows_out, chunk):
            lhs = jnp.concatenate(
                [x_ref[n, r0 + dr:r0 + dr + chunk].reshape(m, depth) for dr in range(3)], axis=1
            )
            y = jnp.dot(lhs, w_ref[n], preferred_element_type=jnp.float32)
            out = (
                y[:, depth:2 * depth]
                + jnp.where(left, pltpu.roll(y[:, :depth], 1, 0), 0.0)
                + jnp.where(right, pltpu.roll(y[:, 2 * depth:], m - 1, 0), 0.0)
            )
            if finish:
                out = out + bias_ref[...]
                ms = jnp.mean(out * out, axis=1, keepdims=True)
                out = out * lax.rsqrt(ms + 1e-06)
                row = where_ref[0] + r0 + flat[:, 0:1] // width
                out = jnp.where((row >= 0) & (row < where_ref[1]), out, 0.0)
            o_ref[n, r0:r0 + chunk, lead:lead + width] = out.reshape(chunk, width, depth).astype(o_ref.dtype)


def conv_rows(field, kernel, flips, bias=None, first_row=None, total_rows=None, pad=(0, 0), dtype=jnp.bfloat16):
    count, rows_in, width, depth = field.shape
    vmem = pl.BlockSpec(memory_space=pltpu.VMEM)
    finish = bias is not None
    args = [field, kernel.astype(field.dtype)]
    specs = [vmem, vmem]
    if finish:
        where = jnp.stack([first_row, total_rows]).astype(jnp.int32)
        args = [where] + args + [bias.astype(jnp.float32).reshape(1, -1)]
        specs = [pl.BlockSpec(memory_space=pltpu.SMEM)] + specs + [vmem]
    return pl.pallas_call(
        functools.partial(_conv_kernel, finish=finish, lead=pad[0], trail=pad[1], flips=flips, plan=None),
        out_shape=jax.ShapeDtypeStruct(
            (count, rows_in - 2, pad[0] + width + pad[1], kernel.shape[3]), dtype if finish else jnp.float32
        ),
        in_specs=specs,
        out_specs=vmem,
        scratch_shapes=[pltpu.VMEM((count, 3 * depth, 3 * kernel.shape[3]), field.dtype)],
    )(*args)


def conv_gather(sources, gather, kernel, flips):
    count, rows_in = len(gather), len(gather[0])
    width, depth = sources[0].shape[-2], sources[0].shape[-1]
    vmem = pl.BlockSpec(memory_space=pltpu.VMEM)
    return pl.pallas_call(
        functools.partial(_conv_kernel, finish=False, lead=0, trail=0, flips=flips, plan=None, gather=gather),
        out_shape=(
            jax.ShapeDtypeStruct((count, rows_in - 2, width, kernel.shape[3]), jnp.float32),
            jax.ShapeDtypeStruct((count, 2, kernel.shape[3]), jnp.float32),
        ),
        in_specs=[vmem] * (len(sources) + 1),
        out_specs=(vmem, vmem),
        scratch_shapes=[
            pltpu.VMEM((count, 3 * depth, 3 * kernel.shape[3]), jnp.bfloat16),
            pltpu.VMEM((count, rows_in, width, depth), jnp.bfloat16),
        ],
    )(*sources, kernel.astype(jnp.bfloat16))


def conv_hidden(sources, plan, mean, inv_scale, kernel, flips, bias, first_in, total_rows, pad=(0, 0),
                dtype=jnp.bfloat16, reverse=False):
    rows_in = len(plan)
    width, depth = sources[0].shape[2], sources[0].shape[3]
    vmem = pl.BlockSpec(memory_space=pltpu.VMEM)
    where = jnp.stack([first_in + 1, total_rows, first_in]).astype(jnp.int32)
    args = [where, *sources, mean.reshape(1, -1), inv_scale.reshape(1, -1),
            kernel.astype(jnp.bfloat16), bias.astype(jnp.float32).reshape(1, -1)]
    specs = [pl.BlockSpec(memory_space=pltpu.SMEM)] + [vmem] * (len(sources) + 4)
    return pl.pallas_call(
        functools.partial(
            _conv_kernel, finish=True, lead=pad[0], trail=pad[1], flips=flips, plan=plan, reverse=reverse
        ),
        out_shape=jax.ShapeDtypeStruct((1, rows_in - 2, pad[0] + width + pad[1], kernel.shape[3]), dtype),
        in_specs=specs,
        out_specs=vmem,
        scratch_shapes=[
            pltpu.VMEM((1, 3 * depth, 3 * kernel.shape[3]), jnp.bfloat16),
            pltpu.VMEM((1, rows_in, width, depth), jnp.bfloat16),
        ],
    )(*args)


def finish_features(second_out, latter_kernel_intercept):
    shifted = second_out + latter_kernel_intercept
    return (
        shifted * lax.rsqrt(jnp.mean(shifted * shifted, axis=-1, keepdims=True) + 1e-06)
    ).astype(jnp.bfloat16)


def in_map(rows_from, count, rows_dev):
    total = rows_dev * lax.axis_size("rows")
    first = lax.axis_index("rows") * rows_dev + rows_from
    row = first + lax.broadcasted_iota(jnp.int32, (count, 1, 1), 0)
    return (row >= 0) & (row < total)


def local(
    specimen_pair_inputs,
    initial_kernel_tensor,
    latter_kernel_tensor,
    latter_kernel_intercept,
    patch_horizontal_shift,
    specimen_presence,
    softmax_sharpening,
):
    x0 = specimen_pair_inputs[0]
    x1 = specimen_pair_inputs[1]
    k1 = initial_kernel_tensor
    rows_dev = x0.shape[0]
    width = x0.shape[1]
    size = lax.axis_size("rows")
    cells_all = rows_dev * size * width
    near, far = 2, 6
    up = [(i, i + 1) for i in range(size - 1)]
    down = [(i + 1, i) for i in range(size - 1)]
    before = lax.ppermute(
        jnp.concatenate([x0[rows_dev - near:], x1[rows_dev - far:]], axis=0), "rows", up
    )
    after = lax.ppermute(
        jnp.concatenate([x0[:near], x1[:far]], axis=0), "rows", down
    )

    def row0(r):
        if r < 0:
            return (1, (near + r,))
        if r >= rows_dev:
            return (2, (r - rows_dev,))
        return (0, (0, r))

    def row1(r):
        if r < 0:
            return (1, (near + far + r,))
        if r >= rows_dev:
            return (2, (near + r - rows_dev,))
        return (0, (1, r))

    def rows_of(pick, lo, hi):
        return tuple(pick(r) for r in range(lo, hi))

    inputs = (specimen_pair_inputs,)
    halos = (specimen_pair_inputs, before, after)
    interior, inner_sums = conv_gather(inputs, (rows_of(row0, 0, rows_dev), rows_of(row1, 0, rows_dev)), k1, (False, False))
    boundary, edge_sums = conv_gather(
        halos,
        (
            rows_of(row0, -1, 2),
            rows_of(row0, rows_dev - 2, rows_dev + 1),
            rows_of(row1, -1, 2),
            rows_of(row1, rows_dev - 2, rows_dev + 1),
        ),
        k1,
        (False, False, False, False),
    )
    per_slide = inner_sums + edge_sums[0::2] + edge_sums[1::2]
    stats = jnp.concatenate([per_slide[:, 0], per_slide[:, 1]], axis=0)
    stats, (edge0, edge1) = butterfly_sum(
        stats,
        "rows",
        [
            lambda: conv_gather(
                halos, (rows_of(row0, -near, 1), rows_of(row0, rows_dev - 1, rows_dev + near)), k1, (False, False)
            )[0],
            lambda: conv_gather(
                halos, (rows_of(row1, -far, 1), rows_of(row1, rows_dev - 1, rows_dev + far)), k1, (False, False)
            )[0],
        ],
    )
    average = stats[0:2] / cells_all
    variance = stats[2:4] / cells_all - average * average
    inv_scale = lax.rsqrt(variance + 1e-05)
    sources = (edge0, boundary, interior, edge1)
    plan0 = ((0, 0, 0), (1, 0, 0)) + tuple((2, 0, r) for r in range(rows_dev - 2)) + ((1, 1, 0), (0, 1, 0))
    halo = far - 1
    plan1 = (
        tuple((2, 0, r) for r in range(halo))
        + ((0, 2, 0),)
        + tuple((1, 1, r) for r in range(rows_dev - 2))
        + ((0, 3, 0),)
        + tuple((2, 1, r) for r in range(halo))
    )
    total = rows_dev * size
    first = lax.axis_index("rows") * rows_dev
    source = conv_hidden(
        sources[:3], plan0, average[0], inv_scale[0], latter_kernel_tensor, (False,),
        latter_kernel_intercept, first - 1, total,
    )[0]
    target_reversed = conv_hidden(
        sources[1:], plan1, average[1], inv_scale[1], latter_kernel_tensor, (True,),
        latter_kernel_intercept, first - halo, total, pad=(64, 8), dtype=jnp.float32, reverse=True,
    )[0]
    return correlation(
        source,
        target_reversed,
        patch_horizontal_shift,
        specimen_presence,
        softmax_sharpening,
    )


def solution(mesh):
    return jax.shard_map(
        local,
        mesh=mesh,
        in_specs=(
            P(None, ("pairs", "rows"), None, None),
            P(),
            P(),
            P(),
            P(("pairs", "rows"), None),
            P(("pairs", "rows"), None),
            P(("pairs", "rows"), None),
        ),
        out_specs=P(None, ("pairs", "rows"), None),
        check_vma=False,
    )
```

```python
import functools

import jax
import jax.numpy as jnp
from jax import lax
from jax.sharding import PartitionSpec as P
from jax.experimental import pallas as pl
from jax.experimental.pallas import tpu as pltpu

DISP = 81


def _corr_kernel(shift_ref, sharp_ref, pres_ref, f0_ref, frev_hbm, out_ref, win_ref, acc_ref, sems):
    rows = f0_ref.shape[0]
    half = f0_ref.shape[1] // 4
    copies = []
    for t in range(2):
        for q in range(2):
            start = 196 - 128 * t - half * q - shift_ref[0, t]
            cp = pltpu.make_async_copy(frev_hbm.at[:, pl.ds(start, 128), :], win_ref.at[2 * t + q],
                                       sems.at[2 * t + q])
            cp.start()
            copies.append(cp)
    lane = lax.broadcasted_iota(jnp.int32, (half, 128), 1)
    band = lane // 9
    li = lax.broadcasted_iota(jnp.int32, (128, 1), 0)
    valid = li < DISP
    row_d = jnp.where(valid, li // 9 - 4, 0).astype(jnp.float32)
    col_d = jnp.where(valid, 4 - li % 9, 0).astype(jnp.float32)
    for t in range(2):
        shift_t = shift_ref[0, t].astype(jnp.float32)
        scale = sharp_ref[0, t] / 128.0
        present = pres_ref[0, t].astype(jnp.float32)
        for q in range(2):
            cols = slice(128 * t + half * q, 128 * t + half * (q + 1))
            copies[2 * t + q].wait()
            acc_ref[...] = jnp.zeros_like(acc_ref)
            for hp in range(rows + 8):
                lo, hi = max(0, hp - 8), min(rows - 1, hp)
                lhs = f0_ref[lo:hi + 1, cols, :].reshape((hi - lo + 1) * half, 128)
                w = win_ref[2 * t + q, hp].astype(jnp.bfloat16)
                s = lax.dot_general(lhs, w, (((1,), (1,)), ((), ())), preferred_element_type=jnp.float32)
                for h in range(lo, hi + 1):
                    a = hp - h
                    blk = s[(h - lo) * half:(h - lo + 1) * half]
                    rolled = pltpu.roll(blk, 9 + 9 * a, 1, stride=1, stride_axis=0)
                    acc_ref[h] = jnp.where(band == a, rolled, acc_ref[h])
            for i in range(rows // 2):
                pair = acc_ref[2 * i:2 * i + 2].reshape(2 * half, 128)
                energy = jnp.transpose(pair) * scale
                energy = jnp.where(valid, energy, -jnp.inf)
                top = jnp.max(energy, axis=0, keepdims=True)
                p = jnp.exp(energy - top)
                inv = 1.0 / jnp.sum(p, axis=0, keepdims=True)
                fy = jnp.sum(p * row_d, axis=0, keepdims=True) * inv * present
                fx = (jnp.sum(p * col_d, axis=0, keepdims=True) * inv + shift_t) * present
                for k in range(2):
                    out_ref[0, 2 * i + k:2 * i + k + 1, cols] = fy[:, k * half:(k + 1) * half]
                    out_ref[1, 2 * i + k:2 * i + k + 1, cols] = fx[:, k * half:(k + 1) * half]


def correlation(f0, f1rev_ext, shift, presence, sharp):
    rows, width, depth = f0.shape
    frev = f1rev_ext
    return pl.pallas_call(
        _corr_kernel,
        out_shape=jax.ShapeDtypeStruct((2, rows, width), jnp.float32),
        in_specs=[pl.BlockSpec(memory_space=pltpu.SMEM)] * 3
        + [pl.BlockSpec(memory_space=pltpu.VMEM), pl.BlockSpec(memory_space=pl.ANY)],
        out_specs=pl.BlockSpec(memory_space=pltpu.VMEM),
        scratch_shapes=[
            pltpu.VMEM((4, rows + 8, 128, depth), jnp.float32),
            pltpu.VMEM((rows, 64, 128), jnp.float32),
            pltpu.SemaphoreType.DMA((4,)),
        ],
    )(shift, sharp, presence, f0, frev)


def extended(array, sides, width):
    for axis, dim in sides:
        size, length = (lax.axis_size(axis), array.shape[dim])
        up = [(i, (i + 1) % size) for i in range(size - 1)]
        down = [(j, i) for i, j in up]
        last = lax.slice_in_dim(array, length - width, length, axis=dim)
        initial = lax.slice_in_dim(array, 0, width, axis=dim)
        before = lax.ppermute(last, axis, up)
        after = lax.ppermute(initial, axis, down)
        array = jnp.concatenate([before, array, after], axis=dim)
    return array


def butterfly_sum(x, axis, fillers):
    size = lax.axis_size(axis)
    if size & (size - 1):
        return lax.psum(x, axis), [fill() for fill in fillers]
    done = []
    step = 1
    while step < size:
        moved = lax.ppermute(x, axis, [(i, i ^ step) for i in range(size)])
        if len(done) < len(fillers):
            value = fillers[len(done)]()
            x, value = lax.optimization_barrier((x + moved, value))
            done.append(value)
        else:
            x = x + moved
        step *= 2
    return x, done + [fill() for fill in fillers[len(done):]]


def _reverse_rows(value):
    tiles = value.shape[0] // 8
    v = value.reshape(tiles, 8, value.shape[1])
    v = jnp.concatenate([v[i:i + 1] for i in reversed(range(tiles))], axis=0)
    sub = lax.broadcasted_iota(jnp.int32, v.shape, 1)
    for step in (1, 2, 4):
        v = jnp.where((sub & step) != 0, pltpu.roll(v, step, 1), pltpu.roll(v, 8 - step, 1))
    return v.reshape(value.shape)


def _conv_kernel(*refs, finish, lead, trail, flips, plan, gather=None, reverse=False):
    sums_ref = None
    if gather:
        *sources, k_ref, o_ref, sums_ref, w_ref, x_ref = refs
        for n, rows in enumerate(gather):
            for r, (which, index) in enumerate(rows):
                x_ref[n, r] = sources[which][index].astype(x_ref.dtype)
    elif plan:
        where_ref, *sources, mean_ref, inv_ref, k_ref, bias_ref, o_ref, w_ref, x_ref = refs
        for r, (which, n, row) in enumerate(plan):
            value = jnp.maximum((sources[which][n, row] - mean_ref[...]) * inv_ref[...], 0.0)
            g = where_ref[2] + r
            keep = (g >= 0) & (g < where_ref[1])
            value = jnp.where(keep, value, 0.0)
            if reverse:
                value = _reverse_rows(value)
            x_ref[0, r] = value.astype(x_ref.dtype)
    elif finish:
        where_ref, x_ref, k_ref, bias_ref, o_ref, w_ref = refs
    else:
        x_ref, k_ref, o_ref, w_ref = refs
    count, rows_out, _, depth = o_ref.shape
    width = x_ref.shape[2]
    for n, flip in enumerate(flips):
        for dr in range(3):
            for dc in range(3):
                w_ref[n, dr * depth:(dr + 1) * depth, dc * depth:(dc + 1) * depth] = k_ref[
                    dr, 2 - dc if flip else dc
                ]
    if lead:
        o_ref[:, :, :lead] = jnp.zeros((count, rows_out, lead, depth), o_ref.dtype)
    if trail:
        o_ref[:, :, lead + width:] = jnp.zeros((count, rows_out, trail, depth), o_ref.dtype)
    chunk = 4 if rows_out % 4 == 0 else (2 if rows_out % 2 == 0 else 1)
    m = chunk * width
    flat = lax.broadcasted_iota(jnp.int32, (m, depth), 0)
    left = flat % width != 0
    right = flat % width != width - 1
    if len(set(flips)) == 1 and chunk < 4:
        cells = [(n, r) for n in range(count) for r in range(rows_out)]
        group = max(1, min(len(cells), 1024 // width))
        while len(cells) % group:
            group -= 1
        m = group * width
        flat = lax.broadcasted_iota(jnp.int32, (m, depth), 0)
        left = flat % width != 0
        right = flat % width != width - 1
        totals = {}
        for g0 in range(0, len(cells), group):
            part = cells[g0:g0 + group]
            lhs = jnp.concatenate(
                [jnp.concatenate([x_ref[n, r + dr] for n, r in part], axis=0) for dr in range(3)], axis=1
            )
            y = jnp.dot(lhs, w_ref[0], preferred_element_type=jnp.float32)
            out = (
                y[:, depth:2 * depth]
                + jnp.where(left, pltpu.roll(y[:, :depth], 1, 0), 0.0)
                + jnp.where(right, pltpu.roll(y[:, 2 * depth:], m - 1, 0), 0.0)
            )
            for k, (n, r) in enumerate(part):
                segment = out[k * width:(k + 1) * width]
                o_ref[n, r] = segment.astype(o_ref.dtype)
                if sums_ref is not None:
                    both = jnp.concatenate(
                        [jnp.sum(segment, axis=0, keepdims=True),
                         jnp.sum(segment * segment, axis=0, keepdims=True)], axis=0
                    )
                    totals[n] = both if n not in totals else totals[n] + both
        if sums_ref is not None:
            for n in range(count):
                sums_ref[n] = totals[n]
        return
    assert sums_ref is None
    for n in range(count):
        for r0 in range(0, rows_out, chunk):
            lhs = jnp.concatenate(
                [x_ref[n, r0 + dr:r0 + dr + chunk].reshape(m, depth) for dr in range(3)], axis=1
            )
            y = jnp.dot(lhs, w_ref[n], preferred_element_type=jnp.float32)
            out = (
                y[:, depth:2 * depth]
                + jnp.where(left, pltpu.roll(y[:, :depth], 1, 0), 0.0)
                + jnp.where(right, pltpu.roll(y[:, 2 * depth:], m - 1, 0), 0.0)
            )
            if finish:
                out = out + bias_ref[...]
                ms = jnp.mean(out * out, axis=1, keepdims=True)
                out = out * lax.rsqrt(ms + 1e-06)
                row = where_ref[0] + r0 + flat[:, 0:1] // width
                out = jnp.where((row >= 0) & (row < where_ref[1]), out, 0.0)
            o_ref[n, r0:r0 + chunk, lead:lead + width] = out.reshape(chunk, width, depth).astype(o_ref.dtype)


def conv_rows(field, kernel, flips, bias=None, first_row=None, total_rows=None, pad=(0, 0), dtype=jnp.bfloat16):
    count, rows_in, width, depth = field.shape
    vmem = pl.BlockSpec(memory_space=pltpu.VMEM)
    finish = bias is not None
    args = [field, kernel.astype(field.dtype)]
    specs = [vmem, vmem]
    if finish:
        where = jnp.stack([first_row, total_rows]).astype(jnp.int32)
        args = [where] + args + [bias.astype(jnp.float32).reshape(1, -1)]
        specs = [pl.BlockSpec(memory_space=pltpu.SMEM)] + specs + [vmem]
    return pl.pallas_call(
        functools.partial(_conv_kernel, finish=finish, lead=pad[0], trail=pad[1], flips=flips, plan=None),
        out_shape=jax.ShapeDtypeStruct(
            (count, rows_in - 2, pad[0] + width + pad[1], kernel.shape[3]), dtype if finish else jnp.float32
        ),
        in_specs=specs,
        out_specs=vmem,
        scratch_shapes=[pltpu.VMEM((count, 3 * depth, 3 * kernel.shape[3]), field.dtype)],
    )(*args)


def conv_gather(sources, gather, kernel, flips):
    count, rows_in = len(gather), len(gather[0])
    width, depth = sources[0].shape[-2], sources[0].shape[-1]
    vmem = pl.BlockSpec(memory_space=pltpu.VMEM)
    return pl.pallas_call(
        functools.partial(_conv_kernel, finish=False, lead=0, trail=0, flips=flips, plan=None, gather=gather),
        out_shape=(
            jax.ShapeDtypeStruct((count, rows_in - 2, width, kernel.shape[3]), jnp.float32),
            jax.ShapeDtypeStruct((count, 2, kernel.shape[3]), jnp.float32),
        ),
        in_specs=[vmem] * (len(sources) + 1),
        out_specs=(vmem, vmem),
        scratch_shapes=[
            pltpu.VMEM((count, 3 * depth, 3 * kernel.shape[3]), jnp.bfloat16),
            pltpu.VMEM((count, rows_in, width, depth), jnp.bfloat16),
        ],
    )(*sources, kernel.astype(jnp.bfloat16))


def conv_hidden(sources, plan, mean, inv_scale, kernel, flips, bias, first_in, total_rows, pad=(0, 0),
                dtype=jnp.bfloat16, reverse=False):
    rows_in = len(plan)
    width, depth = sources[0].shape[2], sources[0].shape[3]
    vmem = pl.BlockSpec(memory_space=pltpu.VMEM)
    where = jnp.stack([first_in + 1, total_rows, first_in]).astype(jnp.int32)
    args = [where, *sources, mean.reshape(1, -1), inv_scale.reshape(1, -1),
            kernel.astype(jnp.bfloat16), bias.astype(jnp.float32).reshape(1, -1)]
    specs = [pl.BlockSpec(memory_space=pltpu.SMEM)] + [vmem] * (len(sources) + 4)
    return pl.pallas_call(
        functools.partial(
            _conv_kernel, finish=True, lead=pad[0], trail=pad[1], flips=flips, plan=plan, reverse=reverse
        ),
        out_shape=jax.ShapeDtypeStruct((1, rows_in - 2, pad[0] + width + pad[1], kernel.shape[3]), dtype),
        in_specs=specs,
        out_specs=vmem,
        scratch_shapes=[
            pltpu.VMEM((1, 3 * depth, 3 * kernel.shape[3]), jnp.bfloat16),
            pltpu.VMEM((1, rows_in, width, depth), jnp.bfloat16),
        ],
    )(*args)


def finish_features(second_out, latter_kernel_intercept):
    shifted = second_out + latter_kernel_intercept
    return (
        shifted * lax.rsqrt(jnp.mean(shifted * shifted, axis=-1, keepdims=True) + 1e-06)
    ).astype(jnp.bfloat16)


def in_map(rows_from, count, rows_dev):
    total = rows_dev * lax.axis_size("rows")
    first = lax.axis_index("rows") * rows_dev + rows_from
    row = first + lax.broadcasted_iota(jnp.int32, (count, 1, 1), 0)
    return (row >= 0) & (row < total)


def local(
    specimen_pair_inputs,
    initial_kernel_tensor,
    latter_kernel_tensor,
    latter_kernel_intercept,
    patch_horizontal_shift,
    specimen_presence,
    softmax_sharpening,
):
    x0 = specimen_pair_inputs[0]
    x1 = specimen_pair_inputs[1]
    k1 = initial_kernel_tensor
    rows_dev = x0.shape[0]
    width = x0.shape[1]
    size = lax.axis_size("rows")
    cells_all = rows_dev * size * width
    near, far = 2, 6
    up = [(i, i + 1) for i in range(size - 1)]
    down = [(i + 1, i) for i in range(size - 1)]
    before = lax.ppermute(
        jnp.concatenate([x0[rows_dev - near:], x1[rows_dev - far:]], axis=0), "rows", up
    )
    after = lax.ppermute(
        jnp.concatenate([x0[:near], x1[:far]], axis=0), "rows", down
    )

    def row0(r):
        if r < 0:
            return (1, (near + r,))
        if r >= rows_dev:
            return (2, (r - rows_dev,))
        return (0, (0, r))

    def row1(r):
        if r < 0:
            return (1, (near + far + r,))
        if r >= rows_dev:
            return (2, (near + r - rows_dev,))
        return (0, (1, r))

    def rows_of(pick, lo, hi):
        return tuple(pick(r) for r in range(lo, hi))

    inputs = (specimen_pair_inputs,)
    halos = (specimen_pair_inputs, before, after)
    interior0, sums0 = conv_gather(inputs, (rows_of(row0, 0, rows_dev),), k1, (False,))
    interior1, sums1 = conv_gather(inputs, (rows_of(row1, 0, rows_dev),), k1, (False,))
    inner_sums = jnp.concatenate([sums0, sums1], axis=0)
    boundary, edge_sums = conv_gather(
        halos,
        (
            rows_of(row0, -1, 2),
            rows_of(row0, rows_dev - 2, rows_dev + 1),
            rows_of(row1, -1, 2),
            rows_of(row1, rows_dev - 2, rows_dev + 1),
        ),
        k1,
        (False, False, False, False),
    )
    per_slide = inner_sums + edge_sums[0::2] + edge_sums[1::2]
    stats = jnp.concatenate([per_slide[:, 0], per_slide[:, 1]], axis=0)
    stats, (edge0, edge1) = butterfly_sum(
        stats,
        "rows",
        [
            lambda: conv_gather(
                halos, (rows_of(row0, -near, 1), rows_of(row0, rows_dev - 1, rows_dev + near)), k1, (False, False)
            )[0],
            lambda: conv_gather(
                halos, (rows_of(row1, -far, 1), rows_of(row1, rows_dev - 1, rows_dev + far)), k1, (False, False)
            )[0],
        ],
    )
    average = stats[0:2] / cells_all
    variance = stats[2:4] / cells_all - average * average
    inv_scale = lax.rsqrt(variance + 1e-05)
    sources = (edge0, boundary, interior0, interior1, edge1)
    plan0 = ((0, 0, 0), (1, 0, 0)) + tuple((2, 0, r) for r in range(rows_dev - 2)) + ((1, 1, 0), (0, 1, 0))
    halo = far - 1
    plan1 = (
        tuple((2, 0, r) for r in range(halo))
        + ((0, 2, 0),)
        + tuple((1, 0, r) for r in range(rows_dev - 2))
        + ((0, 3, 0),)
        + tuple((2, 1, r) for r in range(halo))
    )
    total = rows_dev * size
    first = lax.axis_index("rows") * rows_dev
    source = conv_hidden(
        sources[:3], plan0, average[0], inv_scale[0], latter_kernel_tensor, (False,),
        latter_kernel_intercept, first - 1, total,
    )[0]
    target_reversed = conv_hidden(
        sources[1:2] + sources[3:], plan1, average[1], inv_scale[1], latter_kernel_tensor, (True,),
        latter_kernel_intercept, first - halo, total, pad=(64, 8), dtype=jnp.float32, reverse=True,
    )[0]
    return correlation(
        source,
        target_reversed,
        patch_horizontal_shift,
        specimen_presence,
        softmax_sharpening,
    )


def solution(mesh):
    return jax.shard_map(
        local,
        mesh=mesh,
        in_specs=(
            P(None, ("pairs", "rows"), None, None),
            P(),
            P(),
            P(),
            P(("pairs", "rows"), None),
            P(("pairs", "rows"), None),
            P(("pairs", "rows"), None),
        ),
        out_specs=P(None, ("pairs", "rows"), None),
        check_vma=False,
    )
```

```python
import functools

import jax
import jax.numpy as jnp
from jax import lax
from jax.sharding import PartitionSpec as P
from jax.experimental import pallas as pl
from jax.experimental.pallas import tpu as pltpu

DISP = 81


def _corr_kernel(shift_ref, sharp_ref, pres_ref, f0_ref, frev_hbm, out_ref, win_ref, acc_ref, sems):
    rows = f0_ref.shape[0]
    half = f0_ref.shape[1] // 4
    copies = []
    for t in range(2):
        for q in range(2):
            start = 196 - 128 * t - half * q - shift_ref[0, t]
            cp = pltpu.make_async_copy(frev_hbm.at[:, pl.ds(start, 128), :], win_ref.at[2 * t + q],
                                       sems.at[2 * t + q])
            cp.start()
            copies.append(cp)
    lane = lax.broadcasted_iota(jnp.int32, (half, 128), 1)
    band = lane // 9
    li = lax.broadcasted_iota(jnp.int32, (128, 1), 0)
    valid = li < DISP
    row_d = jnp.where(valid, li // 9 - 4, 0).astype(jnp.float32)
    col_d = jnp.where(valid, 4 - li % 9, 0).astype(jnp.float32)
    for t in range(2):
        shift_t = shift_ref[0, t].astype(jnp.float32)
        scale = sharp_ref[0, t] / 128.0
        present = pres_ref[0, t].astype(jnp.float32)
        for q in range(2):
            cols = slice(128 * t + half * q, 128 * t + half * (q + 1))
            copies[2 * t + q].wait()
            acc_ref[...] = jnp.zeros_like(acc_ref)
            for hp in range(rows + 8):
                lo, hi = max(0, hp - 8), min(rows - 1, hp)
                lhs = f0_ref[lo:hi + 1, cols, :].reshape((hi - lo + 1) * half, 128)
                w = win_ref[2 * t + q, hp].astype(jnp.bfloat16)
                s = lax.dot_general(lhs, w, (((1,), (1,)), ((), ())), preferred_element_type=jnp.float32)
                for h in range(lo, hi + 1):
                    a = hp - h
                    blk = s[(h - lo) * half:(h - lo + 1) * half]
                    rolled = pltpu.roll(blk, 9 + 9 * a, 1, stride=1, stride_axis=0)
                    acc_ref[h] = jnp.where(band == a, rolled, acc_ref[h])
            for i in range(rows // 2):
                pair = acc_ref[2 * i:2 * i + 2].reshape(2 * half, 128)
                energy = jnp.transpose(pair) * scale
                energy = jnp.where(valid, energy, -jnp.inf)
                top = jnp.max(energy, axis=0, keepdims=True)
                p = jnp.exp(energy - top)
                inv = 1.0 / jnp.sum(p, axis=0, keepdims=True)
                fy = jnp.sum(p * row_d, axis=0, keepdims=True) * inv * present
                fx = (jnp.sum(p * col_d, axis=0, keepdims=True) * inv + shift_t) * present
                for k in range(2):
                    out_ref[0, 2 * i + k:2 * i + k + 1, cols] = fy[:, k * half:(k + 1) * half]
                    out_ref[1, 2 * i + k:2 * i + k + 1, cols] = fx[:, k * half:(k + 1) * half]


def correlation(f0, f1rev_ext, shift, presence, sharp):
    rows, width, depth = f0.shape
    frev = f1rev_ext
    return pl.pallas_call(
        _corr_kernel,
        out_shape=jax.ShapeDtypeStruct((2, rows, width), jnp.float32),
        in_specs=[pl.BlockSpec(memory_space=pltpu.SMEM)] * 3
        + [pl.BlockSpec(memory_space=pltpu.VMEM), pl.BlockSpec(memory_space=pl.ANY)],
        out_specs=pl.BlockSpec(memory_space=pltpu.VMEM),
        scratch_shapes=[
            pltpu.VMEM((4, rows + 8, 128, depth), jnp.float32),
            pltpu.VMEM((rows, 64, 128), jnp.float32),
            pltpu.SemaphoreType.DMA((4,)),
        ],
    )(shift, sharp, presence, f0, frev)


def extended(array, sides, width):
    for axis, dim in sides:
        size, length = (lax.axis_size(axis), array.shape[dim])
        up = [(i, (i + 1) % size) for i in range(size - 1)]
        down = [(j, i) for i, j in up]
        last = lax.slice_in_dim(array, length - width, length, axis=dim)
        initial = lax.slice_in_dim(array, 0, width, axis=dim)
        before = lax.ppermute(last, axis, up)
        after = lax.ppermute(initial, axis, down)
        array = jnp.concatenate([before, array, after], axis=dim)
    return array


def butterfly_sum(x, axis, fillers):
    size = lax.axis_size(axis)
    if size & (size - 1):
        return lax.psum(x, axis), [fill() for fill in fillers]
    done = []
    step = 1
    while step < size:
        moved = lax.ppermute(x, axis, [(i, i ^ step) for i in range(size)])
        if len(done) < len(fillers):
            value = fillers[len(done)]()
            x, value = lax.optimization_barrier((x + moved, value))
            done.append(value)
        else:
            x = x + moved
        step *= 2
    return x, done + [fill() for fill in fillers[len(done):]]


def _reverse_rows(value):
    tiles = value.shape[0] // 8
    v = value.reshape(tiles, 8, value.shape[1])
    v = jnp.concatenate([v[i:i + 1] for i in reversed(range(tiles))], axis=0)
    sub = lax.broadcasted_iota(jnp.int32, v.shape, 1)
    for step in (1, 2, 4):
        v = jnp.where((sub & step) != 0, pltpu.roll(v, step, 1), pltpu.roll(v, 8 - step, 1))
    return v.reshape(value.shape)


def _conv_kernel(*refs, finish, lead, trail, flips, plan, gather=None, reverse=False):
    sums_ref = None
    if gather:
        *sources, k_ref, o_ref, sums_ref, w_ref, x_ref = refs
        for n, rows in enumerate(gather):
            for r, (which, index) in enumerate(rows):
                x_ref[n, r] = sources[which][index].astype(x_ref.dtype)
    elif plan:
        where_ref, *sources, mean_ref, inv_ref, k_ref, bias_ref, o_ref, w_ref, x_ref = refs
        for r, (which, n, row) in enumerate(plan):
            value = jnp.maximum((sources[which][n, row] - mean_ref[...]) * inv_ref[...], 0.0)
            g = where_ref[2] + r
            keep = (g >= 0) & (g < where_ref[1])
            value = jnp.where(keep, value, 0.0)
            if reverse:
                value = _reverse_rows(value)
            x_ref[0, r] = value.astype(x_ref.dtype)
    elif finish:
        where_ref, x_ref, k_ref, bias_ref, o_ref, w_ref = refs
    else:
        x_ref, k_ref, o_ref, w_ref = refs
    count, rows_out, _, depth = o_ref.shape
    width = x_ref.shape[2]
    for n, flip in enumerate(flips):
        for dr in range(3):
            for dc in range(3):
                w_ref[n, dr * depth:(dr + 1) * depth, dc * depth:(dc + 1) * depth] = k_ref[
                    dr, 2 - dc if flip else dc
                ]
    if lead:
        o_ref[:, :, :lead] = jnp.zeros((count, rows_out, lead, depth), o_ref.dtype)
    if trail:
        o_ref[:, :, lead + width:] = jnp.zeros((count, rows_out, trail, depth), o_ref.dtype)
    chunk = 4 if rows_out % 4 == 0 else (2 if rows_out % 2 == 0 else 1)
    m = chunk * width
    flat = lax.broadcasted_iota(jnp.int32, (m, depth), 0)
    left = flat % width != 0
    right = flat % width != width - 1
    if len(set(flips)) == 1 and chunk < 4 and count > 1:
        cells = [(n, r) for n in range(count) for r in range(rows_out)]
        group = max(1, min(len(cells), 1024 // width))
        while len(cells) % group:
            group -= 1
        m = group * width
        flat = lax.broadcasted_iota(jnp.int32, (m, depth), 0)
        left = flat % width != 0
        right = flat % width != width - 1
        totals = {}
        for g0 in range(0, len(cells), group):
            part = cells[g0:g0 + group]
            lhs = jnp.concatenate(
                [jnp.concatenate([x_ref[n, r + dr] for n, r in part], axis=0) for dr in range(3)], axis=1
            )
            y = jnp.dot(lhs, w_ref[0], preferred_element_type=jnp.float32)
            out = (
                y[:, depth:2 * depth]
                + jnp.where(left, pltpu.roll(y[:, :depth], 1, 0), 0.0)
                + jnp.where(right, pltpu.roll(y[:, 2 * depth:], m - 1, 0), 0.0)
            )
            for k, (n, r) in enumerate(part):
                segment = out[k * width:(k + 1) * width]
                o_ref[n, r] = segment.astype(o_ref.dtype)
                if sums_ref is not None:
                    both = jnp.concatenate(
                        [jnp.sum(segment, axis=0, keepdims=True),
                         jnp.sum(segment * segment, axis=0, keepdims=True)], axis=0
                    )
                    totals[n] = both if n not in totals else totals[n] + both
        if sums_ref is not None:
            for n in range(count):
                sums_ref[n] = totals[n]
        return
    assert sums_ref is None
    for n in range(count):
        for r0 in range(0, rows_out, chunk):
            lhs = jnp.concatenate(
                [x_ref[n, r0 + dr:r0 + dr + chunk].reshape(m, depth) for dr in range(3)], axis=1
            )
            y = jnp.dot(lhs, w_ref[n], preferred_element_type=jnp.float32)
            out = (
                y[:, depth:2 * depth]
                + jnp.where(left, pltpu.roll(y[:, :depth], 1, 0), 0.0)
                + jnp.where(right, pltpu.roll(y[:, 2 * depth:], m - 1, 0), 0.0)
            )
            if finish:
                out = out + bias_ref[...]
                ms = jnp.mean(out * out, axis=1, keepdims=True)
                out = out * lax.rsqrt(ms + 1e-06)
                row = where_ref[0] + r0 + flat[:, 0:1] // width
                out = jnp.where((row >= 0) & (row < where_ref[1]), out, 0.0)
            o_ref[n, r0:r0 + chunk, lead:lead + width] = out.reshape(chunk, width, depth).astype(o_ref.dtype)


def conv_rows(field, kernel, flips, bias=None, first_row=None, total_rows=None, pad=(0, 0), dtype=jnp.bfloat16):
    count, rows_in, width, depth = field.shape
    vmem = pl.BlockSpec(memory_space=pltpu.VMEM)
    finish = bias is not None
    args = [field, kernel.astype(field.dtype)]
    specs = [vmem, vmem]
    if finish:
        where = jnp.stack([first_row, total_rows]).astype(jnp.int32)
        args = [where] + args + [bias.astype(jnp.float32).reshape(1, -1)]
        specs = [pl.BlockSpec(memory_space=pltpu.SMEM)] + specs + [vmem]
    return pl.pallas_call(
        functools.partial(_conv_kernel, finish=finish, lead=pad[0], trail=pad[1], flips=flips, plan=None),
        out_shape=jax.ShapeDtypeStruct(
            (count, rows_in - 2, pad[0] + width + pad[1], kernel.shape[3]), dtype if finish else jnp.float32
        ),
        in_specs=specs,
        out_specs=vmem,
        scratch_shapes=[pltpu.VMEM((count, 3 * depth, 3 * kernel.shape[3]), field.dtype)],
    )(*args)


def conv_gather(sources, gather, kernel, flips):
    count, rows_in = len(gather), len(gather[0])
    width, depth = sources[0].shape[-2], sources[0].shape[-1]
    vmem = pl.BlockSpec(memory_space=pltpu.VMEM)
    return pl.pallas_call(
        functools.partial(_conv_kernel, finish=False, lead=0, trail=0, flips=flips, plan=None, gather=gather),
        out_shape=(
            jax.ShapeDtypeStruct((count, rows_in - 2, width, kernel.shape[3]), jnp.float32),
            jax.ShapeDtypeStruct((count, 2, kernel.shape[3]), jnp.float32),
        ),
        in_specs=[vmem] * (len(sources) + 1),
        out_specs=(vmem, vmem),
        scratch_shapes=[
            pltpu.VMEM((count, 3 * depth, 3 * kernel.shape[3]), jnp.bfloat16),
            pltpu.VMEM((count, rows_in, width, depth), jnp.bfloat16),
        ],
    )(*sources, kernel.astype(jnp.bfloat16))


def conv_hidden(sources, plan, mean, inv_scale, kernel, flips, bias, first_in, total_rows, pad=(0, 0),
                dtype=jnp.bfloat16, reverse=False):
    rows_in = len(plan)
    width, depth = sources[0].shape[2], sources[0].shape[3]
    vmem = pl.BlockSpec(memory_space=pltpu.VMEM)
    where = jnp.stack([first_in + 1, total_rows, first_in]).astype(jnp.int32)
    args = [where, *sources, mean.reshape(1, -1), inv_scale.reshape(1, -1),
            kernel.astype(jnp.bfloat16), bias.astype(jnp.float32).reshape(1, -1)]
    specs = [pl.BlockSpec(memory_space=pltpu.SMEM)] + [vmem] * (len(sources) + 4)
    return pl.pallas_call(
        functools.partial(
            _conv_kernel, finish=True, lead=pad[0], trail=pad[1], flips=flips, plan=plan, reverse=reverse
        ),
        out_shape=jax.ShapeDtypeStruct((1, rows_in - 2, pad[0] + width + pad[1], kernel.shape[3]), dtype),
        in_specs=specs,
        out_specs=vmem,
        scratch_shapes=[
            pltpu.VMEM((1, 3 * depth, 3 * kernel.shape[3]), jnp.bfloat16),
            pltpu.VMEM((1, rows_in, width, depth), jnp.bfloat16),
        ],
    )(*args)


def finish_features(second_out, latter_kernel_intercept):
    shifted = second_out + latter_kernel_intercept
    return (
        shifted * lax.rsqrt(jnp.mean(shifted * shifted, axis=-1, keepdims=True) + 1e-06)
    ).astype(jnp.bfloat16)


def in_map(rows_from, count, rows_dev):
    total = rows_dev * lax.axis_size("rows")
    first = lax.axis_index("rows") * rows_dev + rows_from
    row = first + lax.broadcasted_iota(jnp.int32, (count, 1, 1), 0)
    return (row >= 0) & (row < total)


def local(
    specimen_pair_inputs,
    initial_kernel_tensor,
    latter_kernel_tensor,
    latter_kernel_intercept,
    patch_horizontal_shift,
    specimen_presence,
    softmax_sharpening,
):
    x0 = specimen_pair_inputs[0]
    x1 = specimen_pair_inputs[1]
    k1 = initial_kernel_tensor
    rows_dev = x0.shape[0]
    width = x0.shape[1]
    size = lax.axis_size("rows")
    cells_all = rows_dev * size * width
    near, far = 2, 6
    up = [(i, i + 1) for i in range(size - 1)]
    down = [(i + 1, i) for i in range(size - 1)]
    before = lax.ppermute(
        jnp.concatenate([x0[rows_dev - near:], x1[rows_dev - far:]], axis=0), "rows", up
    )
    after = lax.ppermute(
        jnp.concatenate([x0[:near], x1[:far]], axis=0), "rows", down
    )

    ends = jnp.concatenate([specimen_pair_inputs[:, :2], specimen_pair_inputs[:, rows_dev - 2:]], axis=1)

    def own(slide, r, halo):
        if not halo:
            return (0, (slide, r))
        return (0, (slide, r if r < 2 else r - rows_dev + 4))

    def row0(r, halo=True):
        if r < 0:
            return (1, (near + r,))
        if r >= rows_dev:
            return (2, (r - rows_dev,))
        return own(0, r, halo)

    def row1(r, halo=True):
        if r < 0:
            return (1, (near + far + r,))
        if r >= rows_dev:
            return (2, (near + r - rows_dev,))
        return own(1, r, halo)

    def rows_of(pick, lo, hi):
        return tuple(pick(r) for r in range(lo, hi))

    inputs = (specimen_pair_inputs,)
    halos = (ends, before, after)
    interior, inner_sums = conv_gather(
        inputs,
        (
            tuple(row0(r, False) for r in range(rows_dev)),
            tuple(row1(r, False) for r in range(rows_dev)),
        ),
        k1,
        (False, False),
    )
    boundary, edge_sums = conv_gather(
        halos,
        (
            rows_of(row0, -1, 2),
            rows_of(row0, rows_dev - 2, rows_dev + 1),
            rows_of(row1, -1, 2),
            rows_of(row1, rows_dev - 2, rows_dev + 1),
        ),
        k1,
        (False, False, False, False),
    )
    per_slide = inner_sums + edge_sums[0::2] + edge_sums[1::2]
    stats = jnp.concatenate([per_slide[:, 0], per_slide[:, 1]], axis=0)
    stats, (edge0, edge1) = butterfly_sum(
        stats,
        "rows",
        [
            lambda: conv_gather(
                halos, (rows_of(row0, -near, 1), rows_of(row0, rows_dev - 1, rows_dev + near)), k1, (False, False)
            )[0],
            lambda: conv_gather(
                halos, (rows_of(row1, -far, 1), rows_of(row1, rows_dev - 1, rows_dev + far)), k1, (False, False)
            )[0],
        ],
    )
    average = stats[0:2] / cells_all
    variance = stats[2:4] / cells_all - average * average
    inv_scale = lax.rsqrt(variance + 1e-05)
    sources = (edge0, boundary, interior, edge1)
    plan0 = ((0, 0, 0), (1, 0, 0)) + tuple((2, 0, r) for r in range(rows_dev - 2)) + ((1, 1, 0), (0, 1, 0))
    halo = far - 1
    plan1 = (
        tuple((2, 0, r) for r in range(halo))
        + ((0, 2, 0),)
        + tuple((1, 1, r) for r in range(rows_dev - 2))
        + ((0, 3, 0),)
        + tuple((2, 1, r) for r in range(halo))
    )
    total = rows_dev * size
    first = lax.axis_index("rows") * rows_dev
    source = conv_hidden(
        sources[:3], plan0, average[0], inv_scale[0], latter_kernel_tensor, (False,),
        latter_kernel_intercept, first - 1, total,
    )[0]
    target_reversed = conv_hidden(
        sources[1:], plan1, average[1], inv_scale[1], latter_kernel_tensor, (True,),
        latter_kernel_intercept, first - halo, total, pad=(64, 8), dtype=jnp.float32, reverse=True,
    )[0]
    return correlation(
        source,
        target_reversed,
        patch_horizontal_shift,
        specimen_presence,
        softmax_sharpening,
    )


def solution(mesh):
    return jax.shard_map(
        local,
        mesh=mesh,
        in_specs=(
            P(None, ("pairs", "rows"), None, None),
            P(),
            P(),
            P(),
            P(("pairs", "rows"), None),
            P(("pairs", "rows"), None),
            P(("pairs", "rows"), None),
        ),
        out_specs=P(None, ("pairs", "rows"), None),
        check_vma=False,
    )
```

```python
import functools

import jax
import jax.numpy as jnp
from jax import lax
from jax.sharding import PartitionSpec as P
from jax.experimental import pallas as pl
from jax.experimental.pallas import tpu as pltpu

DISP = 81


def _corr_kernel(shift_ref, sharp_ref, pres_ref, f0_ref, frev_hbm, out_ref, win_ref, acc_ref, sems):
    rows = f0_ref.shape[0]
    half = f0_ref.shape[1] // 4
    copies = []
    for t in range(2):
        for q in range(2):
            start = 196 - 128 * t - half * q - shift_ref[0, t]
            cp = pltpu.make_async_copy(frev_hbm.at[:, pl.ds(start, 128), :], win_ref.at[2 * t + q],
                                       sems.at[2 * t + q])
            cp.start()
            copies.append(cp)
    lane = lax.broadcasted_iota(jnp.int32, (half, 128), 1)
    band = lane // 9
    li = lax.broadcasted_iota(jnp.int32, (128, 1), 0)
    valid = li < DISP
    row_d = jnp.where(valid, li // 9 - 4, 0).astype(jnp.float32)
    col_d = jnp.where(valid, 4 - li % 9, 0).astype(jnp.float32)
    for t in range(2):
        shift_t = shift_ref[0, t].astype(jnp.float32)
        scale = sharp_ref[0, t] / 128.0
        present = pres_ref[0, t].astype(jnp.float32)
        for q in range(2):
            cols = slice(128 * t + half * q, 128 * t + half * (q + 1))
            copies[2 * t + q].wait()
            acc_ref[...] = jnp.zeros_like(acc_ref)
            for hp in range(rows + 8):
                lo, hi = max(0, hp - 8), min(rows - 1, hp)
                lhs = f0_ref[lo:hi + 1, cols, :].reshape((hi - lo + 1) * half, 128)
                w = win_ref[2 * t + q, hp].astype(jnp.bfloat16)
                s = lax.dot_general(lhs, w, (((1,), (1,)), ((), ())), preferred_element_type=jnp.float32)
                for h in range(lo, hi + 1):
                    a = hp - h
                    blk = s[(h - lo) * half:(h - lo + 1) * half]
                    rolled = pltpu.roll(blk, 9 + 9 * a, 1, stride=1, stride_axis=0)
                    acc_ref[h] = jnp.where(band == a, rolled, acc_ref[h])
            for i in range(rows // 2):
                pair = acc_ref[2 * i:2 * i + 2].reshape(2 * half, 128)
                energy = jnp.transpose(pair) * scale
                energy = jnp.where(valid, energy, -jnp.inf)
                top = jnp.max(energy, axis=0, keepdims=True)
                p = jnp.exp(energy - top)
                inv = 1.0 / jnp.sum(p, axis=0, keepdims=True)
                fy = jnp.sum(p * row_d, axis=0, keepdims=True) * inv * present
                fx = (jnp.sum(p * col_d, axis=0, keepdims=True) * inv + shift_t) * present
                for k in range(2):
                    out_ref[0, 2 * i + k:2 * i + k + 1, cols] = fy[:, k * half:(k + 1) * half]
                    out_ref[1, 2 * i + k:2 * i + k + 1, cols] = fx[:, k * half:(k + 1) * half]


def correlation(f0, f1rev_ext, shift, presence, sharp):
    rows, width, depth = f0.shape
    frev = f1rev_ext
    return pl.pallas_call(
        _corr_kernel,
        out_shape=jax.ShapeDtypeStruct((2, rows, width), jnp.float32),
        in_specs=[pl.BlockSpec(memory_space=pltpu.SMEM)] * 3
        + [pl.BlockSpec(memory_space=pltpu.VMEM), pl.BlockSpec(memory_space=pl.ANY)],
        out_specs=pl.BlockSpec(memory_space=pltpu.VMEM),
        scratch_shapes=[
            pltpu.VMEM((4, rows + 8, 128, depth), jnp.float32),
            pltpu.VMEM((rows, 64, 128), jnp.float32),
            pltpu.SemaphoreType.DMA((4,)),
        ],
    )(shift, sharp, presence, f0, frev)


def extended(array, sides, width):
    for axis, dim in sides:
        size, length = (lax.axis_size(axis), array.shape[dim])
        up = [(i, (i + 1) % size) for i in range(size - 1)]
        down = [(j, i) for i, j in up]
        last = lax.slice_in_dim(array, length - width, length, axis=dim)
        initial = lax.slice_in_dim(array, 0, width, axis=dim)
        before = lax.ppermute(last, axis, up)
        after = lax.ppermute(initial, axis, down)
        array = jnp.concatenate([before, array, after], axis=dim)
    return array


def butterfly_sum(x, axis, fillers):
    size = lax.axis_size(axis)
    if size & (size - 1):
        return lax.psum(x, axis), [fill() for fill in fillers]
    done = []
    step = 1
    while step < size:
        moved = lax.ppermute(x, axis, [(i, i ^ step) for i in range(size)])
        if len(done) < len(fillers):
            value = fillers[len(done)]()
            x, value = lax.optimization_barrier((x + moved, value))
            done.append(value)
        else:
            x = x + moved
        step *= 2
    return x, done + [fill() for fill in fillers[len(done):]]


def _reverse_rows(value):
    tiles = value.shape[0] // 8
    v = value.reshape(tiles, 8, value.shape[1])
    v = jnp.concatenate([v[i:i + 1] for i in reversed(range(tiles))], axis=0)
    sub = lax.broadcasted_iota(jnp.int32, v.shape, 1)
    for step in (1, 2, 4):
        v = jnp.where((sub & step) != 0, pltpu.roll(v, step, 1), pltpu.roll(v, 8 - step, 1))
    return v.reshape(value.shape)


def _conv_kernel(*refs, finish, lead, trail, flips, plan, gather=None, reverse=False):
    sums_ref = None
    if gather:
        *sources, k_ref, o_ref, sums_ref, w_ref, x_ref = refs
        for n, rows in enumerate(gather):
            for r, (which, index) in enumerate(rows):
                x_ref[n, r] = sources[which][index].astype(x_ref.dtype)
    elif plan:
        where_ref, *sources, mean_ref, inv_ref, k_ref, bias_ref, o_ref, w_ref, x_ref = refs
        for r, (which, n, row) in enumerate(plan):
            value = jnp.maximum((sources[which][n, row] - mean_ref[...]) * inv_ref[...], 0.0)
            g = where_ref[2] + r
            keep = (g >= 0) & (g < where_ref[1])
            value = jnp.where(keep, value, 0.0)
            if reverse:
                value = _reverse_rows(value)
            x_ref[0, r] = value.astype(x_ref.dtype)
    elif finish:
        where_ref, x_ref, k_ref, bias_ref, o_ref, w_ref = refs
    else:
        x_ref, k_ref, o_ref, w_ref = refs
    count, rows_out, _, depth = o_ref.shape
    width = x_ref.shape[2]
    for n, flip in enumerate(flips):
        for dr in range(3):
            for dc in range(3):
                w_ref[n, dr * depth:(dr + 1) * depth, dc * depth:(dc + 1) * depth] = k_ref[
                    dr, 2 - dc if flip else dc
                ]
    if lead:
        o_ref[:, :, lead - 8:lead] = jnp.zeros((count, rows_out, 8, depth), o_ref.dtype)
    if trail:
        o_ref[:, :, lead + width:] = jnp.zeros((count, rows_out, trail, depth), o_ref.dtype)
    chunk = 4 if rows_out % 4 == 0 else (2 if rows_out % 2 == 0 else 1)
    m = chunk * width
    flat = lax.broadcasted_iota(jnp.int32, (m, depth), 0)
    left = flat % width != 0
    right = flat % width != width - 1
    if len(set(flips)) == 1 and chunk < 4 and count > 1:
        cells = [(n, r) for n in range(count) for r in range(rows_out)]
        group = max(1, min(len(cells), 1024 // width))
        while len(cells) % group:
            group -= 1
        m = group * width
        flat = lax.broadcasted_iota(jnp.int32, (m, depth), 0)
        left = flat % width != 0
        right = flat % width != width - 1
        totals = {}
        for g0 in range(0, len(cells), group):
            part = cells[g0:g0 + group]
            lhs = jnp.concatenate(
                [jnp.concatenate([x_ref[n, r + dr] for n, r in part], axis=0) for dr in range(3)], axis=1
            )
            y = jnp.dot(lhs, w_ref[0], preferred_element_type=jnp.float32)
            out = (
                y[:, depth:2 * depth]
                + jnp.where(left, pltpu.roll(y[:, :depth], 1, 0), 0.0)
                + jnp.where(right, pltpu.roll(y[:, 2 * depth:], m - 1, 0), 0.0)
            )
            for k, (n, r) in enumerate(part):
                segment = out[k * width:(k + 1) * width]
                o_ref[n, r] = segment.astype(o_ref.dtype)
                if sums_ref is not None:
                    both = jnp.concatenate(
                        [jnp.sum(segment, axis=0, keepdims=True),
                         jnp.sum(segment * segment, axis=0, keepdims=True)], axis=0
                    )
                    totals[n] = both if n not in totals else totals[n] + both
        if sums_ref is not None:
            for n in range(count):
                sums_ref[n] = totals[n]
        return
    assert sums_ref is None
    for n in range(count):
        for r0 in range(0, rows_out, chunk):
            lhs = jnp.concatenate(
                [x_ref[n, r0 + dr:r0 + dr + chunk].reshape(m, depth) for dr in range(3)], axis=1
            )
            y = jnp.dot(lhs, w_ref[n], preferred_element_type=jnp.float32)
            out = (
                y[:, depth:2 * depth]
                + jnp.where(left, pltpu.roll(y[:, :depth], 1, 0), 0.0)
                + jnp.where(right, pltpu.roll(y[:, 2 * depth:], m - 1, 0), 0.0)
            )
            if finish:
                out = out + bias_ref[...]
                ms = jnp.mean(out * out, axis=1, keepdims=True)
                out = out * lax.rsqrt(ms + 1e-06)
                row = where_ref[0] + r0 + flat[:, 0:1] // width
                out = jnp.where((row >= 0) & (row < where_ref[1]), out, 0.0)
            o_ref[n, r0:r0 + chunk, lead:lead + width] = out.reshape(chunk, width, depth).astype(o_ref.dtype)


def conv_rows(field, kernel, flips, bias=None, first_row=None, total_rows=None, pad=(0, 0), dtype=jnp.bfloat16):
    count, rows_in, width, depth = field.shape
    vmem = pl.BlockSpec(memory_space=pltpu.VMEM)
    finish = bias is not None
    args = [field, kernel.astype(field.dtype)]
    specs = [vmem, vmem]
    if finish:
        where = jnp.stack([first_row, total_rows]).astype(jnp.int32)
        args = [where] + args + [bias.astype(jnp.float32).reshape(1, -1)]
        specs = [pl.BlockSpec(memory_space=pltpu.SMEM)] + specs + [vmem]
    return pl.pallas_call(
        functools.partial(_conv_kernel, finish=finish, lead=pad[0], trail=pad[1], flips=flips, plan=None),
        out_shape=jax.ShapeDtypeStruct(
            (count, rows_in - 2, pad[0] + width + pad[1], kernel.shape[3]), dtype if finish else jnp.float32
        ),
        in_specs=specs,
        out_specs=vmem,
        scratch_shapes=[pltpu.VMEM((count, 3 * depth, 3 * kernel.shape[3]), field.dtype)],
    )(*args)


def conv_gather(sources, gather, kernel, flips):
    count, rows_in = len(gather), len(gather[0])
    width, depth = sources[0].shape[-2], sources[0].shape[-1]
    vmem = pl.BlockSpec(memory_space=pltpu.VMEM)
    return pl.pallas_call(
        functools.partial(_conv_kernel, finish=False, lead=0, trail=0, flips=flips, plan=None, gather=gather),
        out_shape=(
            jax.ShapeDtypeStruct((count, rows_in - 2, width, kernel.shape[3]), jnp.float32),
            jax.ShapeDtypeStruct((count, 2, kernel.shape[3]), jnp.float32),
        ),
        in_specs=[vmem] * (len(sources) + 1),
        out_specs=(vmem, vmem),
        scratch_shapes=[
            pltpu.VMEM((count, 3 * depth, 3 * kernel.shape[3]), jnp.bfloat16),
            pltpu.VMEM((count, rows_in, width, depth), jnp.bfloat16),
        ],
    )(*sources, kernel.astype(jnp.bfloat16))


def conv_hidden(sources, plan, mean, inv_scale, kernel, flips, bias, first_in, total_rows, pad=(0, 0),
                dtype=jnp.bfloat16, reverse=False):
    rows_in = len(plan)
    width, depth = sources[0].shape[2], sources[0].shape[3]
    vmem = pl.BlockSpec(memory_space=pltpu.VMEM)
    where = jnp.stack([first_in + 1, total_rows, first_in]).astype(jnp.int32)
    args = [where, *sources, mean.reshape(1, -1), inv_scale.reshape(1, -1),
            kernel.astype(jnp.bfloat16), bias.astype(jnp.float32).reshape(1, -1)]
    specs = [pl.BlockSpec(memory_space=pltpu.SMEM)] + [vmem] * (len(sources) + 4)
    return pl.pallas_call(
        functools.partial(
            _conv_kernel, finish=True, lead=pad[0], trail=pad[1], flips=flips, plan=plan, reverse=reverse
        ),
        out_shape=jax.ShapeDtypeStruct((1, rows_in - 2, pad[0] + width + pad[1], kernel.shape[3]), dtype),
        in_specs=specs,
        out_specs=vmem,
        scratch_shapes=[
            pltpu.VMEM((1, 3 * depth, 3 * kernel.shape[3]), jnp.bfloat16),
            pltpu.VMEM((1, rows_in, width, depth), jnp.bfloat16),
        ],
    )(*args)


def finish_features(second_out, latter_kernel_intercept):
    shifted = second_out + latter_kernel_intercept
    return (
        shifted * lax.rsqrt(jnp.mean(shifted * shifted, axis=-1, keepdims=True) + 1e-06)
    ).astype(jnp.bfloat16)


def in_map(rows_from, count, rows_dev):
    total = rows_dev * lax.axis_size("rows")
    first = lax.axis_index("rows") * rows_dev + rows_from
    row = first + lax.broadcasted_iota(jnp.int32, (count, 1, 1), 0)
    return (row >= 0) & (row < total)


def local(
    specimen_pair_inputs,
    initial_kernel_tensor,
    latter_kernel_tensor,
    latter_kernel_intercept,
    patch_horizontal_shift,
    specimen_presence,
    softmax_sharpening,
):
    x0 = specimen_pair_inputs[0]
    x1 = specimen_pair_inputs[1]
    k1 = initial_kernel_tensor
    rows_dev = x0.shape[0]
    width = x0.shape[1]
    size = lax.axis_size("rows")
    cells_all = rows_dev * size * width
    near, far = 2, 6
    up = [(i, i + 1) for i in range(size - 1)]
    down = [(i + 1, i) for i in range(size - 1)]
    before = lax.ppermute(
        jnp.concatenate([x0[rows_dev - near:], x1[rows_dev - far:]], axis=0), "rows", up
    )
    after = lax.ppermute(
        jnp.concatenate([x0[:near], x1[:far]], axis=0), "rows", down
    )

    ends = jnp.concatenate([specimen_pair_inputs[:, :2], specimen_pair_inputs[:, rows_dev - 2:]], axis=1)

    def own(slide, r, halo):
        if not halo:
            return (0, (slide, r))
        return (0, (slide, r if r < 2 else r - rows_dev + 4))

    def row0(r, halo=True):
        if r < 0:
            return (1, (near + r,))
        if r >= rows_dev:
            return (2, (r - rows_dev,))
        return own(0, r, halo)

    def row1(r, halo=True):
        if r < 0:
            return (1, (near + far + r,))
        if r >= rows_dev:
            return (2, (near + r - rows_dev,))
        return own(1, r, halo)

    def rows_of(pick, lo, hi):
        return tuple(pick(r) for r in range(lo, hi))

    inputs = (specimen_pair_inputs,)
    halos = (ends, before, after)
    interior, inner_sums = conv_gather(
        inputs,
        (
            tuple(row0(r, False) for r in range(rows_dev)),
            tuple(row1(r, False) for r in range(rows_dev)),
        ),
        k1,
        (False, False),
    )
    boundary, edge_sums = conv_gather(
        halos,
        (
            rows_of(row0, -1, 2),
            rows_of(row0, rows_dev - 2, rows_dev + 1),
            rows_of(row1, -1, 2),
            rows_of(row1, rows_dev - 2, rows_dev + 1),
        ),
        k1,
        (False, False, False, False),
    )
    per_slide = inner_sums + edge_sums[0::2] + edge_sums[1::2]
    stats = jnp.concatenate([per_slide[:, 0], per_slide[:, 1]], axis=0)
    stats, (edge0, edge1) = butterfly_sum(
        stats,
        "rows",
        [
            lambda: conv_gather(
                halos, (rows_of(row0, -near, 1), rows_of(row0, rows_dev - 1, rows_dev + near)), k1, (False, False)
            )[0],
            lambda: conv_gather(
                halos, (rows_of(row1, -far, 1), rows_of(row1, rows_dev - 1, rows_dev + far)), k1, (False, False)
            )[0],
        ],
    )
    average = stats[0:2] / cells_all
    variance = stats[2:4] / cells_all - average * average
    inv_scale = lax.rsqrt(variance + 1e-05)
    sources = (edge0, boundary, interior, edge1)
    plan0 = ((0, 0, 0), (1, 0, 0)) + tuple((2, 0, r) for r in range(rows_dev - 2)) + ((1, 1, 0), (0, 1, 0))
    halo = far - 1
    plan1 = (
        tuple((2, 0, r) for r in range(halo))
        + ((0, 2, 0),)
        + tuple((1, 1, r) for r in range(rows_dev - 2))
        + ((0, 3, 0),)
        + tuple((2, 1, r) for r in range(halo))
    )
    total = rows_dev * size
    first = lax.axis_index("rows") * rows_dev
    source = conv_hidden(
        sources[:3], plan0, average[0], inv_scale[0], latter_kernel_tensor, (False,),
        latter_kernel_intercept, first - 1, total,
    )[0]
    target_reversed = conv_hidden(
        sources[1:], plan1, average[1], inv_scale[1], latter_kernel_tensor, (True,),
        latter_kernel_intercept, first - halo, total, pad=(64, 8), dtype=jnp.float32, reverse=True,
    )[0]
    return correlation(
        source,
        target_reversed,
        patch_horizontal_shift,
        specimen_presence,
        softmax_sharpening,
    )


def solution(mesh):
    return jax.shard_map(
        local,
        mesh=mesh,
        in_specs=(
            P(None, ("pairs", "rows"), None, None),
            P(),
            P(),
            P(),
            P(("pairs", "rows"), None),
            P(("pairs", "rows"), None),
            P(("pairs", "rows"), None),
        ),
        out_specs=P(None, ("pairs", "rows"), None),
        check_vma=False,
    )
```

```python
import functools

import jax
import jax.numpy as jnp
from jax import lax
from jax.sharding import PartitionSpec as P
from jax.experimental import pallas as pl
from jax.experimental.pallas import tpu as pltpu

DISP = 81


def _corr_kernel(shift_ref, sharp_ref, pres_ref, f0_ref, frev_hbm, out_ref, win_ref, acc_ref, sems):
    rows = f0_ref.shape[0]
    half = f0_ref.shape[1] // 4
    copies = []
    for t in range(2):
        for q in range(2):
            start = 196 - 128 * t - half * q - shift_ref[0, t]
            cp = pltpu.make_async_copy(frev_hbm.at[:, pl.ds(start, 128), :], win_ref.at[2 * t + q],
                                       sems.at[2 * t + q])
            cp.start()
            copies.append(cp)
    lane = lax.broadcasted_iota(jnp.int32, (half, 128), 1)
    band = lane // 9
    li = lax.broadcasted_iota(jnp.int32, (128, 1), 0)
    valid = li < DISP
    row_d = jnp.where(valid, li // 9 - 4, 0).astype(jnp.float32)
    col_d = jnp.where(valid, 4 - li % 9, 0).astype(jnp.float32)
    acc_ref[...] = jnp.zeros_like(acc_ref)
    for t in range(2):
        shift_t = shift_ref[0, t].astype(jnp.float32)
        scale = sharp_ref[0, t] / 128.0
        present = pres_ref[0, t].astype(jnp.float32)
        for q in range(2):
            cols = slice(128 * t + half * q, 128 * t + half * (q + 1))
            copies[2 * t + q].wait()
            for hp in range(rows + 8):
                lo, hi = max(0, hp - 8), min(rows - 1, hp)
                lhs = f0_ref[lo:hi + 1, cols, :].reshape((hi - lo + 1) * half, 128)
                w = win_ref[2 * t + q, hp].astype(jnp.bfloat16)
                s = lax.dot_general(lhs, w, (((1,), (1,)), ((), ())), preferred_element_type=jnp.float32)
                for h in range(lo, hi + 1):
                    a = hp - h
                    blk = s[(h - lo) * half:(h - lo + 1) * half]
                    rolled = pltpu.roll(blk, 9 + 9 * a, 1, stride=1, stride_axis=0)
                    acc_ref[h] = jnp.where(band == a, rolled, acc_ref[h])
            for i in range(rows // 2):
                pair = acc_ref[2 * i:2 * i + 2].reshape(2 * half, 128)
                energy = jnp.transpose(pair) * scale
                energy = jnp.where(valid, energy, -jnp.inf)
                top = jnp.max(energy, axis=0, keepdims=True)
                p = jnp.exp(energy - top)
                inv = 1.0 / jnp.sum(p, axis=0, keepdims=True)
                fy = jnp.sum(p * row_d, axis=0, keepdims=True) * inv * present
                fx = (jnp.sum(p * col_d, axis=0, keepdims=True) * inv + shift_t) * present
                for k in range(2):
                    out_ref[0, 2 * i + k:2 * i + k + 1, cols] = fy[:, k * half:(k + 1) * half]
                    out_ref[1, 2 * i + k:2 * i + k + 1, cols] = fx[:, k * half:(k + 1) * half]


def correlation(f0, f1rev_ext, shift, presence, sharp):
    rows, width, depth = f0.shape
    frev = f1rev_ext
    return pl.pallas_call(
        _corr_kernel,
        out_shape=jax.ShapeDtypeStruct((2, rows, width), jnp.float32),
        in_specs=[pl.BlockSpec(memory_space=pltpu.SMEM)] * 3
        + [pl.BlockSpec(memory_space=pltpu.VMEM), pl.BlockSpec(memory_space=pl.ANY)],
        out_specs=pl.BlockSpec(memory_space=pltpu.VMEM),
        scratch_shapes=[
            pltpu.VMEM((4, rows + 8, 128, depth), jnp.float32),
            pltpu.VMEM((rows, 64, 128), jnp.float32),
            pltpu.SemaphoreType.DMA((4,)),
        ],
    )(shift, sharp, presence, f0, frev)


def extended(array, sides, width):
    for axis, dim in sides:
        size, length = (lax.axis_size(axis), array.shape[dim])
        up = [(i, (i + 1) % size) for i in range(size - 1)]
        down = [(j, i) for i, j in up]
        last = lax.slice_in_dim(array, length - width, length, axis=dim)
        initial = lax.slice_in_dim(array, 0, width, axis=dim)
        before = lax.ppermute(last, axis, up)
        after = lax.ppermute(initial, axis, down)
        array = jnp.concatenate([before, array, after], axis=dim)
    return array


def butterfly_sum(x, axis, fillers):
    size = lax.axis_size(axis)
    if size & (size - 1):
        return lax.psum(x, axis), [fill() for fill in fillers]
    done = []
    step = 1
    while step < size:
        moved = lax.ppermute(x, axis, [(i, i ^ step) for i in range(size)])
        if len(done) < len(fillers):
            value = fillers[len(done)]()
            x, value = lax.optimization_barrier((x + moved, value))
            done.append(value)
        else:
            x = x + moved
        step *= 2
    return x, done + [fill() for fill in fillers[len(done):]]


def _reverse_rows(value):
    tiles = value.shape[0] // 8
    v = value.reshape(tiles, 8, value.shape[1])
    v = jnp.concatenate([v[i:i + 1] for i in reversed(range(tiles))], axis=0)
    sub = lax.broadcasted_iota(jnp.int32, v.shape, 1)
    for step in (1, 2, 4):
        v = jnp.where((sub & step) != 0, pltpu.roll(v, step, 1), pltpu.roll(v, 8 - step, 1))
    return v.reshape(value.shape)


def _conv_kernel(*refs, finish, lead, trail, flips, plan, gather=None, reverse=False):
    sums_ref = None
    if gather:
        *sources, k_ref, o_ref, sums_ref, w_ref, x_ref = refs
        for n, rows in enumerate(gather):
            for r, (which, index) in enumerate(rows):
                x_ref[n, r] = sources[which][index].astype(x_ref.dtype)
    elif plan:
        where_ref, *sources, mean_ref, inv_ref, k_ref, bias_ref, o_ref, w_ref, x_ref = refs
        for r, (which, n, row) in enumerate(plan):
            value = jnp.maximum((sources[which][n, row] - mean_ref[...]) * inv_ref[...], 0.0)
            g = where_ref[2] + r
            keep = (g >= 0) & (g < where_ref[1])
            value = jnp.where(keep, value, 0.0)
            if reverse:
                value = _reverse_rows(value)
            x_ref[0, r] = value.astype(x_ref.dtype)
    elif finish:
        where_ref, x_ref, k_ref, bias_ref, o_ref, w_ref = refs
    else:
        x_ref, k_ref, o_ref, w_ref = refs
    count, rows_out, _, depth = o_ref.shape
    width = x_ref.shape[2]
    for n, flip in enumerate(flips):
        for dr in range(3):
            for dc in range(3):
                w_ref[n, dr * depth:(dr + 1) * depth, dc * depth:(dc + 1) * depth] = k_ref[
                    dr, 2 - dc if flip else dc
                ]
    if lead:
        o_ref[:, :, :lead] = jnp.zeros((count, rows_out, lead, depth), o_ref.dtype)
    if trail:
        o_ref[:, :, lead + width:] = jnp.zeros((count, rows_out, trail, depth), o_ref.dtype)
    chunk = 4 if rows_out % 4 == 0 else (2 if rows_out % 2 == 0 else 1)
    m = chunk * width
    flat = lax.broadcasted_iota(jnp.int32, (m, depth), 0)
    left = flat % width != 0
    right = flat % width != width - 1
    if len(set(flips)) == 1 and chunk < 4 and count > 1:
        cells = [(n, r) for n in range(count) for r in range(rows_out)]
        group = max(1, min(len(cells), 1024 // width))
        while len(cells) % group:
            group -= 1
        m = group * width
        flat = lax.broadcasted_iota(jnp.int32, (m, depth), 0)
        left = flat % width != 0
        right = flat % width != width - 1
        totals = {}
        for g0 in range(0, len(cells), group):
            part = cells[g0:g0 + group]
            lhs = jnp.concatenate(
                [jnp.concatenate([x_ref[n, r + dr] for n, r in part], axis=0) for dr in range(3)], axis=1
            )
            y = jnp.dot(lhs, w_ref[0], preferred_element_type=jnp.float32)
            out = (
                y[:, depth:2 * depth]
                + jnp.where(left, pltpu.roll(y[:, :depth], 1, 0), 0.0)
                + jnp.where(right, pltpu.roll(y[:, 2 * depth:], m - 1, 0), 0.0)
            )
            for k, (n, r) in enumerate(part):
                segment = out[k * width:(k + 1) * width]
                o_ref[n, r] = segment.astype(o_ref.dtype)
                if sums_ref is not None:
                    both = jnp.concatenate(
                        [jnp.sum(segment, axis=0, keepdims=True),
                         jnp.sum(segment * segment, axis=0, keepdims=True)], axis=0
                    )
                    totals[n] = both if n not in totals else totals[n] + both
        if sums_ref is not None:
            for n in range(count):
                sums_ref[n] = totals[n]
        return
    assert sums_ref is None
    for n in range(count):
        for r0 in range(0, rows_out, chunk):
            lhs = jnp.concatenate(
                [x_ref[n, r0 + dr:r0 + dr + chunk].reshape(m, depth) for dr in range(3)], axis=1
            )
            y = jnp.dot(lhs, w_ref[n], preferred_element_type=jnp.float32)
            out = (
                y[:, depth:2 * depth]
                + jnp.where(left, pltpu.roll(y[:, :depth], 1, 0), 0.0)
                + jnp.where(right, pltpu.roll(y[:, 2 * depth:], m - 1, 0), 0.0)
            )
            if finish:
                out = out + bias_ref[...]
                ms = jnp.mean(out * out, axis=1, keepdims=True)
                out = out * lax.rsqrt(ms + 1e-06)
                row = where_ref[0] + r0 + flat[:, 0:1] // width
                out = jnp.where((row >= 0) & (row < where_ref[1]), out, 0.0)
            o_ref[n, r0:r0 + chunk, lead:lead + width] = out.reshape(chunk, width, depth).astype(o_ref.dtype)


def conv_rows(field, kernel, flips, bias=None, first_row=None, total_rows=None, pad=(0, 0), dtype=jnp.bfloat16):
    count, rows_in, width, depth = field.shape
    vmem = pl.BlockSpec(memory_space=pltpu.VMEM)
    finish = bias is not None
    args = [field, kernel.astype(field.dtype)]
    specs = [vmem, vmem]
    if finish:
        where = jnp.stack([first_row, total_rows]).astype(jnp.int32)
        args = [where] + args + [bias.astype(jnp.float32).reshape(1, -1)]
        specs = [pl.BlockSpec(memory_space=pltpu.SMEM)] + specs + [vmem]
    return pl.pallas_call(
        functools.partial(_conv_kernel, finish=finish, lead=pad[0], trail=pad[1], flips=flips, plan=None),
        out_shape=jax.ShapeDtypeStruct(
            (count, rows_in - 2, pad[0] + width + pad[1], kernel.shape[3]), dtype if finish else jnp.float32
        ),
        in_specs=specs,
        out_specs=vmem,
        scratch_shapes=[pltpu.VMEM((count, 3 * depth, 3 * kernel.shape[3]), field.dtype)],
    )(*args)


def conv_gather(sources, gather, kernel, flips):
    count, rows_in = len(gather), len(gather[0])
    width, depth = sources[0].shape[-2], sources[0].shape[-1]
    vmem = pl.BlockSpec(memory_space=pltpu.VMEM)
    return pl.pallas_call(
        functools.partial(_conv_kernel, finish=False, lead=0, trail=0, flips=flips, plan=None, gather=gather),
        out_shape=(
            jax.ShapeDtypeStruct((count, rows_in - 2, width, kernel.shape[3]), jnp.float32),
            jax.ShapeDtypeStruct((count, 2, kernel.shape[3]), jnp.float32),
        ),
        in_specs=[vmem] * (len(sources) + 1),
        out_specs=(vmem, vmem),
        scratch_shapes=[
            pltpu.VMEM((count, 3 * depth, 3 * kernel.shape[3]), jnp.bfloat16),
            pltpu.VMEM((count, rows_in, width, depth), jnp.bfloat16),
        ],
    )(*sources, kernel.astype(jnp.bfloat16))


def conv_hidden(sources, plan, mean, inv_scale, kernel, flips, bias, first_in, total_rows, pad=(0, 0),
                dtype=jnp.bfloat16, reverse=False):
    rows_in = len(plan)
    width, depth = sources[0].shape[2], sources[0].shape[3]
    vmem = pl.BlockSpec(memory_space=pltpu.VMEM)
    where = jnp.stack([first_in + 1, total_rows, first_in]).astype(jnp.int32)
    args = [where, *sources, mean.reshape(1, -1), inv_scale.reshape(1, -1),
            kernel.astype(jnp.bfloat16), bias.astype(jnp.float32).reshape(1, -1)]
    specs = [pl.BlockSpec(memory_space=pltpu.SMEM)] + [vmem] * (len(sources) + 4)
    return pl.pallas_call(
        functools.partial(
            _conv_kernel, finish=True, lead=pad[0], trail=pad[1], flips=flips, plan=plan, reverse=reverse
        ),
        out_shape=jax.ShapeDtypeStruct((1, rows_in - 2, pad[0] + width + pad[1], kernel.shape[3]), dtype),
        in_specs=specs,
        out_specs=vmem,
        scratch_shapes=[
            pltpu.VMEM((1, 3 * depth, 3 * kernel.shape[3]), jnp.bfloat16),
            pltpu.VMEM((1, rows_in, width, depth), jnp.bfloat16),
        ],
    )(*args)


def finish_features(second_out, latter_kernel_intercept):
    shifted = second_out + latter_kernel_intercept
    return (
        shifted * lax.rsqrt(jnp.mean(shifted * shifted, axis=-1, keepdims=True) + 1e-06)
    ).astype(jnp.bfloat16)


def in_map(rows_from, count, rows_dev):
    total = rows_dev * lax.axis_size("rows")
    first = lax.axis_index("rows") * rows_dev + rows_from
    row = first + lax.broadcasted_iota(jnp.int32, (count, 1, 1), 0)
    return (row >= 0) & (row < total)


def local(
    specimen_pair_inputs,
    initial_kernel_tensor,
    latter_kernel_tensor,
    latter_kernel_intercept,
    patch_horizontal_shift,
    specimen_presence,
    softmax_sharpening,
):
    x0 = specimen_pair_inputs[0]
    x1 = specimen_pair_inputs[1]
    k1 = initial_kernel_tensor
    rows_dev = x0.shape[0]
    width = x0.shape[1]
    size = lax.axis_size("rows")
    cells_all = rows_dev * size * width
    near, far = 2, 6
    up = [(i, i + 1) for i in range(size - 1)]
    down = [(i + 1, i) for i in range(size - 1)]
    before = lax.ppermute(
        jnp.concatenate([x0[rows_dev - near:], x1[rows_dev - far:]], axis=0), "rows", up
    )
    after = lax.ppermute(
        jnp.concatenate([x0[:near], x1[:far]], axis=0), "rows", down
    )

    ends = jnp.concatenate([specimen_pair_inputs[:, :2], specimen_pair_inputs[:, rows_dev - 2:]], axis=1)

    def own(slide, r, halo):
        if not halo:
            return (0, (slide, r))
        return (0, (slide, r if r < 2 else r - rows_dev + 4))

    def row0(r, halo=True):
        if r < 0:
            return (1, (near + r,))
        if r >= rows_dev:
            return (2, (r - rows_dev,))
        return own(0, r, halo)

    def row1(r, halo=True):
        if r < 0:
            return (1, (near + far + r,))
        if r >= rows_dev:
            return (2, (near + r - rows_dev,))
        return own(1, r, halo)

    def rows_of(pick, lo, hi):
        return tuple(pick(r) for r in range(lo, hi))

    inputs = (specimen_pair_inputs,)
    halos = (ends, before, after)
    interior, inner_sums = conv_gather(
        inputs,
        (
            tuple(row0(r, False) for r in range(rows_dev)),
            tuple(row1(r, False) for r in range(rows_dev)),
        ),
        k1,
        (False, False),
    )
    boundary, edge_sums = conv_gather(
        halos,
        (
            rows_of(row0, -1, 2),
            rows_of(row0, rows_dev - 2, rows_dev + 1),
            rows_of(row1, -1, 2),
            rows_of(row1, rows_dev - 2, rows_dev + 1),
        ),
        k1,
        (False, False, False, False),
    )
    per_slide = inner_sums + edge_sums[0::2] + edge_sums[1::2]
    stats = jnp.concatenate([per_slide[:, 0], per_slide[:, 1]], axis=0)
    stats, (edge0, edge1) = butterfly_sum(
        stats,
        "rows",
        [
            lambda: conv_gather(
                halos, (rows_of(row0, -near, 1), rows_of(row0, rows_dev - 1, rows_dev + near)), k1, (False, False)
            )[0],
            lambda: conv_gather(
                halos, (rows_of(row1, -far, 1), rows_of(row1, rows_dev - 1, rows_dev + far)), k1, (False, False)
            )[0],
        ],
    )
    average = stats[0:2] / cells_all
    variance = stats[2:4] / cells_all - average * average
    inv_scale = lax.rsqrt(variance + 1e-05)
    sources = (edge0, boundary, interior, edge1)
    plan0 = ((0, 0, 0), (1, 0, 0)) + tuple((2, 0, r) for r in range(rows_dev - 2)) + ((1, 1, 0), (0, 1, 0))
    halo = far - 1
    plan1 = (
        tuple((2, 0, r) for r in range(halo))
        + ((0, 2, 0),)
        + tuple((1, 1, r) for r in range(rows_dev - 2))
        + ((0, 3, 0),)
        + tuple((2, 1, r) for r in range(halo))
    )
    total = rows_dev * size
    first = lax.axis_index("rows") * rows_dev
    source = conv_hidden(
        sources[:3], plan0, average[0], inv_scale[0], latter_kernel_tensor, (False,),
        latter_kernel_intercept, first - 1, total,
    )[0]
    target_reversed = conv_hidden(
        sources[1:], plan1, average[1], inv_scale[1], latter_kernel_tensor, (True,),
        latter_kernel_intercept, first - halo, total, pad=(64, 8), dtype=jnp.float32, reverse=True,
    )[0]
    return correlation(
        source,
        target_reversed,
        patch_horizontal_shift,
        specimen_presence,
        softmax_sharpening,
    )


def solution(mesh):
    return jax.shard_map(
        local,
        mesh=mesh,
        in_specs=(
            P(None, ("pairs", "rows"), None, None),
            P(),
            P(),
            P(),
            P(("pairs", "rows"), None),
            P(("pairs", "rows"), None),
            P(("pairs", "rows"), None),
        ),
        out_specs=P(None, ("pairs", "rows"), None),
        check_vma=False,
    )
```

```python
import functools

import jax
import jax.numpy as jnp
from jax import lax
from jax.sharding import PartitionSpec as P
from jax.experimental import pallas as pl
from jax.experimental.pallas import tpu as pltpu

DISP = 81


def _corr_kernel(shift_ref, sharp_ref, pres_ref, f0_ref, frev_hbm, out_ref, win_ref, acc_ref, sems):
    rows = f0_ref.shape[0]
    half = f0_ref.shape[1] // 4
    copies = []
    for t in range(2):
        for q in range(2):
            start = 196 - 128 * t - half * q - shift_ref[0, t]
            cp = pltpu.make_async_copy(frev_hbm.at[:, pl.ds(start, 128), :], win_ref.at[2 * t + q],
                                       sems.at[2 * t + q])
            cp.start()
            copies.append(cp)
    lane = lax.broadcasted_iota(jnp.int32, (half, 128), 1)
    band = lane // 9
    li = lax.broadcasted_iota(jnp.int32, (128, 1), 0)
    valid = li < DISP
    row_d = jnp.where(valid, li // 9 - 4, 0).astype(jnp.float32)
    col_d = jnp.where(valid, 4 - li % 9, 0).astype(jnp.float32)
    for t in range(2):
        shift_t = shift_ref[0, t].astype(jnp.float32)
        scale = sharp_ref[0, t] / 128.0
        present = pres_ref[0, t].astype(jnp.float32)
        for q in range(2):
            cols = slice(128 * t + half * q, 128 * t + half * (q + 1))
            copies[2 * t + q].wait()
            acc_ref[...] = jnp.zeros_like(acc_ref)
            for hp in range(rows + 8):
                lo, hi = max(0, hp - 8), min(rows - 1, hp)
                lhs = f0_ref[lo:hi + 1, cols, :].reshape((hi - lo + 1) * half, 128)
                w = win_ref[2 * t + q, hp].astype(jnp.bfloat16)
                s = lax.dot_general(lhs, w, (((1,), (1,)), ((), ())), preferred_element_type=jnp.float32)
                for h in range(lo, hi + 1):
                    a = hp - h
                    blk = s[(h - lo) * half:(h - lo + 1) * half]
                    rolled = pltpu.roll(blk, 9 + 9 * a, 1, stride=1, stride_axis=0)
                    acc_ref[h] = jnp.where(band == a, rolled, acc_ref[h])
            for i in range(rows // 2):
                pair = acc_ref[2 * i:2 * i + 2].reshape(2 * half, 128)
                energy = jnp.transpose(pair) * scale
                energy = jnp.where(valid, energy, -jnp.inf)
                top = jnp.max(energy, axis=0, keepdims=True)
                p = jnp.exp(energy - top)
                inv = 1.0 / jnp.sum(p, axis=0, keepdims=True)
                fy = jnp.sum(p * row_d, axis=0, keepdims=True) * inv * present
                fx = (jnp.sum(p * col_d, axis=0, keepdims=True) * inv + shift_t) * present
                for k in range(2):
                    out_ref[0, 2 * i + k:2 * i + k + 1, cols] = fy[:, k * half:(k + 1) * half]
                    out_ref[1, 2 * i + k:2 * i + k + 1, cols] = fx[:, k * half:(k + 1) * half]


def correlation(f0, f1rev_ext, shift, presence, sharp):
    rows, width, depth = f0.shape
    frev = f1rev_ext
    return pl.pallas_call(
        _corr_kernel,
        out_shape=jax.ShapeDtypeStruct((2, rows, width), jnp.float32),
        in_specs=[pl.BlockSpec(memory_space=pltpu.SMEM)] * 3
        + [pl.BlockSpec(memory_space=pltpu.VMEM), pl.BlockSpec(memory_space=pl.ANY)],
        out_specs=pl.BlockSpec(memory_space=pltpu.VMEM),
        scratch_shapes=[
            pltpu.VMEM((4, rows + 8, 128, depth), jnp.float32),
            pltpu.VMEM((rows, 64, 128), jnp.float32),
            pltpu.SemaphoreType.DMA((4,)),
        ],
    )(shift, sharp, presence, f0, frev)


def extended(array, sides, width):
    for axis, dim in sides:
        size, length = (lax.axis_size(axis), array.shape[dim])
        up = [(i, (i + 1) % size) for i in range(size - 1)]
        down = [(j, i) for i, j in up]
        last = lax.slice_in_dim(array, length - width, length, axis=dim)
        initial = lax.slice_in_dim(array, 0, width, axis=dim)
        before = lax.ppermute(last, axis, up)
        after = lax.ppermute(initial, axis, down)
        array = jnp.concatenate([before, array, after], axis=dim)
    return array


def butterfly_sum(x, axis, fillers):
    size = lax.axis_size(axis)
    if size & (size - 1):
        return lax.psum(x, axis), [fill() for fill in fillers]
    done = []
    step = 1
    while step < size:
        moved = lax.ppermute(x, axis, [(i, i ^ step) for i in range(size)])
        if len(done) < len(fillers):
            value = fillers[len(done)]()
            x, value = lax.optimization_barrier((x + moved, value))
            done.append(value)
        else:
            x = x + moved
        step *= 2
    return x, done + [fill() for fill in fillers[len(done):]]


def _reverse_rows(value):
    tiles = value.shape[0] // 8
    v = value.reshape(tiles, 8, value.shape[1])
    v = jnp.concatenate([v[i:i + 1] for i in reversed(range(tiles))], axis=0)
    sub = lax.broadcasted_iota(jnp.int32, v.shape, 1)
    for step in (1, 2, 4):
        v = jnp.where((sub & step) != 0, pltpu.roll(v, step, 1), pltpu.roll(v, 8 - step, 1))
    return v.reshape(value.shape)


def _conv_kernel(*refs, finish, lead, trail, flips, plan, gather=None, reverse=False):
    sums_ref = None
    if gather:
        *sources, k_ref, o_ref, sums_ref, w_ref, x_ref = refs
        for n, rows in enumerate(gather):
            for r, (which, index) in enumerate(rows):
                x_ref[n, r] = sources[which][index].astype(x_ref.dtype)
    elif plan:
        where_ref, *sources, mean_ref, inv_ref, k_ref, bias_ref, o_ref, w_ref, x_ref = refs
        for r, (which, n, row) in enumerate(plan):
            value = jnp.maximum((sources[which][n, row] - mean_ref[...]) * inv_ref[...], 0.0)
            g = where_ref[2] + r
            keep = (g >= 0) & (g < where_ref[1])
            value = jnp.where(keep, value, 0.0)
            if reverse:
                value = _reverse_rows(value)
            x_ref[0, r] = value.astype(x_ref.dtype)
    elif finish:
        where_ref, x_ref, k_ref, bias_ref, o_ref, w_ref = refs
    else:
        x_ref, k_ref, o_ref, w_ref = refs
    count, rows_out, _, depth = o_ref.shape
    width = x_ref.shape[2]
    for n, flip in enumerate(flips):
        for dr in range(3):
            for dc in range(3):
                w_ref[n, dr * depth:(dr + 1) * depth, dc * depth:(dc + 1) * depth] = k_ref[
                    dr, 2 - dc if flip else dc
                ]
    if lead:
        o_ref[:, :, :lead] = jnp.zeros((count, rows_out, lead, depth), o_ref.dtype)
    if trail:
        o_ref[:, :, lead + width:] = jnp.zeros((count, rows_out, trail, depth), o_ref.dtype)
    chunk = 4 if rows_out % 4 == 0 else (2 if rows_out % 2 == 0 else 1)
    m = chunk * width
    flat = lax.broadcasted_iota(jnp.int32, (m, depth), 0)
    left = flat % width != 0
    right = flat % width != width - 1
    if len(set(flips)) == 1 and chunk < 4 and count > 1:
        cells = [(n, r) for n in range(count) for r in range(rows_out)]
        group = max(1, min(len(cells), 1024 // width))
        while len(cells) % group:
            group -= 1
        m = group * width
        flat = lax.broadcasted_iota(jnp.int32, (m, depth), 0)
        left = flat % width != 0
        right = flat % width != width - 1
        totals = {}
        for g0 in range(0, len(cells), group):
            part = cells[g0:g0 + group]
            lhs = jnp.concatenate(
                [jnp.concatenate([x_ref[n, r + dr] for n, r in part], axis=0) for dr in range(3)], axis=1
            )
            y = jnp.dot(lhs, w_ref[0], preferred_element_type=jnp.float32)
            out = (
                y[:, depth:2 * depth]
                + jnp.where(left, pltpu.roll(y[:, :depth], 1, 0), 0.0)
                + jnp.where(right, pltpu.roll(y[:, 2 * depth:], m - 1, 0), 0.0)
            )
            for k, (n, r) in enumerate(part):
                segment = out[k * width:(k + 1) * width]
                o_ref[n, r] = segment.astype(o_ref.dtype)
                if sums_ref is not None:
                    both = jnp.concatenate(
                        [jnp.sum(segment, axis=0, keepdims=True),
                         jnp.sum(segment * segment, axis=0, keepdims=True)], axis=0
                    )
                    totals[n] = both if n not in totals else totals[n] + both
        if sums_ref is not None:
            for n in range(count):
                sums_ref[n] = totals[n]
        return
    assert sums_ref is None
    for n in range(count):
        for r0 in range(0, rows_out, chunk):
            lhs = jnp.concatenate(
                [x_ref[n, r0 + dr:r0 + dr + chunk].reshape(m, depth) for dr in range(3)], axis=1
            )
            y = jnp.dot(lhs, w_ref[n], preferred_element_type=jnp.float32)
            out = (
                y[:, depth:2 * depth]
                + jnp.where(left, pltpu.roll(y[:, :depth], 1, 0), 0.0)
                + jnp.where(right, pltpu.roll(y[:, 2 * depth:], m - 1, 0), 0.0)
            )
            if finish:
                out = out + bias_ref[...]
                ms = jnp.mean(out * out, axis=1, keepdims=True)
                out = out * lax.rsqrt(ms + 1e-06)
                row = where_ref[0] + r0 + flat[:, 0:1] // width
                out = jnp.where((row >= 0) & (row < where_ref[1]), out, 0.0)
            o_ref[n, r0:r0 + chunk, lead:lead + width] = out.reshape(chunk, width, depth).astype(o_ref.dtype)


def conv_rows(field, kernel, flips, bias=None, first_row=None, total_rows=None, pad=(0, 0), dtype=jnp.bfloat16):
    count, rows_in, width, depth = field.shape
    vmem = pl.BlockSpec(memory_space=pltpu.VMEM)
    finish = bias is not None
    args = [field, kernel.astype(field.dtype)]
    specs = [vmem, vmem]
    if finish:
        where = jnp.stack([first_row, total_rows]).astype(jnp.int32)
        args = [where] + args + [bias.astype(jnp.float32).reshape(1, -1)]
        specs = [pl.BlockSpec(memory_space=pltpu.SMEM)] + specs + [vmem]
    return pl.pallas_call(
        functools.partial(_conv_kernel, finish=finish, lead=pad[0], trail=pad[1], flips=flips, plan=None),
        out_shape=jax.ShapeDtypeStruct(
            (count, rows_in - 2, pad[0] + width + pad[1], kernel.shape[3]), dtype if finish else jnp.float32
        ),
        in_specs=specs,
        out_specs=vmem,
        scratch_shapes=[pltpu.VMEM((count, 3 * depth, 3 * kernel.shape[3]), field.dtype)],
    )(*args)


def conv_gather(sources, gather, kernel, flips):
    count, rows_in = len(gather), len(gather[0])
    width, depth = sources[0].shape[-2], sources[0].shape[-1]
    vmem = pl.BlockSpec(memory_space=pltpu.VMEM)
    return pl.pallas_call(
        functools.partial(_conv_kernel, finish=False, lead=0, trail=0, flips=flips, plan=None, gather=gather),
        out_shape=(
            jax.ShapeDtypeStruct((count, rows_in - 2, width, kernel.shape[3]), jnp.float32),
            jax.ShapeDtypeStruct((count, 2, kernel.shape[3]), jnp.float32),
        ),
        in_specs=[vmem] * (len(sources) + 1),
        out_specs=(vmem, vmem),
        scratch_shapes=[
            pltpu.VMEM((count, 3 * depth, 3 * kernel.shape[3]), jnp.bfloat16),
            pltpu.VMEM((count, rows_in, width, depth), jnp.bfloat16),
        ],
    )(*sources, kernel.astype(jnp.bfloat16))


def conv_hidden(sources, plan, mean, inv_scale, kernel, flips, bias, first_in, total_rows, pad=(0, 0),
                dtype=jnp.bfloat16, reverse=False):
    rows_in = len(plan)
    width, depth = sources[0].shape[2], sources[0].shape[3]
    vmem = pl.BlockSpec(memory_space=pltpu.VMEM)
    where = jnp.stack([first_in + 1, total_rows, first_in]).astype(jnp.int32)
    args = [where, *sources, mean.reshape(1, -1), inv_scale.reshape(1, -1),
            kernel.astype(jnp.bfloat16), bias.astype(jnp.float32).reshape(1, -1)]
    specs = [pl.BlockSpec(memory_space=pltpu.SMEM)] + [vmem] * (len(sources) + 4)
    return pl.pallas_call(
        functools.partial(
            _conv_kernel, finish=True, lead=pad[0], trail=pad[1], flips=flips, plan=plan, reverse=reverse
        ),
        out_shape=jax.ShapeDtypeStruct((1, rows_in - 2, pad[0] + width + pad[1], kernel.shape[3]), dtype),
        in_specs=specs,
        out_specs=vmem,
        scratch_shapes=[
            pltpu.VMEM((1, 3 * depth, 3 * kernel.shape[3]), jnp.bfloat16),
            pltpu.VMEM((1, rows_in, width, depth), jnp.bfloat16),
        ],
    )(*args)


def finish_features(second_out, latter_kernel_intercept):
    shifted = second_out + latter_kernel_intercept
    return (
        shifted * lax.rsqrt(jnp.mean(shifted * shifted, axis=-1, keepdims=True) + 1e-06)
    ).astype(jnp.bfloat16)


def in_map(rows_from, count, rows_dev):
    total = rows_dev * lax.axis_size("rows")
    first = lax.axis_index("rows") * rows_dev + rows_from
    row = first + lax.broadcasted_iota(jnp.int32, (count, 1, 1), 0)
    return (row >= 0) & (row < total)


def local(
    specimen_pair_inputs,
    initial_kernel_tensor,
    latter_kernel_tensor,
    latter_kernel_intercept,
    patch_horizontal_shift,
    specimen_presence,
    softmax_sharpening,
):
    x0 = specimen_pair_inputs[0]
    x1 = specimen_pair_inputs[1]
    k1 = initial_kernel_tensor
    rows_dev = x0.shape[0]
    width = x0.shape[1]
    size = lax.axis_size("rows")
    cells_all = rows_dev * size * width
    near, far = 2, 6
    up = [(i, i + 1) for i in range(size - 1)]
    down = [(i + 1, i) for i in range(size - 1)]
    before = lax.ppermute(
        jnp.concatenate([x0[rows_dev - near:], x1[rows_dev - far:]], axis=0), "rows", up
    )
    after = lax.ppermute(
        jnp.concatenate([x0[:near], x1[:far]], axis=0), "rows", down
    )

    ends = jnp.concatenate([specimen_pair_inputs[:, :2], specimen_pair_inputs[:, rows_dev - 2:]], axis=1)

    def own(slide, r, halo):
        if not halo:
            return (0, (slide, r))
        return (0, (slide, r if r < 2 else r - rows_dev + 4))

    def row0(r, halo=True):
        if r < 0:
            return (1, (near + r,))
        if r >= rows_dev:
            return (2, (r - rows_dev,))
        return own(0, r, halo)

    def row1(r, halo=True):
        if r < 0:
            return (1, (near + far + r,))
        if r >= rows_dev:
            return (2, (near + r - rows_dev,))
        return own(1, r, halo)

    def rows_of(pick, lo, hi):
        return tuple(pick(r) for r in range(lo, hi))

    inputs = (specimen_pair_inputs,)
    halos = (ends, before, after)
    interior, inner_sums = conv_gather(
        inputs,
        (
            tuple(row0(r, False) for r in range(rows_dev)),
            tuple(row1(r, False) for r in range(rows_dev)),
        ),
        k1,
        (False, False),
    )
    boundary, edge_sums = conv_gather(
        halos,
        (
            rows_of(row0, -1, 2),
            rows_of(row0, rows_dev - 2, rows_dev + 1),
            rows_of(row1, -1, 2),
            rows_of(row1, rows_dev - 2, rows_dev + 1),
        ),
        k1,
        (False, False, False, False),
    )
    per_slide = inner_sums + edge_sums[0::2] + edge_sums[1::2]
    stats = jnp.concatenate([per_slide[:, 0], per_slide[:, 1]], axis=0)
    stats, (edge1, edge0) = butterfly_sum(
        stats,
        "rows",
        [
            lambda: conv_gather(
                halos, (rows_of(row1, -far, 1), rows_of(row1, rows_dev - 1, rows_dev + far)), k1, (False, False)
            )[0],
            lambda: conv_gather(
                halos, (rows_of(row0, -near, 1), rows_of(row0, rows_dev - 1, rows_dev + near)), k1, (False, False)
            )[0],
        ],
    )
    average = stats[0:2] / cells_all
    variance = stats[2:4] / cells_all - average * average
    inv_scale = lax.rsqrt(variance + 1e-05)
    sources = (edge0, boundary, interior, edge1)
    plan0 = ((0, 0, 0), (1, 0, 0)) + tuple((2, 0, r) for r in range(rows_dev - 2)) + ((1, 1, 0), (0, 1, 0))
    halo = far - 1
    plan1 = (
        tuple((2, 0, r) for r in range(halo))
        + ((0, 2, 0),)
        + tuple((1, 1, r) for r in range(rows_dev - 2))
        + ((0, 3, 0),)
        + tuple((2, 1, r) for r in range(halo))
    )
    total = rows_dev * size
    first = lax.axis_index("rows") * rows_dev
    source = conv_hidden(
        sources[:3], plan0, average[0], inv_scale[0], latter_kernel_tensor, (False,),
        latter_kernel_intercept, first - 1, total,
    )[0]
    target_reversed = conv_hidden(
        sources[1:], plan1, average[1], inv_scale[1], latter_kernel_tensor, (True,),
        latter_kernel_intercept, first - halo, total, pad=(64, 8), dtype=jnp.float32, reverse=True,
    )[0]
    return correlation(
        source,
        target_reversed,
        patch_horizontal_shift,
        specimen_presence,
        softmax_sharpening,
    )


def solution(mesh):
    return jax.shard_map(
        local,
        mesh=mesh,
        in_specs=(
            P(None, ("pairs", "rows"), None, None),
            P(),
            P(),
            P(),
            P(("pairs", "rows"), None),
            P(("pairs", "rows"), None),
            P(("pairs", "rows"), None),
        ),
        out_specs=P(None, ("pairs", "rows"), None),
        check_vma=False,
    )
```
